32 devices in a mesh: groups: 2 (over x), seq: 8 (over z, y), chan: 2 (over core).
Axes of the slice: x: 2, y: 2, z: 4, core: 2. Of those that a mesh axis runs over, the one named last changes fastest.
Arguments:
- cached_input: bfloat16 [2048, 4096], P(('groups', 'seq'), 'chan'), parts along dimension 0, may hold values from -6 to 6
- cached_gate: bfloat16 [2048, 4096], P(('groups', 'seq'), 'chan'), parts along dimension 0, may hold values from -6 to 6
- out_grad: bfloat16 [2048, 4096], P(('groups', 'seq'), 'chan'), parts along dimension 0, may hold values from -1.75 to 1.75
- filter_taps: bfloat16 [1024, 32], P('seq', 'chan'), may hold values from -6 to 6
- skip_gain: float32 [4096], P('chan'), may hold values from -1 to 1
Outputs:
- input_grad: bfloat16 [2048, 4096], P(('groups', 'seq'), 'chan'), parts along dimension 0
- filter_grad: float32 [2048, 32], P(('groups', 'seq'), 'chan'), parts along dimension 0
The draws below stay inside these ranges and needn't reach their ends.
There are 2 independent parts, one for each index of `groups`. The reference program is written for one: setup_inputs(seed, part) draws one part's arguments, and reference() takes and returns one part's arrays. A program takes and returns all parts, laid end to end along the dimension named above; an argument that names none is the same for every part. Nothing has to cross between parts.
All inputs are finite; a program needn't handle non-finite values.
Results may differ from the reference program's by a relative error of at most 0.005.
Values may be sent and summed in bfloat16 or wider, within the bound.
No kernel may reach another device: no remote copies, remote signals or barrier semaphores. Data moves between devices by JAX's collectives and lax.ppermute only.
A program may use at most 64 MiB of HBM per device.

```python
import math
import jax
import jax.numpy as jnp
from jax import lax

D = 4096
GROUP = 128
FILTERS = 32
LENGTH = 1024


def level_of(key, shape, pieces, low, largest):
    factor_of = 1.0
    for dim, shards_of in pieces:
        heights = jax.random.uniform(jax.random.fold_in(jax.random.fold_in(key, 6), dim), (shards_of,), jnp.float32, low / len(pieces), largest / len(pieces))
        factor_of = factor_of * jnp.repeat(jnp.exp(heights), shape[dim] // shards_of).reshape((-1,) + (1,) * (len(shape) - 1 - dim))
    return factor_of


def noise(key, shape, width, reach, shards=(), kind=jnp.bfloat16):
    gain = level_of(key, shape, shards, -0.22, 0.18) if shards else 1.0
    result = jax.random.normal(key, shape, jnp.float32) * width * gain
    return jnp.minimum(jnp.maximum(result, -reach), reach).astype(kind)


def setup_inputs(seed: int = 0, part: int = 0) -> dict:
    key_list = jax.random.split(jax.random.key(seed), 6)
    part_splits = jax.random.split(jax.random.fold_in(key_list[5], part), 6)
    return {
        "cached_input": noise(part_splits[0], (LENGTH, D), 1.0, 6.0, ((0, 8), (1, 2))),
        "cached_gate": noise(part_splits[1], (LENGTH, D), 1.0, 6.0, ((0, 8), (1, 2))),
        "out_grad": noise(part_splits[2], (LENGTH, D), 0.3, 1.75, ((0, 8), (1, 2))),
        "filter_taps": noise(key_list[3], (LENGTH, FILTERS), 1.0, 6.0, ((0, 8), (1, 2))),
        "skip_gain": jnp.clip(jax.random.uniform(key_list[4], (D,), jnp.float32, -1.0, 1.0) * level_of(key_list[4], (D,), ((0, 2),), -0.4, 0.0), -1.0, 1.0),
    }


def reference(cached_input, cached_gate, out_grad, filter_taps, skip_gain):
    gated_grad = (out_grad.astype(jnp.float32) * cached_gate.astype(jnp.float32)).astype(jnp.bfloat16)
    gated_grad = lax.optimization_barrier(gated_grad).astype(jnp.float32)
    length = gated_grad.shape[0]
    chan_width = gated_grad.shape[1]
    taps_scale = 1.0 / math.sqrt(length)
    fft_length = 2 * length
    taps_wide = jnp.repeat(filter_taps.astype(jnp.float32), GROUP, axis=1)
    spec_grad = jnp.fft.rfft(gated_grad, n=fft_length, axis=0)
    spec_taps = jnp.fft.rfft(taps_wide, n=fft_length, axis=0)
    conv_grad = jnp.fft.irfft(spec_grad * jnp.conj(spec_taps), n=fft_length, axis=0)[:length]
    input_grad = (conv_grad * taps_scale + skip_gain[None, :] * gated_grad).astype(jnp.bfloat16)
    spec_input = jnp.fft.rfft(cached_input.astype(jnp.float32), n=fft_length, axis=0)
    cross_spec = (spec_grad * jnp.conj(spec_input)).reshape(spec_grad.shape[0], chan_width // GROUP, GROUP).sum(axis=2)
    filter_grad = jnp.fft.irfft(cross_spec, n=fft_length, axis=0)[:length] * taps_scale
    return (input_grad, filter_grad.astype(jnp.float32))
```

```python
import math

import jax
import numpy as np
import jax.numpy as jnp
from jax import lax
from jax.sharding import PartitionSpec as P

lag_group = 4


def toeplitz_blocks(windows, block_rows):
    flipped = windows[..., ::-1]
    tiled = jnp.tile(flipped, (1, 1, block_rows))
    trimmed = tiled[..., : block_rows * (2 * block_rows - 1)]
    shaped = trimmed.reshape(windows.shape[0], windows.shape[1], block_rows, 2 * block_rows - 1)
    return shaped[..., block_rows - 1 : 2 * block_rows - 1]


def diagonal_sums(products, block_rows):
    flipped = products[..., ::-1]
    padded = jnp.pad(flipped, ((0, 0), (0, 0), (0, 0), (0, block_rows)))
    flattened = padded.reshape(products.shape[0], products.shape[1], 2 * block_rows * block_rows)
    trimmed = flattened[..., : block_rows * (2 * block_rows - 1)]
    shaped = trimmed.reshape(products.shape[0], products.shape[1], block_rows, 2 * block_rows - 1)
    diag_sums = jnp.sum(shaped, axis=2)
    return jnp.pad(diag_sums, ((0, 0), (0, 0), (1, 0)))


def fold_windows(window_grads, block_rows):
    front_half = jnp.pad(window_grads[..., :block_rows], ((0, 1), (0, 0), (0, 0)))
    back_half = jnp.pad(window_grads[..., block_rows:], ((1, 0), (0, 0), (0, 0)))
    joined = front_half + back_half
    return jnp.transpose(joined, (1, 0, 2)).reshape(window_grads.shape[1], -1)


def lag_table(taps_all, block_rows):
    return jnp.pad(jnp.transpose(taps_all), ((0, 0), (block_rows, lag_group * block_rows)))


def lag_sweep(
    blocks, base_block, block_count, sources, tap_table, block_rows, trip_count, seq_count
):
    filters = sources.shape[2]
    group_width = sources.shape[3]

    def advance(lag_step, state_pair):
        input_acc, lag_acc = state_pair
        lag_start = lag_step * lag_group
        stacked = jnp.stack(
            [
                lax.dynamic_slice_in_dim(blocks, base_block + lag_start + offset, block_count, 0)
                for offset in range(lag_group)
            ],
            axis=1,
        )
        lag_span = lax.dynamic_slice_in_dim(
            tap_table, lag_start * block_rows, (lag_group + 1) * block_rows, 1
        )
        windows = jnp.stack(
            [
                lag_span[:, offset * block_rows : (offset + 2) * block_rows]
                for offset in range(lag_group)
            ],
            axis=0,
        )
        toeplitz = toeplitz_blocks(windows, block_rows)
        input_acc = input_acc + jnp.einsum(
            "kfts,iktfg->isfg", toeplitz, stacked, preferred_element_type=jnp.float32
        )
        products = jnp.einsum(
            "iktfg,isfg->kfts", stacked, sources, preferred_element_type=jnp.float32
        )
        folded = fold_windows(diagonal_sums(products, block_rows), block_rows)
        previous = lax.dynamic_slice_in_dim(
            lag_acc, lag_start * block_rows, (lag_group + 1) * block_rows, 1
        )
        lag_acc = lax.dynamic_update_slice_in_dim(
            lag_acc, previous + folded, lag_start * block_rows, 1
        )
        return (input_acc, lag_acc)

    initial = (
        jnp.zeros((block_count, block_rows, filters, group_width), jnp.float32),
        jnp.zeros((filters, (seq_count + 1 + lag_group) * block_rows), jnp.float32),
    )
    return lax.fori_loop(0, trip_count, advance, initial)


def per_device(cached_input, cached_gate, out_grad, filter_taps, skip_gain):
    block_rows = cached_input.shape[0]
    chan_width = cached_input.shape[1]
    filters = filter_taps.shape[1]
    group_width = chan_width // filters
    seq_count = lax.axis_size("seq")
    seq_index = lax.axis_index("seq")
    length = block_rows * seq_count
    taps_scale = 1.0 / math.sqrt(length)
    gated_grad = (out_grad.astype(jnp.float32) * cached_gate.astype(jnp.float32)).astype(
        jnp.bfloat16
    )
    stretch_width = chan_width // seq_count
    stretch_filters = max(1, stretch_width // group_width)
    stretch_group = stretch_width // stretch_filters
    first_filter = seq_index * stretch_width // group_width
    tap_columns = np.array(
        [
            (target * stretch_width) // group_width + offset
            for target in range(seq_count)
            for offset in range(stretch_filters)
        ]
    )
    routed_taps = filter_taps[:, tap_columns].reshape(block_rows, seq_count, stretch_filters)
    packed = jnp.concatenate(
        [
            gated_grad.reshape(block_rows, seq_count, stretch_width),
            cached_input.reshape(block_rows, seq_count, stretch_width),
            routed_taps,
        ],
        axis=2,
    )
    moved = lax.all_to_all(packed, "seq", split_axis=1, concat_axis=0, tiled=True)
    moved = moved.reshape(length, 2 * stretch_width + stretch_filters)
    moved_grad = moved[:, :stretch_width]
    moved_input = moved[:, stretch_width : 2 * stretch_width]
    stretch_taps = moved[:, 2 * stretch_width :]
    shaped_grad = moved_grad.reshape(seq_count, block_rows, stretch_filters, stretch_group)
    blocks = jnp.pad(shaped_grad, ((0, seq_count - 1 + lag_group), (0, 0), (0, 0), (0, 0)))
    sources = moved_input.reshape(seq_count, block_rows, stretch_filters, stretch_group)
    trip_count = (seq_count + lag_group - 1) // lag_group
    input_acc, lag_acc = lag_sweep(
        blocks,
        0,
        seq_count,
        sources,
        lag_table(stretch_taps, block_rows),
        block_rows,
        trip_count,
        seq_count,
    )
    stretch_gain = lax.dynamic_slice_in_dim(skip_gain, seq_index * stretch_width, stretch_width, 0)
    conv_grad = input_acc.reshape(length, stretch_width) * taps_scale
    local_grad = (conv_grad + stretch_gain[None, :] * moved_grad.astype(jnp.float32)).astype(
        jnp.bfloat16
    )
    input_grad = lax.all_to_all(local_grad, "seq", split_axis=0, concat_axis=1, tiled=True)
    stretch_term = jnp.transpose(lag_acc[:, block_rows : block_rows + length]) * taps_scale
    lag_parts = lax.all_to_all(
        stretch_term.reshape(seq_count, block_rows, stretch_filters),
        "seq",
        split_axis=0,
        concat_axis=0,
        tiled=True,
    )
    sharers = seq_count * stretch_filters // filters
    filter_grad = (
        jnp.transpose(lag_parts, (1, 0, 2))
        .reshape(block_rows, filters, sharers)
        .sum(axis=2)
    )
    return (input_grad, filter_grad)


def solution(mesh):
    return jax.shard_map(
        per_device,
        mesh=mesh,
        in_specs=(
            P(("groups", "seq"), "chan"),
            P(("groups", "seq"), "chan"),
            P(("groups", "seq"), "chan"),
            P("seq", "chan"),
            P("chan"),
        ),
        out_specs=(P(("groups", "seq"), "chan"), P(("groups", "seq"), "chan")),
        check_vma=False,
    )
```

```python
import functools
import math

import jax
import jax.numpy as jnp
import numpy as np
from jax import lax
from jax.experimental import pallas as pl
from jax.experimental.pallas import tpu as pltpu
from jax.sharding import PartitionSpec as P


def local_kernel(g_ref, x_ref, v_ref, gain_ref, out_ref, diag_ref, *, nb, br, scale):
    n = nb * br
    width = n + br
    taps_row = jnp.broadcast_to(v_ref[...], (br, width))
    toeplitz = pltpu.roll(taps_row, width - br, 1, stride=1, stride_axis=0)
    toeplitz = toeplitz[:, :n].astype(jnp.bfloat16)
    gain = gain_ref[...]
    for i in range(nb):
        conv = jnp.dot(
            toeplitz[:, : n - i * br], g_ref[i * br :, :], preferred_element_type=jnp.float32
        )
        own = g_ref[i * br : (i + 1) * br, :].astype(jnp.float32)
        out_ref[i * br : (i + 1) * br, :] = (conv * scale + gain * own).astype(out_ref.dtype)
    sums = [None] * nb
    for j in range(nb):
        row = lax.dot_general(
            g_ref[j * br : (j + 1) * br, :],
            x_ref[: (j + 1) * br, :],
            (((1,), (1,)), ((), ())),
            preferred_element_type=jnp.float32,
        )
        for i in range(j + 1):
            piece = row[:, i * br : (i + 1) * br]
            sums[j - i] = piece if sums[j - i] is None else sums[j - i] + piece
    zeros = jnp.zeros((br, br), jnp.float32)
    for k in range(nb):
        padded = jnp.concatenate([sums[k], zeros], axis=1)
        skewed = pltpu.roll(padded, 0, 1, stride=1, stride_axis=0)
        diag_ref[k : k + 1, :] = jnp.sum(skewed, axis=0, keepdims=True)


def local_grads(moved_grad, moved_input, stretch_taps, stretch_gain, nb, br, sf, sg, scale):
    n = nb * br
    width = n + br
    taps_rows = jnp.pad(jnp.transpose(stretch_taps).astype(jnp.float32), ((0, 0), (br, 0)))
    return pl.pallas_call(
        functools.partial(local_kernel, nb=nb, br=br, scale=scale),
        grid=(sf,),
        in_specs=[
            pl.BlockSpec((n, sg), lambda f: (0, f)),
            pl.BlockSpec((n, sg), lambda f: (0, f)),
            pl.BlockSpec((None, 1, width), lambda f: (f, 0, 0)),
            pl.BlockSpec((None, 1, sg), lambda f: (f, 0, 0)),
        ],
        out_specs=[
            pl.BlockSpec((n, sg), lambda f: (0, f)),
            pl.BlockSpec((None, nb, 2 * br), lambda f: (f, 0, 0)),
        ],
        out_shape=[
            jax.ShapeDtypeStruct((n, sf * sg), jnp.bfloat16),
            jax.ShapeDtypeStruct((sf, nb, 2 * br), jnp.float32),
        ],
    )(moved_grad, moved_input, taps_rows[:, None, :], stretch_gain.reshape(sf, 1, sg))


def per_device(cached_input, cached_gate, out_grad, filter_taps, skip_gain):
    block_rows = cached_input.shape[0]
    chan_width = cached_input.shape[1]
    filters = filter_taps.shape[1]
    group_width = chan_width // filters
    seq_count = lax.axis_size("seq")
    seq_index = lax.axis_index("seq")
    length = block_rows * seq_count
    taps_scale = 1.0 / math.sqrt(length)
    gated_grad = (out_grad.astype(jnp.float32) * cached_gate.astype(jnp.float32)).astype(
        jnp.bfloat16
    )
    stretch_width = chan_width // seq_count
    stretch_filters = max(1, stretch_width // group_width)
    stretch_group = stretch_width // stretch_filters
    tap_columns = np.array(
        [
            (target * stretch_width) // group_width + offset
            for target in range(seq_count)
            for offset in range(stretch_filters)
        ]
    )
    routed_taps = filter_taps[:, tap_columns].reshape(block_rows, seq_count, stretch_filters)
    packed = jnp.concatenate(
        [
            gated_grad.reshape(block_rows, seq_count, stretch_width),
            cached_input[::-1].reshape(block_rows, seq_count, stretch_width),
            routed_taps,
        ],
        axis=2,
    )
    moved = lax.all_to_all(packed, "seq", split_axis=1, concat_axis=0, tiled=True)
    moved = moved.reshape(length, 2 * stretch_width + stretch_filters)
    moved_grad = moved[:, :stretch_width]
    moved_input = moved[:, stretch_width : 2 * stretch_width]
    stretch_taps = moved[:, 2 * stretch_width :]
    stretch_gain = lax.dynamic_slice_in_dim(skip_gain, seq_index * stretch_width, stretch_width, 0)
    local_grad, diag = local_grads(
        moved_grad,
        moved_input,
        stretch_taps,
        stretch_gain,
        seq_count,
        block_rows,
        stretch_filters,
        stretch_group,
        taps_scale,
    )
    input_grad = lax.all_to_all(local_grad, "seq", split_axis=0, concat_axis=1, tiled=True)
    front = jnp.pad(diag[:, :, :block_rows], ((0, 0), (0, 1), (0, 0)))
    back = jnp.pad(diag[:, :, block_rows:], ((0, 0), (1, 0), (0, 0)))
    lag_sums = (front + back).reshape(stretch_filters, (seq_count + 1) * block_rows)
    stretch_term = (
        jnp.transpose(lag_sums[:, block_rows - 1 : block_rows - 1 + length]) * taps_scale
    )
    lag_parts = lax.all_to_all(
        stretch_term.reshape(seq_count, block_rows, stretch_filters),
        "seq",
        split_axis=0,
        concat_axis=0,
        tiled=True,
    )
    sharers = seq_count * stretch_filters // filters
    filter_grad = (
        jnp.transpose(lag_parts, (1, 0, 2))
        .reshape(block_rows, filters, sharers)
        .sum(axis=2)
    )
    return (input_grad, filter_grad)


def solution(mesh):
    return jax.shard_map(
        per_device,
        mesh=mesh,
        in_specs=(
            P(("groups", "seq"), "chan"),
            P(("groups", "seq"), "chan"),
            P(("groups", "seq"), "chan"),
            P("seq", "chan"),
            P("chan"),
        ),
        out_specs=(P(("groups", "seq"), "chan"), P(("groups", "seq"), "chan")),
        check_vma=False,
    )
```

```python
import functools
import math

import jax
import jax.numpy as jnp
import numpy as np
from jax import lax
from jax.experimental import pallas as pl
from jax.experimental.pallas import tpu as pltpu
from jax.sharding import PartitionSpec as P


def local_kernel(g_ref, x_ref, v_ref, gain_ref, out_ref, diag_ref, xrev_ref, *, nb, br, scale):
    n = nb * br
    width = n + br
    taps_row = jnp.broadcast_to(v_ref[...], (br, width))
    toeplitz = pltpu.roll(taps_row, width - br, 1, stride=1, stride_axis=0)
    toeplitz = toeplitz[:, :n].astype(jnp.bfloat16)
    gain = gain_ref[...]
    for i in range(nb):
        conv = jnp.dot(
            toeplitz[:, : n - i * br], g_ref[i * br :, :], preferred_element_type=jnp.float32
        )
        own = g_ref[i * br : (i + 1) * br, :].astype(jnp.float32)
        out_ref[i * br : (i + 1) * br, :] = (conv * scale + gain * own).astype(out_ref.dtype)
    rows = lax.broadcasted_iota(jnp.int32, (br, br), 0)
    cols = lax.broadcasted_iota(jnp.int32, (br, br), 1)
    flip = (rows + cols == br - 1).astype(jnp.bfloat16)
    for i in range(nb):
        xrev_ref[i * br : (i + 1) * br, :] = jnp.dot(
            flip, x_ref[i * br : (i + 1) * br, :], preferred_element_type=jnp.float32
        ).astype(xrev_ref.dtype)
    sums = [None] * nb
    for j in range(nb):
        row = lax.dot_general(
            g_ref[j * br : (j + 1) * br, :],
            xrev_ref[: (j + 1) * br, :],
            (((1,), (1,)), ((), ())),
            preferred_element_type=jnp.float32,
        )
        for i in range(j + 1):
            piece = row[:, i * br : (i + 1) * br]
            sums[j - i] = piece if sums[j - i] is None else sums[j - i] + piece
    zeros = jnp.zeros((br, br), jnp.float32)
    for k in range(nb):
        padded = jnp.concatenate([sums[k], zeros], axis=1)
        skewed = pltpu.roll(padded, 0, 1, stride=1, stride_axis=0)
        diag_ref[k : k + 1, :] = jnp.sum(skewed, axis=0, keepdims=True)


def local_grads(moved_grad, moved_input, stretch_taps, stretch_gain, nb, br, sf, sg, scale):
    n = nb * br
    width = n + br
    taps_rows = jnp.pad(jnp.transpose(stretch_taps).astype(jnp.float32), ((0, 0), (br, 0)))
    return pl.pallas_call(
        functools.partial(local_kernel, nb=nb, br=br, scale=scale),
        grid=(sf,),
        in_specs=[
            pl.BlockSpec((n, sg), lambda f: (0, f)),
            pl.BlockSpec((n, sg), lambda f: (0, f)),
            pl.BlockSpec((None, 1, width), lambda f: (f, 0, 0)),
            pl.BlockSpec((None, 1, sg), lambda f: (f, 0, 0)),
        ],
        out_specs=[
            pl.BlockSpec((n, sg), lambda f: (0, f)),
            pl.BlockSpec((None, nb, 2 * br), lambda f: (f, 0, 0)),
        ],
        out_shape=[
            jax.ShapeDtypeStruct((n, sf * sg), jnp.bfloat16),
            jax.ShapeDtypeStruct((sf, nb, 2 * br), jnp.float32),
        ],
        scratch_shapes=[pltpu.VMEM((n, sg), jnp.bfloat16)],
    )(moved_grad, moved_input, taps_rows[:, None, :], stretch_gain.reshape(sf, 1, sg))


def per_device(cached_input, cached_gate, out_grad, filter_taps, skip_gain):
    block_rows = cached_input.shape[0]
    chan_width = cached_input.shape[1]
    filters = filter_taps.shape[1]
    group_width = chan_width // filters
    seq_count = lax.axis_size("seq")
    seq_index = lax.axis_index("seq")
    length = block_rows * seq_count
    taps_scale = 1.0 / math.sqrt(length)
    gated_grad = (out_grad.astype(jnp.float32) * cached_gate.astype(jnp.float32)).astype(
        jnp.bfloat16
    )
    stretch_width = chan_width // seq_count
    stretch_filters = max(1, stretch_width // group_width)
    stretch_group = stretch_width // stretch_filters
    tap_columns = np.array(
        [
            (target * stretch_width) // group_width + offset
            for target in range(seq_count)
            for offset in range(stretch_filters)
        ]
    )
    routed_taps = filter_taps[:, tap_columns].reshape(block_rows, seq_count, stretch_filters)
    packed = jnp.concatenate(
        [
            gated_grad.reshape(block_rows, seq_count, stretch_width),
            cached_input.reshape(block_rows, seq_count, stretch_width),
            routed_taps,
        ],
        axis=2,
    )
    moved = lax.all_to_all(packed, "seq", split_axis=1, concat_axis=0, tiled=True)
    moved = moved.reshape(length, 2 * stretch_width + stretch_filters)
    moved_grad = moved[:, :stretch_width]
    moved_input = moved[:, stretch_width : 2 * stretch_width]
    stretch_taps = moved[:, 2 * stretch_width :]
    stretch_gain = lax.dynamic_slice_in_dim(skip_gain, seq_index * stretch_width, stretch_width, 0)
    local_grad, diag = local_grads(
        moved_grad,
        moved_input,
        stretch_taps,
        stretch_gain,
        seq_count,
        block_rows,
        stretch_filters,
        stretch_group,
        taps_scale,
    )
    front = jnp.pad(diag[:, :, :block_rows], ((0, 0), (0, 1), (0, 0)))
    back = jnp.pad(diag[:, :, block_rows:], ((0, 0), (1, 0), (0, 0)))
    lag_sums = (front + back).reshape(stretch_filters, (seq_count + 1) * block_rows)
    stretch_term = (
        jnp.transpose(lag_sums[:, block_rows - 1 : block_rows - 1 + length]) * taps_scale
    )
    high = lax.reduce_precision(stretch_term, exponent_bits=8, mantissa_bits=7)
    rest = stretch_term - high
    middle = lax.reduce_precision(rest, exponent_bits=8, mantissa_bits=7)
    low = rest - middle
    outgoing = jnp.concatenate(
        [local_grad, high.astype(jnp.bfloat16), middle.astype(jnp.bfloat16), low.astype(jnp.bfloat16)],
        axis=1,
    )
    returned = lax.all_to_all(outgoing, "seq", split_axis=0, concat_axis=1, tiled=True)
    returned = returned.reshape(block_rows, seq_count, stretch_width + 3 * stretch_filters)
    input_grad = returned[:, :, :stretch_width].reshape(block_rows, chan_width)
    parts = returned[:, :, stretch_width:].astype(jnp.float32)
    lag_parts = (
        parts[:, :, :stretch_filters]
        + parts[:, :, stretch_filters : 2 * stretch_filters]
        + parts[:, :, 2 * stretch_filters :]
    )
    sharers = seq_count * stretch_filters // filters
    filter_grad = lag_parts.reshape(block_rows, filters, sharers).sum(axis=2)
    return (input_grad, filter_grad)


def solution(mesh):
    return jax.shard_map(
        per_device,
        mesh=mesh,
        in_specs=(
            P(("groups", "seq"), "chan"),
            P(("groups", "seq"), "chan"),
            P(("groups", "seq"), "chan"),
            P("seq", "chan"),
            P("chan"),
        ),
        out_specs=(P(("groups", "seq"), "chan"), P(("groups", "seq"), "chan")),
        check_vma=False,
    )
```

```python
import functools
import math

import jax
import jax.numpy as jnp
import numpy as np
from jax import lax
from jax.experimental import pallas as pl
from jax.experimental.pallas import tpu as pltpu
from jax.sharding import PartitionSpec as P


def local_kernel(g_ref, x_ref, v_ref, gain_ref, out_ref, diag_ref, xrev_ref, *, nb, br, scale):
    n = nb * br
    width = n + br
    taps_row = jnp.broadcast_to(v_ref[...], (br, width))
    toeplitz = pltpu.roll(taps_row, width - br, 1, stride=1, stride_axis=0)
    toeplitz = toeplitz[:, :n].astype(jnp.bfloat16)
    gain = gain_ref[...]
    for i in range(nb):
        conv = jnp.dot(
            toeplitz[:, : n - i * br], g_ref[i * br :, :], preferred_element_type=jnp.float32
        )
        own = g_ref[i * br : (i + 1) * br, :].astype(jnp.float32)
        out_ref[i * br : (i + 1) * br, :] = (conv * scale + gain * own).astype(out_ref.dtype)
    rows = lax.broadcasted_iota(jnp.int32, (br, br), 0)
    cols = lax.broadcasted_iota(jnp.int32, (br, br), 1)
    flip = (rows + cols == br - 1).astype(jnp.bfloat16)
    for i in range(nb):
        xrev_ref[i * br : (i + 1) * br, :] = jnp.dot(
            flip, x_ref[i * br : (i + 1) * br, :], preferred_element_type=jnp.float32
        ).astype(xrev_ref.dtype)
    sums = [None] * nb
    for j in range(nb):
        row = lax.dot_general(
            g_ref[j * br : (j + 1) * br, :],
            xrev_ref[: (j + 1) * br, :],
            (((1,), (1,)), ((), ())),
            preferred_element_type=jnp.float32,
        )
        for i in range(j + 1):
            piece = row[:, i * br : (i + 1) * br]
            sums[j - i] = piece if sums[j - i] is None else sums[j - i] + piece
    zeros = jnp.zeros((br, br), jnp.float32)
    for k in range(nb):
        padded = jnp.concatenate([sums[k], zeros], axis=1)
        skewed = pltpu.roll(padded, 0, 1, stride=1, stride_axis=0)
        diag_ref[k : k + 1, :] = jnp.sum(skewed, axis=0, keepdims=True)


def local_grads(moved, stretch_taps, stretch_gain, nb, br, sf, sg, scale):
    n = nb * br
    width = n + br
    sw = sf * sg
    if sg % 128 == 0:
        grad_in, input_in, input_base = moved, moved, sf
    else:
        grad_in, input_in, input_base = moved[:, :sw], moved[:, sw : 2 * sw], 0
    taps_rows = jnp.pad(jnp.transpose(stretch_taps).astype(jnp.float32), ((0, 0), (br, 0)))
    return pl.pallas_call(
        functools.partial(local_kernel, nb=nb, br=br, scale=scale),
        grid=(sf,),
        in_specs=[
            pl.BlockSpec((n, sg), lambda f: (0, f)),
            pl.BlockSpec((n, sg), lambda f: (0, input_base + f)),
            pl.BlockSpec((None, 1, width), lambda f: (f, 0, 0)),
            pl.BlockSpec((None, 1, sg), lambda f: (f, 0, 0)),
        ],
        out_specs=[
            pl.BlockSpec((n, sg), lambda f: (0, f)),
            pl.BlockSpec((None, nb, 2 * br), lambda f: (f, 0, 0)),
        ],
        out_shape=[
            jax.ShapeDtypeStruct((n, sw), jnp.bfloat16),
            jax.ShapeDtypeStruct((sf, nb, 2 * br), jnp.float32),
        ],
        scratch_shapes=[pltpu.VMEM((n, sg), jnp.bfloat16)],
    )(grad_in, input_in, taps_rows[:, None, :], stretch_gain.reshape(sf, 1, sg))


def per_device(cached_input, cached_gate, out_grad, filter_taps, skip_gain):
    block_rows = cached_input.shape[0]
    chan_width = cached_input.shape[1]
    filters = filter_taps.shape[1]
    group_width = chan_width // filters
    seq_count = lax.axis_size("seq")
    seq_index = lax.axis_index("seq")
    length = block_rows * seq_count
    taps_scale = 1.0 / math.sqrt(length)
    gated_grad = (out_grad.astype(jnp.float32) * cached_gate.astype(jnp.float32)).astype(
        jnp.bfloat16
    )
    stretch_width = chan_width // seq_count
    stretch_filters = max(1, stretch_width // group_width)
    stretch_group = stretch_width // stretch_filters
    tap_columns = np.array(
        [
            (target * stretch_width) // group_width + offset
            for target in range(seq_count)
            for offset in range(stretch_filters)
        ]
    )
    routed_taps = filter_taps[:, tap_columns].reshape(block_rows, seq_count, stretch_filters)
    packed = jnp.concatenate(
        [
            gated_grad.reshape(block_rows, seq_count, stretch_width),
            cached_input.reshape(block_rows, seq_count, stretch_width),
            routed_taps,
        ],
        axis=2,
    )
    packed = jnp.transpose(packed, (1, 0, 2))
    moved = lax.all_to_all(packed, "seq", split_axis=0, concat_axis=0, tiled=True)
    moved = moved.reshape(length, 2 * stretch_width + stretch_filters)
    stretch_taps = moved[:, 2 * stretch_width :]
    stretch_gain = lax.dynamic_slice_in_dim(skip_gain, seq_index * stretch_width, stretch_width, 0)
    local_grad, diag = local_grads(
        moved,
        stretch_taps,
        stretch_gain,
        seq_count,
        block_rows,
        stretch_filters,
        stretch_group,
        taps_scale,
    )
    front = jnp.pad(diag[:, :, :block_rows], ((0, 0), (0, 1), (0, 0)))
    back = jnp.pad(diag[:, :, block_rows:], ((0, 0), (1, 0), (0, 0)))
    lag_sums = (front + back).reshape(stretch_filters, (seq_count + 1) * block_rows)
    stretch_term = (
        jnp.transpose(lag_sums[:, block_rows - 1 : block_rows - 1 + length]) * taps_scale
    )
    high = lax.reduce_precision(stretch_term, exponent_bits=8, mantissa_bits=7)
    rest = stretch_term - high
    middle = lax.reduce_precision(rest, exponent_bits=8, mantissa_bits=7)
    low = rest - middle
    outgoing = jnp.concatenate(
        [local_grad, high.astype(jnp.bfloat16), middle.astype(jnp.bfloat16), low.astype(jnp.bfloat16)],
        axis=1,
    )
    returned = lax.all_to_all(
        outgoing.reshape(seq_count, block_rows, stretch_width + 3 * stretch_filters),
        "seq",
        split_axis=0,
        concat_axis=0,
        tiled=True,
    )
    returned = jnp.transpose(returned, (1, 0, 2))
    input_grad = returned[:, :, :stretch_width].reshape(block_rows, chan_width)
    parts = returned[:, :, stretch_width:].astype(jnp.float32)
    lag_parts = (
        parts[:, :, :stretch_filters]
        + parts[:, :, stretch_filters : 2 * stretch_filters]
        + parts[:, :, 2 * stretch_filters :]
    )
    sharers = seq_count * stretch_filters // filters
    filter_grad = lag_parts.reshape(block_rows, filters, sharers).sum(axis=2)
    return (input_grad, filter_grad)


def solution(mesh):
    return jax.shard_map(
        per_device,
        mesh=mesh,
        in_specs=(
            P(("groups", "seq"), "chan"),
            P(("groups", "seq"), "chan"),
            P(("groups", "seq"), "chan"),
            P("seq", "chan"),
            P("chan"),
        ),
        out_specs=(P(("groups", "seq"), "chan"), P(("groups", "seq"), "chan")),
        check_vma=False,
    )
```

```python
import functools
import math

import jax
import jax.numpy as jnp
import numpy as np
from jax import lax
from jax.experimental import pallas as pl
from jax.experimental.pallas import tpu as pltpu
from jax.sharding import PartitionSpec as P


def local_kernel(g_ref, x_ref, t_ref, gain_ref, out_ref, diag_ref, g_scr, xrev_ref, *, nb, br, scale):
    f = pl.program_id(0)
    n = nb * br
    width = n + br
    pick = lax.broadcasted_iota(jnp.int32, (8, 128), 0) == f
    taps = jnp.concatenate(
        [jnp.zeros((1, br), jnp.float32)]
        + [
            jnp.sum(
                jnp.where(pick, t_ref[j].astype(jnp.float32), 0.0), axis=0, keepdims=True
            )
            for j in range(nb)
        ],
        axis=1,
    )
    taps_row = jnp.broadcast_to(taps, (br, width))
    toeplitz = pltpu.roll(taps_row, width - br, 1, stride=1, stride_axis=0)
    toeplitz = toeplitz[:, :n].astype(jnp.bfloat16)
    rows = lax.broadcasted_iota(jnp.int32, (br, br), 0)
    cols = lax.broadcasted_iota(jnp.int32, (br, br), 1)
    flip = (rows + cols == br - 1).astype(jnp.bfloat16)
    for i in range(nb):
        g_scr[i * br : (i + 1) * br, :] = g_ref[i]
        xrev_ref[i * br : (i + 1) * br, :] = jnp.dot(
            flip, x_ref[i], preferred_element_type=jnp.float32
        ).astype(xrev_ref.dtype)
    gain = gain_ref[...]
    for i in range(nb):
        conv = jnp.dot(
            toeplitz[:, : n - i * br], g_scr[i * br :, :], preferred_element_type=jnp.float32
        )
        own = g_ref[i].astype(jnp.float32)
        out_ref[i] = (conv * scale + gain * own).astype(out_ref.dtype)
    sums = [None] * nb
    for j in range(nb):
        row = lax.dot_general(
            g_ref[j],
            xrev_ref[: (j + 1) * br, :],
            (((1,), (1,)), ((), ())),
            preferred_element_type=jnp.float32,
        )
        for i in range(j + 1):
            piece = row[:, i * br : (i + 1) * br]
            sums[j - i] = piece if sums[j - i] is None else sums[j - i] + piece
    zeros = jnp.zeros((br, br), jnp.float32)
    for k in range(nb):
        padded = jnp.concatenate([sums[k], zeros], axis=1)
        skewed = pltpu.roll(padded, 0, 1, stride=1, stride_axis=0)
        diag_ref[k : k + 1, :] = jnp.sum(skewed, axis=0, keepdims=True)


def local_grads(moved, stretch_gain, nb, br, sf, sg, scale):
    sw = sf * sg
    if sg % 128 == 0:
        grad_in, input_in, input_base = moved, moved, sf
    else:
        grad_in = moved[:, :br, :sw]
        input_in = moved[:, :br, sw : 2 * sw]
        input_base = 0
    tap_in = moved[:, br : br + 8, :128]
    return pl.pallas_call(
        functools.partial(local_kernel, nb=nb, br=br, scale=scale),
        grid=(sf,),
        in_specs=[
            pl.BlockSpec((nb, br, sg), lambda f: (0, 0, f)),
            pl.BlockSpec((nb, br, sg), lambda f: (0, 0, input_base + f)),
            pl.BlockSpec((nb, 8, 128), lambda f: (0, 0, 0)),
            pl.BlockSpec((None, 1, sg), lambda f: (f, 0, 0)),
        ],
        out_specs=[
            pl.BlockSpec((nb, br, sg), lambda f: (0, 0, f)),
            pl.BlockSpec((None, nb, 2 * br), lambda f: (f, 0, 0)),
        ],
        out_shape=[
            jax.ShapeDtypeStruct((nb, br, sw), jnp.bfloat16),
            jax.ShapeDtypeStruct((sf, nb, 2 * br), jnp.float32),
        ],
        scratch_shapes=[
            pltpu.VMEM((nb * br, sg), jnp.bfloat16),
            pltpu.VMEM((nb * br, sg), jnp.bfloat16),
        ],
    )(grad_in, input_in, tap_in, stretch_gain.reshape(sf, 1, sg))


def per_device(cached_input, cached_gate, out_grad, filter_taps, skip_gain):
    block_rows = cached_input.shape[0]
    chan_width = cached_input.shape[1]
    filters = filter_taps.shape[1]
    group_width = chan_width // filters
    seq_count = lax.axis_size("seq")
    seq_index = lax.axis_index("seq")
    length = block_rows * seq_count
    taps_scale = 1.0 / math.sqrt(length)
    gated_grad = (out_grad.astype(jnp.float32) * cached_gate.astype(jnp.float32)).astype(
        jnp.bfloat16
    )
    stretch_width = chan_width // seq_count
    stretch_filters = max(1, stretch_width // group_width)
    stretch_group = stretch_width // stretch_filters
    tap_columns = np.array(
        [
            (target * stretch_width) // group_width + offset
            for target in range(seq_count)
            for offset in range(stretch_filters)
        ]
    )
    routed_taps = jnp.transpose(filter_taps[:, tap_columns]).reshape(
        seq_count, stretch_filters, block_rows
    )
    tap_rows = jnp.pad(
        routed_taps,
        ((0, 0), (0, 8 - stretch_filters), (0, 2 * stretch_width - block_rows)),
    )
    body = jnp.concatenate(
        [
            jnp.transpose(gated_grad.reshape(block_rows, seq_count, stretch_width), (1, 0, 2)),
            jnp.transpose(cached_input.reshape(block_rows, seq_count, stretch_width), (1, 0, 2)),
        ],
        axis=2,
    )
    packed = jnp.concatenate([body, tap_rows], axis=1)
    moved = lax.all_to_all(packed, "seq", split_axis=0, concat_axis=0, tiled=True)
    stretch_gain = lax.dynamic_slice_in_dim(skip_gain, seq_index * stretch_width, stretch_width, 0)
    local_grad, diag = local_grads(
        moved,
        stretch_gain,
        seq_count,
        block_rows,
        stretch_filters,
        stretch_group,
        taps_scale,
    )
    front = jnp.pad(diag[:, :, :block_rows], ((0, 0), (0, 1), (0, 0)))
    back = jnp.pad(diag[:, :, block_rows:], ((0, 0), (1, 0), (0, 0)))
    lag_sums = (front + back).reshape(stretch_filters, (seq_count + 1) * block_rows)
    stretch_term = lag_sums[:, block_rows - 1 : block_rows - 1 + length] * taps_scale
    high = lax.reduce_precision(stretch_term, exponent_bits=8, mantissa_bits=7)
    rest = stretch_term - high
    middle = lax.reduce_precision(rest, exponent_bits=8, mantissa_bits=7)
    low = rest - middle
    split = jnp.stack([high, middle, low], axis=0).astype(jnp.bfloat16)
    split = jnp.transpose(split.reshape(3, stretch_filters, seq_count, block_rows), (2, 0, 1, 3))
    used_rows = 3 * stretch_filters * block_rows // stretch_width
    extra_rows = -(-used_rows // 8) * 8
    split = split.reshape(seq_count, used_rows, stretch_width)
    split = jnp.pad(split, ((0, 0), (0, extra_rows - used_rows), (0, 0)))
    outgoing = jnp.concatenate([local_grad, split], axis=1)
    returned = lax.all_to_all(outgoing, "seq", split_axis=0, concat_axis=0, tiled=True)
    input_grad = jnp.transpose(returned[:, :block_rows, :], (1, 0, 2)).reshape(
        block_rows, chan_width
    )
    parts = returned[:, block_rows : block_rows + used_rows, :].astype(jnp.float32)
    parts = parts.reshape(seq_count, 3, stretch_filters, block_rows).sum(axis=1)
    sharers = seq_count * stretch_filters // filters
    filter_grad = jnp.transpose(
        parts.reshape(filters, sharers, block_rows).sum(axis=1)
    )
    return (input_grad, filter_grad)


def solution(mesh):
    return jax.shard_map(
        per_device,
        mesh=mesh,
        in_specs=(
            P(("groups", "seq"), "chan"),
            P(("groups", "seq"), "chan"),
            P(("groups", "seq"), "chan"),
            P("seq", "chan"),
            P("chan"),
        ),
        out_specs=(P(("groups", "seq"), "chan"), P(("groups", "seq"), "chan")),
        check_vma=False,
    )
```

```python
import functools
import math

import jax
import jax.numpy as jnp
import numpy as np
from jax import lax
from jax.experimental import pallas as pl
from jax.experimental.pallas import tpu as pltpu
from jax.sharding import PartitionSpec as P


def local_kernel(g_ref, x_ref, t_ref, gain_ref, out_ref, diag_ref, g_scr, xrev_ref, *, nb, br, scale):
    f = pl.program_id(0)
    n = nb * br
    width = n + br
    pick = lax.broadcasted_iota(jnp.int32, (8, 128), 0) == f
    taps = jnp.concatenate(
        [jnp.zeros((1, br), jnp.float32)]
        + [
            jnp.sum(
                jnp.where(pick, t_ref[j].astype(jnp.float32), 0.0), axis=0, keepdims=True
            )
            for j in range(nb)
        ],
        axis=1,
    )
    taps_row = jnp.broadcast_to(taps, (br, width))
    toeplitz = pltpu.roll(taps_row, width - br, 1, stride=1, stride_axis=0)
    toeplitz = toeplitz[:, :n].astype(jnp.bfloat16)
    rows = lax.broadcasted_iota(jnp.int32, (br, br), 0)
    cols = lax.broadcasted_iota(jnp.int32, (br, br), 1)
    flip = (rows + cols == br - 1).astype(jnp.bfloat16)
    for i in range(nb):
        g_scr[i * br : (i + 1) * br, :] = g_ref[i]
        xrev_ref[i * br : (i + 1) * br, :] = jnp.dot(
            flip, x_ref[i], preferred_element_type=jnp.float32
        ).astype(xrev_ref.dtype)
    gain = gain_ref[...]
    for i in range(nb):
        conv = jnp.dot(
            toeplitz[:, : n - i * br], g_scr[i * br :, :], preferred_element_type=jnp.float32
        )
        own = g_ref[i].astype(jnp.float32)
        out_ref[i] = (conv * scale + gain * own).astype(out_ref.dtype)
    sums = [None] * nb
    for j in range(nb):
        row = lax.dot_general(
            g_ref[j],
            xrev_ref[: (j + 1) * br, :],
            (((1,), (1,)), ((), ())),
            preferred_element_type=jnp.float32,
        )
        for i in range(j + 1):
            piece = row[:, i * br : (i + 1) * br]
            sums[j - i] = piece if sums[j - i] is None else sums[j - i] + piece
    zeros = jnp.zeros((br, br), jnp.float32)
    for k in range(nb):
        padded = jnp.concatenate([sums[k], zeros], axis=1)
        skewed = pltpu.roll(padded, 0, 1, stride=1, stride_axis=0)
        diag_ref[k : k + 1, :] = jnp.sum(skewed, axis=0, keepdims=True)


def pack_kernel(og_ref, gate_ref, x_ref, taps_ref, out_ref, *, nb, br, sw):
    for j in range(nb):
        cols = slice(j * sw, (j + 1) * sw)
        gated = og_ref[:, cols].astype(jnp.float32) * gate_ref[:, cols].astype(jnp.float32)
        out_ref[j, :br, :sw] = gated.astype(out_ref.dtype)
        out_ref[j, :br, sw:] = x_ref[:, cols]
        out_ref[j, br:, :] = taps_ref[j]


def unpack_kernel(in_ref, out_ref, *, nb, br, sw):
    for j in range(nb):
        out_ref[:, j * sw : (j + 1) * sw] = in_ref[j, :br, :]


def local_grads(moved, stretch_gain, nb, br, sf, sg, scale, out_rows):
    sw = sf * sg
    if sg % 128 == 0:
        grad_in, input_in, input_base = moved, moved, sf
    else:
        grad_in = moved[:, :br, :sw]
        input_in = moved[:, :br, sw : 2 * sw]
        input_base = 0
    tap_in = moved[:, br : br + 8, :128]
    return pl.pallas_call(
        functools.partial(local_kernel, nb=nb, br=br, scale=scale),
        grid=(sf,),
        in_specs=[
            pl.BlockSpec((nb, br, sg), lambda f: (0, 0, f)),
            pl.BlockSpec((nb, br, sg), lambda f: (0, 0, input_base + f)),
            pl.BlockSpec((nb, 8, 128), lambda f: (0, 0, 0)),
            pl.BlockSpec((None, 1, sg), lambda f: (f, 0, 0)),
        ],
        out_specs=[
            pl.BlockSpec((nb, br, sg), lambda f: (0, 0, f)),
            pl.BlockSpec((None, nb, 2 * br), lambda f: (f, 0, 0)),
        ],
        out_shape=[
            jax.ShapeDtypeStruct((nb, out_rows, sw), jnp.bfloat16),
            jax.ShapeDtypeStruct((sf, nb, 2 * br), jnp.float32),
        ],
        scratch_shapes=[
            pltpu.VMEM((nb * br, sg), jnp.bfloat16),
            pltpu.VMEM((nb * br, sg), jnp.bfloat16),
        ],
    )(grad_in, input_in, tap_in, stretch_gain.reshape(sf, 1, sg))


def per_device(cached_input, cached_gate, out_grad, filter_taps, skip_gain):
    block_rows = cached_input.shape[0]
    chan_width = cached_input.shape[1]
    filters = filter_taps.shape[1]
    group_width = chan_width // filters
    seq_count = lax.axis_size("seq")
    seq_index = lax.axis_index("seq")
    length = block_rows * seq_count
    taps_scale = 1.0 / math.sqrt(length)
    stretch_width = chan_width // seq_count
    stretch_filters = max(1, stretch_width // group_width)
    stretch_group = stretch_width // stretch_filters
    tap_columns = np.array(
        [
            (target * stretch_width) // group_width + offset
            for target in range(seq_count)
            for offset in range(stretch_filters)
        ]
    )
    routed_taps = jnp.transpose(filter_taps[:, tap_columns]).reshape(
        seq_count, stretch_filters, block_rows
    )
    tap_rows = jnp.pad(
        routed_taps,
        ((0, 0), (0, 8 - stretch_filters), (0, 2 * stretch_width - block_rows)),
    )
    def gated_grad():
        product = out_grad.astype(jnp.float32) * cached_gate.astype(jnp.float32)
        return product.astype(jnp.bfloat16)

    if stretch_width % 128 == 0:
        packed = pl.pallas_call(
            functools.partial(pack_kernel, nb=seq_count, br=block_rows, sw=stretch_width),
            out_shape=jax.ShapeDtypeStruct(
                (seq_count, block_rows + 8, 2 * stretch_width), jnp.bfloat16
            ),
        )(out_grad, cached_gate, cached_input, tap_rows)
    else:
        body = jnp.concatenate(
            [
                jnp.transpose(gated_grad().reshape(block_rows, seq_count, stretch_width), (1, 0, 2)),
                jnp.transpose(cached_input.reshape(block_rows, seq_count, stretch_width), (1, 0, 2)),
            ],
            axis=2,
        )
        packed = jnp.concatenate([body, tap_rows], axis=1)
    moved = lax.all_to_all(packed, "seq", split_axis=0, concat_axis=0, tiled=True)
    stretch_gain = lax.dynamic_slice_in_dim(skip_gain, seq_index * stretch_width, stretch_width, 0)
    used_rows = 3 * stretch_filters * block_rows // stretch_width
    extra_rows = -(-used_rows // 8) * 8
    local_grad, diag = local_grads(
        moved,
        stretch_gain,
        seq_count,
        block_rows,
        stretch_filters,
        stretch_group,
        taps_scale,
        block_rows + extra_rows,
    )
    front = jnp.pad(diag[:, :, :block_rows], ((0, 0), (0, 1), (0, 0)))
    back = jnp.pad(diag[:, :, block_rows:], ((0, 0), (1, 0), (0, 0)))
    lag_sums = (front + back).reshape(stretch_filters, (seq_count + 1) * block_rows)
    stretch_term = lag_sums[:, block_rows - 1 : block_rows - 1 + length] * taps_scale
    high = lax.reduce_precision(stretch_term, exponent_bits=8, mantissa_bits=7)
    rest = stretch_term - high
    middle = lax.reduce_precision(rest, exponent_bits=8, mantissa_bits=7)
    low = rest - middle
    split = jnp.stack([high, middle, low], axis=0).astype(jnp.bfloat16)
    split = jnp.transpose(split.reshape(3, stretch_filters, seq_count, block_rows), (2, 0, 1, 3))
    split = split.reshape(seq_count, used_rows, stretch_width)
    split = jnp.pad(split, ((0, 0), (0, extra_rows - used_rows), (0, 0)))
    outgoing = lax.dynamic_update_slice_in_dim(local_grad, split, block_rows, 1)
    returned = lax.all_to_all(outgoing, "seq", split_axis=0, concat_axis=0, tiled=True)
    if stretch_width % 128 == 0:
        input_grad = pl.pallas_call(
            functools.partial(unpack_kernel, nb=seq_count, br=block_rows, sw=stretch_width),
            out_shape=jax.ShapeDtypeStruct((block_rows, chan_width), jnp.bfloat16),
        )(returned)
    else:
        input_grad = jnp.transpose(returned[:, :block_rows, :], (1, 0, 2)).reshape(
            block_rows, chan_width
        )
    parts = returned[:, block_rows : block_rows + used_rows, :].astype(jnp.float32)
    parts = parts.reshape(seq_count, 3, stretch_filters, block_rows).sum(axis=1)
    sharers = seq_count * stretch_filters // filters
    filter_grad = jnp.transpose(
        parts.reshape(filters, sharers, block_rows).sum(axis=1)
    )
    return (input_grad, filter_grad)


def solution(mesh):
    return jax.shard_map(
        per_device,
        mesh=mesh,
        in_specs=(
            P(("groups", "seq"), "chan"),
            P(("groups", "seq"), "chan"),
            P(("groups", "seq"), "chan"),
            P("seq", "chan"),
            P("chan"),
        ),
        out_specs=(P(("groups", "seq"), "chan"), P(("groups", "seq"), "chan")),
        check_vma=False,
    )
```

```python
import functools
import math

import jax
import jax.numpy as jnp
import numpy as np
from jax import lax
from jax.experimental import pallas as pl
from jax.experimental.pallas import tpu as pltpu
from jax.sharding import PartitionSpec as P


def local_kernel(g_ref, x_ref, t_ref, gain_ref, out_ref, diag_ref, g_scr, xrev_ref, *, nb, br, scale):
    f = pl.program_id(0)
    n = nb * br
    width = n + br
    pick = lax.broadcasted_iota(jnp.int32, (8, 128), 0) == f
    taps = jnp.concatenate(
        [jnp.zeros((1, br), jnp.float32)]
        + [
            jnp.sum(
                jnp.where(pick, t_ref[j].astype(jnp.float32), 0.0), axis=0, keepdims=True
            )
            for j in range(nb)
        ],
        axis=1,
    )
    taps_row = jnp.broadcast_to(taps, (br, width))
    toeplitz = pltpu.roll(taps_row, width - br, 1, stride=1, stride_axis=0)
    toeplitz = toeplitz[:, :n].astype(jnp.bfloat16)
    rows = lax.broadcasted_iota(jnp.int32, (br, br), 0)
    cols = lax.broadcasted_iota(jnp.int32, (br, br), 1)
    flip = (rows + cols == br - 1).astype(jnp.bfloat16)
    for i in range(nb):
        g_scr[i * br : (i + 1) * br, :] = g_ref[i]
        xrev_ref[i * br : (i + 1) * br, :] = jnp.dot(
            flip, x_ref[i], preferred_element_type=jnp.float32
        ).astype(xrev_ref.dtype)
    gain = gain_ref[...]
    for i in range(nb):
        conv = jnp.dot(
            toeplitz[:, : n - i * br], g_scr[i * br :, :], preferred_element_type=jnp.float32
        )
        own = g_ref[i].astype(jnp.float32)
        out_ref[i] = (conv * scale + gain * own).astype(out_ref.dtype)
    sums = [None] * nb
    for j in range(nb):
        row = lax.dot_general(
            g_ref[j],
            xrev_ref[: (j + 1) * br, :],
            (((1,), (1,)), ((), ())),
            preferred_element_type=jnp.float32,
        )
        for i in range(j + 1):
            piece = row[:, i * br : (i + 1) * br]
            sums[j - i] = piece if sums[j - i] is None else sums[j - i] + piece
    zeros = jnp.zeros((br, br), jnp.float32)
    for k in range(nb):
        padded = jnp.concatenate([sums[k], zeros], axis=1)
        skewed = pltpu.roll(padded, 0, 1, stride=1, stride_axis=0)
        diag_ref[k : k + 1, :] = jnp.sum(skewed, axis=0, keepdims=True)


def pack_kernel(og_ref, gate_ref, x_ref, taps_ref, out_ref, *, br, sw, sf, gw):
    j = pl.program_id(0)
    gated = og_ref[...].astype(jnp.float32) * gate_ref[...].astype(jnp.float32)
    out_ref[:br, :sw] = gated.astype(out_ref.dtype)
    out_ref[:br, sw:] = x_ref[...]
    filters = taps_ref.shape[1]
    rows = lax.broadcasted_iota(jnp.int32, (8, filters), 0)
    cols = lax.broadcasted_iota(jnp.int32, (8, filters), 1)
    pick = ((cols == (j * sw) // gw + rows) & (rows < sf)).astype(jnp.bfloat16)
    tap_rows = lax.dot_general(
        pick, taps_ref[...], (((1,), (1,)), ((), ())), preferred_element_type=jnp.float32
    )
    out_ref[br:, :br] = tap_rows.astype(out_ref.dtype)
    out_ref[br:, br:] = jnp.zeros((8, 2 * sw - br), out_ref.dtype)


def unpack_kernel(in_ref, out_ref, *, br):
    out_ref[...] = in_ref[:br, :]


def local_grads(moved, stretch_gain, nb, br, sf, sg, scale, out_rows):
    sw = sf * sg
    if sg % 128 == 0:
        grad_in, input_in, input_base = moved, moved, sf
    else:
        grad_in = moved[:, :br, :sw]
        input_in = moved[:, :br, sw : 2 * sw]
        input_base = 0
    if sg % 128 == 0:
        tap_in, tap_base = moved, br // 8
    else:
        tap_in, tap_base = moved[:, br : br + 8, :128], 0
    return pl.pallas_call(
        functools.partial(local_kernel, nb=nb, br=br, scale=scale),
        grid=(sf,),
        in_specs=[
            pl.BlockSpec((nb, br, sg), lambda f: (0, 0, f)),
            pl.BlockSpec((nb, br, sg), lambda f: (0, 0, input_base + f)),
            pl.BlockSpec((nb, 8, 128), lambda f: (0, tap_base, 0)),
            pl.BlockSpec((None, 1, sg), lambda f: (f, 0, 0)),
        ],
        out_specs=[
            pl.BlockSpec((nb, br, sg), lambda f: (0, 0, f)),
            pl.BlockSpec((None, nb, 2 * br), lambda f: (f, 0, 0)),
        ],
        out_shape=[
            jax.ShapeDtypeStruct((nb, out_rows, sw), jnp.bfloat16),
            jax.ShapeDtypeStruct((sf, nb, 2 * br), jnp.float32),
        ],
        scratch_shapes=[
            pltpu.VMEM((nb * br, sg), jnp.bfloat16),
            pltpu.VMEM((nb * br, sg), jnp.bfloat16),
        ],
    )(grad_in, input_in, tap_in, stretch_gain.reshape(sf, 1, sg))


def per_device(cached_input, cached_gate, out_grad, filter_taps, skip_gain):
    block_rows = cached_input.shape[0]
    chan_width = cached_input.shape[1]
    filters = filter_taps.shape[1]
    group_width = chan_width // filters
    seq_count = lax.axis_size("seq")
    seq_index = lax.axis_index("seq")
    length = block_rows * seq_count
    taps_scale = 1.0 / math.sqrt(length)
    stretch_width = chan_width // seq_count
    stretch_filters = max(1, stretch_width // group_width)
    stretch_group = stretch_width // stretch_filters
    tap_columns = np.array(
        [
            (target * stretch_width) // group_width + offset
            for target in range(seq_count)
            for offset in range(stretch_filters)
        ]
    )
    def gated_grad():
        product = out_grad.astype(jnp.float32) * cached_gate.astype(jnp.float32)
        return product.astype(jnp.bfloat16)

    if stretch_width % 128 == 0:
        column_block = pl.BlockSpec((block_rows, stretch_width), lambda j: (0, j))
        packed = pl.pallas_call(
            functools.partial(
                pack_kernel,
                br=block_rows,
                sw=stretch_width,
                sf=stretch_filters,
                gw=group_width,
            ),
            grid=(seq_count,),
            in_specs=[
                column_block,
                column_block,
                column_block,
                pl.BlockSpec((block_rows, filters), lambda j: (0, 0)),
            ],
            out_specs=pl.BlockSpec(
                (None, block_rows + 8, 2 * stretch_width), lambda j: (j, 0, 0)
            ),
            out_shape=jax.ShapeDtypeStruct(
                (seq_count, block_rows + 8, 2 * stretch_width), jnp.bfloat16
            ),
        )(out_grad, cached_gate, cached_input, filter_taps)
    else:
        routed_taps = jnp.transpose(filter_taps[:, tap_columns]).reshape(
            seq_count, stretch_filters, block_rows
        )
        tap_rows = jnp.pad(
            routed_taps,
            ((0, 0), (0, 8 - stretch_filters), (0, 2 * stretch_width - block_rows)),
        )
        body = jnp.concatenate(
            [
                jnp.transpose(gated_grad().reshape(block_rows, seq_count, stretch_width), (1, 0, 2)),
                jnp.transpose(cached_input.reshape(block_rows, seq_count, stretch_width), (1, 0, 2)),
            ],
            axis=2,
        )
        packed = jnp.concatenate([body, tap_rows], axis=1)
    moved = lax.all_to_all(packed, "seq", split_axis=0, concat_axis=0, tiled=True)
    stretch_gain = lax.dynamic_slice_in_dim(skip_gain, seq_index * stretch_width, stretch_width, 0)
    used_rows = 3 * stretch_filters * block_rows // stretch_width
    extra_rows = -(-used_rows // 8) * 8
    local_grad, diag = local_grads(
        moved,
        stretch_gain,
        seq_count,
        block_rows,
        stretch_filters,
        stretch_group,
        taps_scale,
        block_rows + extra_rows,
    )
    front = jnp.pad(diag[:, :, :block_rows], ((0, 0), (0, 1), (0, 0)))
    back = jnp.pad(diag[:, :, block_rows:], ((0, 0), (1, 0), (0, 0)))
    lag_sums = (front + back).reshape(stretch_filters, (seq_count + 1) * block_rows)
    stretch_term = lag_sums[:, block_rows - 1 : block_rows - 1 + length] * taps_scale
    high = lax.reduce_precision(stretch_term, exponent_bits=8, mantissa_bits=7)
    rest = stretch_term - high
    middle = lax.reduce_precision(rest, exponent_bits=8, mantissa_bits=7)
    low = rest - middle
    split = jnp.stack([high, middle, low], axis=0).astype(jnp.bfloat16)
    split = jnp.transpose(split.reshape(3, stretch_filters, seq_count, block_rows), (2, 0, 1, 3))
    split = split.reshape(seq_count, used_rows, stretch_width)
    split = jnp.pad(split, ((0, 0), (0, extra_rows - used_rows), (0, 0)))
    outgoing = lax.dynamic_update_slice_in_dim(local_grad, split, block_rows, 1)
    returned = lax.all_to_all(outgoing, "seq", split_axis=0, concat_axis=0, tiled=True)
    if stretch_width % 128 == 0:
        input_grad = pl.pallas_call(
            functools.partial(unpack_kernel, br=block_rows),
            grid=(seq_count,),
            in_specs=[
                pl.BlockSpec((None, block_rows + extra_rows, stretch_width), lambda j: (j, 0, 0))
            ],
            out_specs=pl.BlockSpec((block_rows, stretch_width), lambda j: (0, j)),
            out_shape=jax.ShapeDtypeStruct((block_rows, chan_width), jnp.bfloat16),
        )(returned)
    else:
        input_grad = jnp.transpose(returned[:, :block_rows, :], (1, 0, 2)).reshape(
            block_rows, chan_width
        )
    parts = returned[:, block_rows : block_rows + used_rows, :].astype(jnp.float32)
    parts = parts.reshape(seq_count, 3, stretch_filters, block_rows).sum(axis=1)
    sharers = seq_count * stretch_filters // filters
    filter_grad = jnp.transpose(
        parts.reshape(filters, sharers, block_rows).sum(axis=1)
    )
    return (input_grad, filter_grad)


def solution(mesh):
    return jax.shard_map(
        per_device,
        mesh=mesh,
        in_specs=(
            P(("groups", "seq"), "chan"),
            P(("groups", "seq"), "chan"),
            P(("groups", "seq"), "chan"),
            P("seq", "chan"),
            P("chan"),
        ),
        out_specs=(P(("groups", "seq"), "chan"), P(("groups", "seq"), "chan")),
        check_vma=False,
    )
```

```python
import functools
import math

import jax
import jax.numpy as jnp
import numpy as np
from jax import lax
from jax.experimental import pallas as pl
from jax.experimental.pallas import tpu as pltpu
from jax.sharding import PartitionSpec as P


def local_kernel(g_ref, x_ref, t_ref, gain_ref, out_ref, diag_ref, g_scr, xrev_ref, *, nb, br, scale):
    f = pl.program_id(0)
    n = nb * br
    width = n + br
    pick = lax.broadcasted_iota(jnp.int32, (8, 128), 0) == f
    taps = jnp.concatenate(
        [jnp.zeros((1, br), jnp.float32)]
        + [
            jnp.sum(
                jnp.where(pick, t_ref[j].astype(jnp.float32), 0.0), axis=0, keepdims=True
            )
            for j in range(nb)
        ],
        axis=1,
    )
    taps_row = jnp.broadcast_to(taps, (br, width))
    toeplitz = pltpu.roll(taps_row, width - br, 1, stride=1, stride_axis=0)
    toeplitz = toeplitz[:, :n].astype(jnp.bfloat16)
    rows = lax.broadcasted_iota(jnp.int32, (br, br), 0)
    cols = lax.broadcasted_iota(jnp.int32, (br, br), 1)
    flip = (rows + cols == br - 1).astype(jnp.bfloat16)
    for i in range(nb):
        g_scr[i * br : (i + 1) * br, :] = g_ref[i]
        xrev_ref[i * br : (i + 1) * br, :] = jnp.dot(
            flip, x_ref[i], preferred_element_type=jnp.float32
        ).astype(xrev_ref.dtype)
    gain = gain_ref[...]
    for i in range(nb):
        conv = jnp.dot(
            toeplitz[:, : n - i * br], g_scr[i * br :, :], preferred_element_type=jnp.float32
        )
        own = g_ref[i].astype(jnp.float32)
        out_ref[i] = (conv * scale + gain * own).astype(out_ref.dtype)
    sums = [None] * nb
    for j in range(nb):
        row = lax.dot_general(
            g_ref[j],
            xrev_ref[: (j + 1) * br, :],
            (((1,), (1,)), ((), ())),
            preferred_element_type=jnp.float32,
        )
        for i in range(j + 1):
            piece = row[:, i * br : (i + 1) * br]
            sums[j - i] = piece if sums[j - i] is None else sums[j - i] + piece
    zeros = jnp.zeros((br, br), jnp.float32)
    for k in range(nb):
        padded = jnp.concatenate([sums[k], zeros], axis=1)
        skewed = pltpu.roll(padded, 0, 1, stride=1, stride_axis=0)
        diag_ref[k : k + 1, :] = jnp.sum(skewed, axis=0, keepdims=True)


def pack_kernel(og_ref, gate_ref, x_ref, taps_ref, out_ref, *, br, sw, sf, gw, per_step):
    filters = taps_ref.shape[0]
    rows = lax.broadcasted_iota(jnp.int32, (8, filters), 0)
    cols = lax.broadcasted_iota(jnp.int32, (8, filters), 1)
    for d in range(per_step):
        j = pl.program_id(0) * per_step + d
        span = slice(d * sw, (d + 1) * sw)
        gated = og_ref[:, span].astype(jnp.float32) * gate_ref[:, span].astype(jnp.float32)
        out_ref[d, :br, :sw] = gated.astype(out_ref.dtype)
        out_ref[d, :br, sw:] = x_ref[:, span]
        pick = ((cols == (j * sw) // gw + rows) & (rows < sf)).astype(jnp.bfloat16)
        tap_rows = jnp.dot(pick, taps_ref[...], preferred_element_type=jnp.float32)
        out_ref[d, br:, :br] = tap_rows.astype(out_ref.dtype)
        out_ref[d, br:, br:] = jnp.zeros((8, 2 * sw - br), out_ref.dtype)


def local_grads(moved, stretch_gain, nb, br, sf, sg, scale, out_rows):
    sw = sf * sg
    if sg % 128 == 0:
        grad_in, input_in, input_base = moved, moved, sf
    else:
        grad_in = moved[:, :br, :sw]
        input_in = moved[:, :br, sw : 2 * sw]
        input_base = 0
    if sg % 128 == 0:
        tap_in, tap_base = moved, br // 8
    else:
        tap_in, tap_base = moved[:, br : br + 8, :128], 0
    return pl.pallas_call(
        functools.partial(local_kernel, nb=nb, br=br, scale=scale),
        grid=(sf,),
        in_specs=[
            pl.BlockSpec((nb, br, sg), lambda f: (0, 0, f)),
            pl.BlockSpec((nb, br, sg), lambda f: (0, 0, input_base + f)),
            pl.BlockSpec((nb, 8, 128), lambda f: (0, tap_base, 0)),
            pl.BlockSpec((None, 1, sg), lambda f: (f, 0, 0)),
        ],
        out_specs=[
            pl.BlockSpec((nb, br, sg), lambda f: (0, 0, f)),
            pl.BlockSpec((None, nb, 2 * br), lambda f: (f, 0, 0)),
        ],
        out_shape=[
            jax.ShapeDtypeStruct((nb, out_rows, sw), jnp.bfloat16),
            jax.ShapeDtypeStruct((sf, nb, 2 * br), jnp.float32),
        ],
        scratch_shapes=[
            pltpu.VMEM((nb * br, sg), jnp.bfloat16),
            pltpu.VMEM((nb * br, sg), jnp.bfloat16),
        ],
    )(grad_in, input_in, tap_in, stretch_gain.reshape(sf, 1, sg))


def per_device(cached_input, cached_gate, out_grad, filter_taps, skip_gain):
    block_rows = cached_input.shape[0]
    chan_width = cached_input.shape[1]
    filters = filter_taps.shape[1]
    group_width = chan_width // filters
    seq_count = lax.axis_size("seq")
    seq_index = lax.axis_index("seq")
    length = block_rows * seq_count
    taps_scale = 1.0 / math.sqrt(length)
    stretch_width = chan_width // seq_count
    stretch_filters = max(1, stretch_width // group_width)
    stretch_group = stretch_width // stretch_filters
    tap_columns = np.array(
        [
            (target * stretch_width) // group_width + offset
            for target in range(seq_count)
            for offset in range(stretch_filters)
        ]
    )
    def gated_grad():
        product = out_grad.astype(jnp.float32) * cached_gate.astype(jnp.float32)
        return product.astype(jnp.bfloat16)

    if stretch_width % 128 == 0:
        per_step = seq_count // 2 if seq_count % 2 == 0 else seq_count
        column_block = pl.BlockSpec((block_rows, per_step * stretch_width), lambda j: (0, j))
        packed = pl.pallas_call(
            functools.partial(
                pack_kernel,
                br=block_rows,
                sw=stretch_width,
                sf=stretch_filters,
                gw=group_width,
                per_step=per_step,
            ),
            grid=(seq_count // per_step,),
            in_specs=[
                column_block,
                column_block,
                column_block,
                pl.BlockSpec((filters, block_rows), lambda j: (0, 0)),
            ],
            out_specs=pl.BlockSpec(
                (per_step, block_rows + 8, 2 * stretch_width), lambda j: (j, 0, 0)
            ),
            out_shape=jax.ShapeDtypeStruct(
                (seq_count, block_rows + 8, 2 * stretch_width), jnp.bfloat16
            ),
        )(out_grad, cached_gate, cached_input, jnp.transpose(filter_taps))
    else:
        routed_taps = jnp.transpose(filter_taps[:, tap_columns]).reshape(
            seq_count, stretch_filters, block_rows
        )
        tap_rows = jnp.pad(
            routed_taps,
            ((0, 0), (0, 8 - stretch_filters), (0, 2 * stretch_width - block_rows)),
        )
        body = jnp.concatenate(
            [
                jnp.transpose(gated_grad().reshape(block_rows, seq_count, stretch_width), (1, 0, 2)),
                jnp.transpose(cached_input.reshape(block_rows, seq_count, stretch_width), (1, 0, 2)),
            ],
            axis=2,
        )
        packed = jnp.concatenate([body, tap_rows], axis=1)
    moved = lax.all_to_all(packed, "seq", split_axis=0, concat_axis=0, tiled=True)
    stretch_gain = lax.dynamic_slice_in_dim(skip_gain, seq_index * stretch_width, stretch_width, 0)
    used_rows = 3 * stretch_filters * block_rows // stretch_width
    extra_rows = -(-used_rows // 8) * 8
    local_grad, diag = local_grads(
        moved,
        stretch_gain,
        seq_count,
        block_rows,
        stretch_filters,
        stretch_group,
        taps_scale,
        block_rows + extra_rows,
    )
    front = jnp.pad(diag[:, :, :block_rows], ((0, 0), (0, 1), (0, 0)))
    back = jnp.pad(diag[:, :, block_rows:], ((0, 0), (1, 0), (0, 0)))
    lag_sums = (front + back).reshape(stretch_filters, (seq_count + 1) * block_rows)
    stretch_term = lag_sums[:, block_rows - 1 : block_rows - 1 + length] * taps_scale
    high = lax.reduce_precision(stretch_term, exponent_bits=8, mantissa_bits=7)
    rest = stretch_term - high
    middle = lax.reduce_precision(rest, exponent_bits=8, mantissa_bits=7)
    low = rest - middle
    split = jnp.stack([high, middle, low], axis=0).astype(jnp.bfloat16)
    split = jnp.transpose(split.reshape(3, stretch_filters, seq_count, block_rows), (2, 0, 1, 3))
    split = split.reshape(seq_count, used_rows, stretch_width)
    split = jnp.pad(split, ((0, 0), (0, extra_rows - used_rows), (0, 0)))
    outgoing = lax.dynamic_update_slice_in_dim(local_grad, split, block_rows, 1)
    returned = lax.all_to_all(outgoing, "seq", split_axis=0, concat_axis=0, tiled=True)
    input_grad = jnp.transpose(returned[:, :block_rows, :], (1, 0, 2)).reshape(
        block_rows, chan_width
    )
    parts = returned[:, block_rows : block_rows + used_rows, :].astype(jnp.float32)
    parts = parts.reshape(seq_count, 3, stretch_filters, block_rows).sum(axis=1)
    sharers = seq_count * stretch_filters // filters
    filter_grad = jnp.transpose(
        parts.reshape(filters, sharers, block_rows).sum(axis=1)
    )
    return (input_grad, filter_grad)


def solution(mesh):
    return jax.shard_map(
        per_device,
        mesh=mesh,
        in_specs=(
            P(("groups", "seq"), "chan"),
            P(("groups", "seq"), "chan"),
            P(("groups", "seq"), "chan"),
            P("seq", "chan"),
            P("chan"),
        ),
        out_specs=(P(("groups", "seq"), "chan"), P(("groups", "seq"), "chan")),
        check_vma=False,
    )
```

```python
import functools
import math

import jax
import jax.numpy as jnp
import numpy as np
from jax import lax
from jax.experimental import pallas as pl
from jax.experimental.pallas import tpu as pltpu
from jax.sharding import PartitionSpec as P


def local_kernel(g_ref, x_ref, t_ref, gain_ref, out_ref, diag_ref, g_scr, xrev_ref, *, nb, br, scale, fold_rows):
    f = pl.program_id(0)
    n = nb * br
    width = n + br
    pick = lax.broadcasted_iota(jnp.int32, (8, 128), 0) == f
    taps = jnp.concatenate(
        [jnp.zeros((1, br), jnp.float32)]
        + [
            jnp.sum(
                jnp.where(pick, t_ref[j].astype(jnp.float32), 0.0), axis=0, keepdims=True
            )
            for j in range(nb)
        ],
        axis=1,
    )
    taps_row = jnp.broadcast_to(taps, (br, width))
    toeplitz = pltpu.roll(taps_row, width - br, 1, stride=1, stride_axis=0)
    toeplitz = toeplitz[:, :n].astype(jnp.bfloat16)
    rows = lax.broadcasted_iota(jnp.int32, (br, br), 0)
    cols = lax.broadcasted_iota(jnp.int32, (br, br), 1)
    flip = (rows + cols == br - 1).astype(jnp.bfloat16)
    for i in range(nb):
        g_scr[i * br : (i + 1) * br, :] = g_ref[i]
        xrev_ref[i * br : (i + 1) * br, :] = jnp.dot(
            flip, x_ref[i], preferred_element_type=jnp.float32
        ).astype(xrev_ref.dtype)
    gain = gain_ref[...]
    for i in range(nb):
        conv = jnp.dot(
            toeplitz[:, : n - i * br], g_scr[i * br :, :], preferred_element_type=jnp.float32
        )
        own = g_ref[i].astype(jnp.float32)
        out_ref[i, :br, :] = (conv * scale + gain * own).astype(out_ref.dtype)
    sums = [None] * nb
    for j in range(nb):
        row = lax.dot_general(
            g_ref[j],
            xrev_ref[: (j + 1) * br, :],
            (((1,), (1,)), ((), ())),
            preferred_element_type=jnp.float32,
        )
        for i in range(j + 1):
            piece = row[:, i * br : (i + 1) * br]
            sums[j - i] = piece if sums[j - i] is None else sums[j - i] + piece
    zeros = jnp.zeros((br, br), jnp.float32)
    for k in range(nb):
        padded = jnp.concatenate([sums[k], zeros], axis=1)
        skewed = pltpu.roll(padded, 0, 1, stride=1, stride_axis=0)
        diag_ref[k : k + 1, :] = jnp.sum(skewed, axis=0, keepdims=True)
    if fold_rows:
        diag = diag_ref[...]
        own = pltpu.roll(diag, br + 1, 1)[:, :br]
        nxt = pltpu.roll(diag, 1, 1)[:, :br]
        nxt = jnp.concatenate([nxt[1:], jnp.zeros((1, br), jnp.float32)], axis=0)
        lag_term = (own + nxt) * scale
        high = lag_term.astype(jnp.bfloat16).astype(jnp.float32)
        rest = lag_term - high
        middle = rest.astype(jnp.bfloat16).astype(jnp.float32)
        low = rest - middle
        pick = lax.broadcasted_iota(jnp.int32, (nb, 8, br), 1)
        tile = jnp.where(
            pick == 0,
            high[:, None, :],
            jnp.where(pick == 1, middle[:, None, :], jnp.where(pick == 2, low[:, None, :], 0.0)),
        )
        out_ref[:, br : br + 8, :br] = tile.astype(out_ref.dtype)


def pack_kernel(og_ref, gate_ref, x_ref, taps_ref, out_ref, *, br, sw, sf, gw, per_step):
    filters = taps_ref.shape[0]
    rows = lax.broadcasted_iota(jnp.int32, (8, filters), 0)
    cols = lax.broadcasted_iota(jnp.int32, (8, filters), 1)
    for d in range(per_step):
        j = pl.program_id(0) * per_step + d
        span = slice(d * sw, (d + 1) * sw)
        gated = og_ref[:, span].astype(jnp.float32) * gate_ref[:, span].astype(jnp.float32)
        out_ref[d, :br, :sw] = gated.astype(out_ref.dtype)
        out_ref[d, :br, sw:] = x_ref[:, span]
        pick = ((cols == (j * sw) // gw + rows) & (rows < sf)).astype(jnp.bfloat16)
        tap_rows = jnp.dot(pick, taps_ref[...], preferred_element_type=jnp.float32)
        out_ref[d, br:, :br] = tap_rows.astype(out_ref.dtype)
        out_ref[d, br:, br:] = jnp.zeros((8, 2 * sw - br), out_ref.dtype)


def local_grads(moved, stretch_gain, nb, br, sf, sg, scale, out_rows):
    sw = sf * sg
    fold_rows = sg % 128 == 0
    if sg % 128 == 0:
        grad_in, input_in, input_base = moved, moved, sf
    else:
        grad_in = moved[:, :br, :sw]
        input_in = moved[:, :br, sw : 2 * sw]
        input_base = 0
    if sg % 128 == 0:
        tap_in, tap_base = moved, br // 8
    else:
        tap_in, tap_base = moved[:, br : br + 8, :128], 0
    return pl.pallas_call(
        functools.partial(local_kernel, nb=nb, br=br, scale=scale, fold_rows=fold_rows),
        grid=(sf,),
        in_specs=[
            pl.BlockSpec((nb, br, sg), lambda f: (0, 0, f)),
            pl.BlockSpec((nb, br, sg), lambda f: (0, 0, input_base + f)),
            pl.BlockSpec((nb, 8, 128), lambda f: (0, tap_base, 0)),
            pl.BlockSpec((None, 1, sg), lambda f: (f, 0, 0)),
        ],
        out_specs=[
            pl.BlockSpec((nb, out_rows if fold_rows else br, sg), lambda f: (0, 0, f)),
            pl.BlockSpec((None, nb, 2 * br), lambda f: (f, 0, 0)),
        ],
        out_shape=[
            jax.ShapeDtypeStruct((nb, out_rows, sw), jnp.bfloat16),
            jax.ShapeDtypeStruct((sf, nb, 2 * br), jnp.float32),
        ],
        scratch_shapes=[
            pltpu.VMEM((nb * br, sg), jnp.bfloat16),
            pltpu.VMEM((nb * br, sg), jnp.bfloat16),
        ],
    )(grad_in, input_in, tap_in, stretch_gain.reshape(sf, 1, sg))


def per_device(cached_input, cached_gate, out_grad, filter_taps, skip_gain):
    block_rows = cached_input.shape[0]
    chan_width = cached_input.shape[1]
    filters = filter_taps.shape[1]
    group_width = chan_width // filters
    seq_count = lax.axis_size("seq")
    seq_index = lax.axis_index("seq")
    length = block_rows * seq_count
    taps_scale = 1.0 / math.sqrt(length)
    stretch_width = chan_width // seq_count
    stretch_filters = max(1, stretch_width // group_width)
    stretch_group = stretch_width // stretch_filters
    tap_columns = np.array(
        [
            (target * stretch_width) // group_width + offset
            for target in range(seq_count)
            for offset in range(stretch_filters)
        ]
    )
    def gated_grad():
        product = out_grad.astype(jnp.float32) * cached_gate.astype(jnp.float32)
        return product.astype(jnp.bfloat16)

    if stretch_width % 128 == 0:
        per_step = seq_count // 2 if seq_count % 2 == 0 else seq_count
        column_block = pl.BlockSpec((block_rows, per_step * stretch_width), lambda j: (0, j))
        packed = pl.pallas_call(
            functools.partial(
                pack_kernel,
                br=block_rows,
                sw=stretch_width,
                sf=stretch_filters,
                gw=group_width,
                per_step=per_step,
            ),
            grid=(seq_count // per_step,),
            in_specs=[
                column_block,
                column_block,
                column_block,
                pl.BlockSpec((filters, block_rows), lambda j: (0, 0)),
            ],
            out_specs=pl.BlockSpec(
                (per_step, block_rows + 8, 2 * stretch_width), lambda j: (j, 0, 0)
            ),
            out_shape=jax.ShapeDtypeStruct(
                (seq_count, block_rows + 8, 2 * stretch_width), jnp.bfloat16
            ),
        )(out_grad, cached_gate, cached_input, jnp.transpose(filter_taps))
    else:
        routed_taps = jnp.transpose(filter_taps[:, tap_columns]).reshape(
            seq_count, stretch_filters, block_rows
        )
        tap_rows = jnp.pad(
            routed_taps,
            ((0, 0), (0, 8 - stretch_filters), (0, 2 * stretch_width - block_rows)),
        )
        body = jnp.concatenate(
            [
                jnp.transpose(gated_grad().reshape(block_rows, seq_count, stretch_width), (1, 0, 2)),
                jnp.transpose(cached_input.reshape(block_rows, seq_count, stretch_width), (1, 0, 2)),
            ],
            axis=2,
        )
        packed = jnp.concatenate([body, tap_rows], axis=1)
    moved = lax.all_to_all(packed, "seq", split_axis=0, concat_axis=0, tiled=True)
    stretch_gain = lax.dynamic_slice_in_dim(skip_gain, seq_index * stretch_width, stretch_width, 0)
    used_rows = 3 * stretch_filters * block_rows // stretch_width
    extra_rows = -(-used_rows // 8) * 8
    local_grad, diag = local_grads(
        moved,
        stretch_gain,
        seq_count,
        block_rows,
        stretch_filters,
        stretch_group,
        taps_scale,
        block_rows + extra_rows,
    )
    if stretch_group % 128 == 0:
        outgoing = local_grad
    else:
        front = jnp.pad(diag[:, :, :block_rows], ((0, 0), (0, 1), (0, 0)))
        back = jnp.pad(diag[:, :, block_rows:], ((0, 0), (1, 0), (0, 0)))
        lag_sums = (front + back).reshape(stretch_filters, (seq_count + 1) * block_rows)
        stretch_term = lag_sums[:, block_rows - 1 : block_rows - 1 + length] * taps_scale
        high = lax.reduce_precision(stretch_term, exponent_bits=8, mantissa_bits=7)
        rest = stretch_term - high
        middle = lax.reduce_precision(rest, exponent_bits=8, mantissa_bits=7)
        low = rest - middle
        split = jnp.stack([high, middle, low], axis=0).astype(jnp.bfloat16)
        split = jnp.transpose(split.reshape(3, stretch_filters, seq_count, block_rows), (2, 0, 1, 3))
        split = split.reshape(seq_count, used_rows, stretch_width)
        split = jnp.pad(split, ((0, 0), (0, extra_rows - used_rows), (0, 0)))
        outgoing = lax.dynamic_update_slice_in_dim(local_grad, split, block_rows, 1)
    returned = lax.all_to_all(outgoing, "seq", split_axis=0, concat_axis=0, tiled=True)
    input_grad = jnp.transpose(returned[:, :block_rows, :], (1, 0, 2)).reshape(
        block_rows, chan_width
    )
    sharers = seq_count * stretch_filters // filters
    if stretch_group % 128 == 0:
        parts = returned[:, block_rows : block_rows + 3, :].astype(jnp.float32)
        parts = parts.reshape(seq_count, 3, stretch_filters, stretch_group)[..., :block_rows]
        parts = parts[:, 0] + parts[:, 1] + parts[:, 2]
    else:
        parts = returned[:, block_rows : block_rows + used_rows, :].astype(jnp.float32)
        parts = parts.reshape(seq_count, 3, stretch_filters, block_rows).sum(axis=1)
    filter_grad = jnp.transpose(
        parts.reshape(filters, sharers, block_rows).sum(axis=1)
    )
    return (input_grad, filter_grad)


def solution(mesh):
    return jax.shard_map(
        per_device,
        mesh=mesh,
        in_specs=(
            P(("groups", "seq"), "chan"),
            P(("groups", "seq"), "chan"),
            P(("groups", "seq"), "chan"),
            P("seq", "chan"),
            P("chan"),
        ),
        out_specs=(P(("groups", "seq"), "chan"), P(("groups", "seq"), "chan")),
        check_vma=False,
    )
```

```python
import functools
import math

import jax
import jax.numpy as jnp
import numpy as np
from jax import lax
from jax.experimental import pallas as pl
from jax.experimental.pallas import tpu as pltpu
from jax.sharding import PartitionSpec as P


def local_kernel(g_ref, x_ref, t_ref, gain_ref, out_ref, diag_ref, g_scr, xrev_ref, *, nb, br, scale, fold_rows):
    f = pl.program_id(0)
    n = nb * br
    width = n + br
    pick = lax.broadcasted_iota(jnp.int32, (8, 128), 0) == f
    taps = jnp.concatenate(
        [jnp.zeros((1, br), jnp.float32)]
        + [
            jnp.sum(
                jnp.where(pick, t_ref[j].astype(jnp.float32), 0.0), axis=0, keepdims=True
            )
            for j in range(nb)
        ],
        axis=1,
    )
    taps_row = jnp.broadcast_to(taps, (br, width))
    toeplitz = pltpu.roll(taps_row, width - br, 1, stride=1, stride_axis=0)
    toeplitz = toeplitz[:, :n].astype(jnp.bfloat16)
    rows = lax.broadcasted_iota(jnp.int32, (br, br), 0)
    cols = lax.broadcasted_iota(jnp.int32, (br, br), 1)
    flip = (rows + cols == br - 1).astype(jnp.bfloat16)
    for i in range(nb):
        g_scr[i * br : (i + 1) * br, :] = g_ref[i]
        xrev_ref[i * br : (i + 1) * br, :] = jnp.dot(
            flip, x_ref[i], preferred_element_type=jnp.float32
        ).astype(xrev_ref.dtype)
    gain = gain_ref[...]
    for i in range(nb):
        conv = jnp.dot(
            toeplitz[:, : n - i * br], g_scr[i * br :, :], preferred_element_type=jnp.float32
        )
        own = g_ref[i].astype(jnp.float32)
        out_ref[i, :br, :] = (conv * scale + gain * own).astype(out_ref.dtype)
    sums = [None] * nb
    for j in range(nb):
        row = lax.dot_general(
            g_ref[j],
            xrev_ref[: (j + 1) * br, :],
            (((1,), (1,)), ((), ())),
            preferred_element_type=jnp.float32,
        )
        for i in range(j + 1):
            piece = row[:, i * br : (i + 1) * br]
            sums[j - i] = piece if sums[j - i] is None else sums[j - i] + piece
    zeros = jnp.zeros((br, br), jnp.float32)
    for k in range(nb):
        padded = jnp.concatenate([sums[k], zeros], axis=1)
        skewed = pltpu.roll(padded, 0, 1, stride=1, stride_axis=0)
        diag_ref[k : k + 1, :] = jnp.sum(skewed, axis=0, keepdims=True)
    if fold_rows:
        diag = diag_ref[...]
        own = pltpu.roll(diag, br + 1, 1)[:, :br]
        nxt = pltpu.roll(diag, 1, 1)[:, :br]
        nxt = jnp.concatenate([nxt[1:], jnp.zeros((1, br), jnp.float32)], axis=0)
        lag_term = (own + nxt) * scale
        high = lag_term.astype(jnp.bfloat16).astype(jnp.float32)
        rest = lag_term - high
        middle = rest.astype(jnp.bfloat16).astype(jnp.float32)
        low = rest - middle
        pick = lax.broadcasted_iota(jnp.int32, (nb, 8, br), 1)
        tile = jnp.where(
            pick == 0,
            high[:, None, :],
            jnp.where(pick == 1, middle[:, None, :], jnp.where(pick == 2, low[:, None, :], 0.0)),
        )
        out_ref[:, br : br + 8, :br] = tile.astype(out_ref.dtype)


def pack_kernel(og_ref, gate_ref, x_ref, taps_ref, out_ref, *, br, sw, sf, gw, per_step):
    filters = taps_ref.shape[0]
    rows = lax.broadcasted_iota(jnp.int32, (8, filters), 0)
    cols = lax.broadcasted_iota(jnp.int32, (8, filters), 1)
    for d in range(per_step):
        j = pl.program_id(0) * per_step + d
        span = slice(d * sw, (d + 1) * sw)
        gated = og_ref[:, span].astype(jnp.float32) * gate_ref[:, span].astype(jnp.float32)
        out_ref[d, :br, :sw] = gated.astype(out_ref.dtype)
        out_ref[d, :br, sw:] = x_ref[:, span]
        pick = ((cols == (j * sw) // gw + rows) & (rows < sf)).astype(jnp.bfloat16)
        tap_rows = jnp.dot(pick, taps_ref[...], preferred_element_type=jnp.float32)
        out_ref[d, br:, :br] = tap_rows.astype(out_ref.dtype)
        out_ref[d, br:, br:] = jnp.zeros((8, 2 * sw - br), out_ref.dtype)


def local_grads(moved, stretch_gain, nb, br, sf, sg, scale, out_rows):
    sw = sf * sg
    fold_rows = sg % 128 == 0
    if sg % 128 == 0:
        grad_in, input_in, input_base = moved, moved, sf
    else:
        grad_in = moved[:, :br, :sw]
        input_in = moved[:, :br, sw : 2 * sw]
        input_base = 0
    if sg % 128 == 0:
        tap_in, tap_base = moved, br // 8
    else:
        tap_in, tap_base = moved[:, br : br + 8, :128], 0
    return pl.pallas_call(
        functools.partial(local_kernel, nb=nb, br=br, scale=scale, fold_rows=fold_rows),
        grid=(sf,),
        in_specs=[
            pl.BlockSpec((nb, br, sg), lambda f: (0, 0, f)),
            pl.BlockSpec((nb, br, sg), lambda f: (0, 0, input_base + f)),
            pl.BlockSpec((nb, 8, 128), lambda f: (0, tap_base, 0)),
            pl.BlockSpec((None, 1, sg), lambda f: (f, 0, 0)),
        ],
        out_specs=[
            pl.BlockSpec((nb, out_rows if fold_rows else br, sg), lambda f: (0, 0, f)),
            pl.BlockSpec((None, nb, 2 * br), lambda f: (f, 0, 0)),
        ],
        out_shape=[
            jax.ShapeDtypeStruct((nb, out_rows, sw), jnp.bfloat16),
            jax.ShapeDtypeStruct((sf, nb, 2 * br), jnp.float32),
        ],
        scratch_shapes=[
            pltpu.VMEM((nb * br, sg), jnp.bfloat16),
            pltpu.VMEM((nb * br, sg), jnp.bfloat16),
        ],
    )(grad_in, input_in, tap_in, stretch_gain.reshape(sf, 1, sg))


def per_device(cached_input, cached_gate, out_grad, filter_taps, skip_gain):
    block_rows = cached_input.shape[0]
    chan_width = cached_input.shape[1]
    filters = filter_taps.shape[1]
    group_width = chan_width // filters
    seq_count = lax.axis_size("seq")
    seq_index = lax.axis_index("seq")
    length = block_rows * seq_count
    taps_scale = 1.0 / math.sqrt(length)
    stretch_width = chan_width // seq_count
    stretch_filters = max(1, stretch_width // group_width)
    stretch_group = stretch_width // stretch_filters
    tap_columns = np.array(
        [
            (target * stretch_width) // group_width + offset
            for target in range(seq_count)
            for offset in range(stretch_filters)
        ]
    )
    def gated_grad():
        product = out_grad.astype(jnp.float32) * cached_gate.astype(jnp.float32)
        return product.astype(jnp.bfloat16)

    if stretch_width % 128 == 0:
        per_step = seq_count // 4 if seq_count % 4 == 0 else seq_count
        column_block = pl.BlockSpec((block_rows, per_step * stretch_width), lambda j: (0, j))
        packed = pl.pallas_call(
            functools.partial(
                pack_kernel,
                br=block_rows,
                sw=stretch_width,
                sf=stretch_filters,
                gw=group_width,
                per_step=per_step,
            ),
            grid=(seq_count // per_step,),
            in_specs=[
                column_block,
                column_block,
                column_block,
                pl.BlockSpec((filters, block_rows), lambda j: (0, 0)),
            ],
            out_specs=pl.BlockSpec(
                (per_step, block_rows + 8, 2 * stretch_width), lambda j: (j, 0, 0)
            ),
            out_shape=jax.ShapeDtypeStruct(
                (seq_count, block_rows + 8, 2 * stretch_width), jnp.bfloat16
            ),
        )(out_grad, cached_gate, cached_input, jnp.transpose(filter_taps))
    else:
        routed_taps = jnp.transpose(filter_taps[:, tap_columns]).reshape(
            seq_count, stretch_filters, block_rows
        )
        tap_rows = jnp.pad(
            routed_taps,
            ((0, 0), (0, 8 - stretch_filters), (0, 2 * stretch_width - block_rows)),
        )
        body = jnp.concatenate(
            [
                jnp.transpose(gated_grad().reshape(block_rows, seq_count, stretch_width), (1, 0, 2)),
                jnp.transpose(cached_input.reshape(block_rows, seq_count, stretch_width), (1, 0, 2)),
            ],
            axis=2,
        )
        packed = jnp.concatenate([body, tap_rows], axis=1)
    moved = lax.all_to_all(packed, "seq", split_axis=0, concat_axis=0, tiled=True)
    stretch_gain = lax.dynamic_slice_in_dim(skip_gain, seq_index * stretch_width, stretch_width, 0)
    used_rows = 3 * stretch_filters * block_rows // stretch_width
    extra_rows = -(-used_rows // 8) * 8
    local_grad, diag = local_grads(
        moved,
        stretch_gain,
        seq_count,
        block_rows,
        stretch_filters,
        stretch_group,
        taps_scale,
        block_rows + extra_rows,
    )
    if stretch_group % 128 == 0:
        outgoing = local_grad
    else:
        front = jnp.pad(diag[:, :, :block_rows], ((0, 0), (0, 1), (0, 0)))
        back = jnp.pad(diag[:, :, block_rows:], ((0, 0), (1, 0), (0, 0)))
        lag_sums = (front + back).reshape(stretch_filters, (seq_count + 1) * block_rows)
        stretch_term = lag_sums[:, block_rows - 1 : block_rows - 1 + length] * taps_scale
        high = lax.reduce_precision(stretch_term, exponent_bits=8, mantissa_bits=7)
        rest = stretch_term - high
        middle = lax.reduce_precision(rest, exponent_bits=8, mantissa_bits=7)
        low = rest - middle
        split = jnp.stack([high, middle, low], axis=0).astype(jnp.bfloat16)
        split = jnp.transpose(split.reshape(3, stretch_filters, seq_count, block_rows), (2, 0, 1, 3))
        split = split.reshape(seq_count, used_rows, stretch_width)
        split = jnp.pad(split, ((0, 0), (0, extra_rows - used_rows), (0, 0)))
        outgoing = lax.dynamic_update_slice_in_dim(local_grad, split, block_rows, 1)
    returned = lax.all_to_all(outgoing, "seq", split_axis=0, concat_axis=0, tiled=True)
    input_grad = jnp.transpose(returned[:, :block_rows, :], (1, 0, 2)).reshape(
        block_rows, chan_width
    )
    sharers = seq_count * stretch_filters // filters
    if stretch_group % 128 == 0:
        parts = returned[:, block_rows : block_rows + 3, :].astype(jnp.float32)
        parts = parts.reshape(seq_count, 3, stretch_filters, stretch_group)[..., :block_rows]
        parts = parts[:, 0] + parts[:, 1] + parts[:, 2]
    else:
        parts = returned[:, block_rows : block_rows + used_rows, :].astype(jnp.float32)
        parts = parts.reshape(seq_count, 3, stretch_filters, block_rows).sum(axis=1)
    filter_grad = jnp.transpose(
        parts.reshape(filters, sharers, block_rows).sum(axis=1)
    )
    return (input_grad, filter_grad)


def solution(mesh):
    return jax.shard_map(
        per_device,
        mesh=mesh,
        in_specs=(
            P(("groups", "seq"), "chan"),
            P(("groups", "seq"), "chan"),
            P(("groups", "seq"), "chan"),
            P("seq", "chan"),
            P("chan"),
        ),
        out_specs=(P(("groups", "seq"), "chan"), P(("groups", "seq"), "chan")),
        check_vma=False,
    )
```

```python
import functools
import math

import jax
import jax.numpy as jnp
import numpy as np
from jax import lax
from jax.experimental import pallas as pl
from jax.experimental.pallas import tpu as pltpu
from jax.sharding import PartitionSpec as P


def local_kernel(g_ref, x_ref, t_ref, gain_ref, out_ref, diag_ref, g_scr, xrev_ref, *, nb, br, scale, fold_rows):
    f = pl.program_id(0)
    me = lax.axis_index("seq")
    slot = [(me - i + nb) % nb for i in range(nb)]
    n = nb * br
    width = n + br
    pick = lax.broadcasted_iota(jnp.int32, (8, 128), 0) == f
    taps = jnp.concatenate(
        [jnp.zeros((1, br), jnp.float32)]
        + [
            jnp.sum(
                jnp.where(pick, t_ref[slot[j]].astype(jnp.float32), 0.0), axis=0, keepdims=True
            )
            for j in range(nb)
        ],
        axis=1,
    )
    taps_row = jnp.broadcast_to(taps, (br, width))
    toeplitz = pltpu.roll(taps_row, width - br, 1, stride=1, stride_axis=0)
    toeplitz = toeplitz[:, :n].astype(jnp.bfloat16)
    rows = lax.broadcasted_iota(jnp.int32, (br, br), 0)
    cols = lax.broadcasted_iota(jnp.int32, (br, br), 1)
    flip = (rows + cols == br - 1).astype(jnp.bfloat16)
    for i in range(nb):
        g_scr[i * br : (i + 1) * br, :] = g_ref[slot[i]]
        xrev_ref[i * br : (i + 1) * br, :] = jnp.dot(
            flip, x_ref[slot[i]], preferred_element_type=jnp.float32
        ).astype(xrev_ref.dtype)
    gain = gain_ref[...]
    for i in range(nb):
        conv = jnp.dot(
            toeplitz[:, : n - i * br], g_scr[i * br :, :], preferred_element_type=jnp.float32
        )
        own = g_scr[i * br : (i + 1) * br, :].astype(jnp.float32)
        out_ref[i, :br, :] = (conv * scale + gain * own).astype(out_ref.dtype)
    sums = [None] * nb
    for j in range(nb):
        row = lax.dot_general(
            g_scr[j * br : (j + 1) * br, :],
            xrev_ref[: (j + 1) * br, :],
            (((1,), (1,)), ((), ())),
            preferred_element_type=jnp.float32,
        )
        for i in range(j + 1):
            piece = row[:, i * br : (i + 1) * br]
            sums[j - i] = piece if sums[j - i] is None else sums[j - i] + piece
    zeros = jnp.zeros((br, br), jnp.float32)
    for k in range(nb):
        padded = jnp.concatenate([sums[k], zeros], axis=1)
        skewed = pltpu.roll(padded, 0, 1, stride=1, stride_axis=0)
        diag_ref[k : k + 1, :] = jnp.sum(skewed, axis=0, keepdims=True)
    if fold_rows:
        diag = diag_ref[...]
        own = pltpu.roll(diag, br + 1, 1)[:, :br]
        nxt = pltpu.roll(diag, 1, 1)[:, :br]
        nxt = jnp.concatenate([nxt[1:], jnp.zeros((1, br), jnp.float32)], axis=0)
        lag_term = (own + nxt) * scale
        high = lag_term.astype(jnp.bfloat16).astype(jnp.float32)
        rest = lag_term - high
        middle = rest.astype(jnp.bfloat16).astype(jnp.float32)
        low = rest - middle
        pick = lax.broadcasted_iota(jnp.int32, (nb, 8, br), 1)
        tile = jnp.where(
            pick == 0,
            high[:, None, :],
            jnp.where(pick == 1, middle[:, None, :], jnp.where(pick == 2, low[:, None, :], 0.0)),
        )
        out_ref[:, br : br + 8, :br] = tile.astype(out_ref.dtype)


def pack_kernel(og_ref, gate_ref, x_ref, taps_ref, out_ref, *, br, sw, sf, gw, per_step):
    filters = taps_ref.shape[0]
    rows = lax.broadcasted_iota(jnp.int32, (8, filters), 0)
    cols = lax.broadcasted_iota(jnp.int32, (8, filters), 1)
    for d in range(per_step):
        j = pl.program_id(0) * per_step + d
        span = slice(d * sw, (d + 1) * sw)
        gated = og_ref[:, span].astype(jnp.float32) * gate_ref[:, span].astype(jnp.float32)
        out_ref[d, :br, :sw] = gated.astype(out_ref.dtype)
        out_ref[d, :br, sw:] = x_ref[:, span]
        pick = ((cols == (j * sw) // gw + rows) & (rows < sf)).astype(jnp.bfloat16)
        tap_rows = jnp.dot(pick, taps_ref[...], preferred_element_type=jnp.float32)
        out_ref[d, br:, :br] = tap_rows.astype(out_ref.dtype)
        out_ref[d, br:, br:] = jnp.zeros((8, 2 * sw - br), out_ref.dtype)


def local_grads(moved, stretch_gain, nb, br, sf, sg, scale, out_rows):
    sw = sf * sg
    fold_rows = sg % 128 == 0
    if sg % 128 == 0:
        grad_in, input_in, input_base = moved, moved, sf
    else:
        grad_in = moved[:, :br, :sw]
        input_in = moved[:, :br, sw : 2 * sw]
        input_base = 0
    if sg % 128 == 0:
        tap_in, tap_base = moved, br // 8
    else:
        tap_in, tap_base = moved[:, br : br + 8, :128], 0
    return pl.pallas_call(
        functools.partial(local_kernel, nb=nb, br=br, scale=scale, fold_rows=fold_rows),
        grid=(sf,),
        in_specs=[
            pl.BlockSpec((nb, br, sg), lambda f: (0, 0, f)),
            pl.BlockSpec((nb, br, sg), lambda f: (0, 0, input_base + f)),
            pl.BlockSpec((nb, 8, 128), lambda f: (0, tap_base, 0)),
            pl.BlockSpec((None, 1, sg), lambda f: (f, 0, 0)),
        ],
        out_specs=[
            pl.BlockSpec((nb, out_rows if fold_rows else br, sg), lambda f: (0, 0, f)),
            pl.BlockSpec((None, nb, 2 * br), lambda f: (f, 0, 0)),
        ],
        out_shape=[
            jax.ShapeDtypeStruct((nb, out_rows, sw), jnp.bfloat16),
            jax.ShapeDtypeStruct((sf, nb, 2 * br), jnp.float32),
        ],
        scratch_shapes=[
            pltpu.VMEM((nb * br, sg), jnp.bfloat16),
            pltpu.VMEM((nb * br, sg), jnp.bfloat16),
        ],
    )(grad_in, input_in, tap_in, stretch_gain.reshape(sf, 1, sg))


def per_device(cached_input, cached_gate, out_grad, filter_taps, skip_gain):
    block_rows = cached_input.shape[0]
    chan_width = cached_input.shape[1]
    filters = filter_taps.shape[1]
    group_width = chan_width // filters
    seq_count = lax.axis_size("seq")
    seq_index = lax.axis_index("seq")
    length = block_rows * seq_count
    taps_scale = 1.0 / math.sqrt(length)
    stretch_width = chan_width // seq_count
    stretch_filters = max(1, stretch_width // group_width)
    stretch_group = stretch_width // stretch_filters
    tap_columns = np.array(
        [
            (target * stretch_width) // group_width + offset
            for target in range(seq_count)
            for offset in range(stretch_filters)
        ]
    )
    def gated_grad():
        product = out_grad.astype(jnp.float32) * cached_gate.astype(jnp.float32)
        return product.astype(jnp.bfloat16)

    if stretch_width % 128 == 0:
        per_step = seq_count // 2 if seq_count % 2 == 0 else seq_count
        column_block = pl.BlockSpec((block_rows, per_step * stretch_width), lambda j: (0, j))
        packed = pl.pallas_call(
            functools.partial(
                pack_kernel,
                br=block_rows,
                sw=stretch_width,
                sf=stretch_filters,
                gw=group_width,
                per_step=per_step,
            ),
            grid=(seq_count // per_step,),
            in_specs=[
                column_block,
                column_block,
                column_block,
                pl.BlockSpec((filters, block_rows), lambda j: (0, 0)),
            ],
            out_specs=pl.BlockSpec(
                (per_step, block_rows + 8, 2 * stretch_width), lambda j: (j, 0, 0)
            ),
            out_shape=jax.ShapeDtypeStruct(
                (seq_count, block_rows + 8, 2 * stretch_width), jnp.bfloat16
            ),
        )(out_grad, cached_gate, cached_input, jnp.transpose(filter_taps))
    else:
        routed_taps = jnp.transpose(filter_taps[:, tap_columns]).reshape(
            seq_count, stretch_filters, block_rows
        )
        tap_rows = jnp.pad(
            routed_taps,
            ((0, 0), (0, 8 - stretch_filters), (0, 2 * stretch_width - block_rows)),
        )
        body = jnp.concatenate(
            [
                jnp.transpose(gated_grad().reshape(block_rows, seq_count, stretch_width), (1, 0, 2)),
                jnp.transpose(cached_input.reshape(block_rows, seq_count, stretch_width), (1, 0, 2)),
            ],
            axis=2,
        )
        packed = jnp.concatenate([body, tap_rows], axis=1)
    arrived = [lax.dynamic_index_in_dim(packed, seq_index, 0, keepdims=True)]
    for shift in range(1, seq_count):
        chunk = lax.dynamic_index_in_dim(packed, (seq_index + shift) % seq_count, 0, keepdims=True)
        pairs = [(i, (i + shift) % seq_count) for i in range(seq_count)]
        arrived.append(lax.ppermute(chunk, "seq", pairs))
    moved = jnp.concatenate(arrived, axis=0)
    stretch_gain = lax.dynamic_slice_in_dim(skip_gain, seq_index * stretch_width, stretch_width, 0)
    used_rows = 3 * stretch_filters * block_rows // stretch_width
    extra_rows = -(-used_rows // 8) * 8
    local_grad, diag = local_grads(
        moved,
        stretch_gain,
        seq_count,
        block_rows,
        stretch_filters,
        stretch_group,
        taps_scale,
        block_rows + extra_rows,
    )
    if stretch_group % 128 == 0:
        outgoing = local_grad
    else:
        front = jnp.pad(diag[:, :, :block_rows], ((0, 0), (0, 1), (0, 0)))
        back = jnp.pad(diag[:, :, block_rows:], ((0, 0), (1, 0), (0, 0)))
        lag_sums = (front + back).reshape(stretch_filters, (seq_count + 1) * block_rows)
        stretch_term = lag_sums[:, block_rows - 1 : block_rows - 1 + length] * taps_scale
        high = lax.reduce_precision(stretch_term, exponent_bits=8, mantissa_bits=7)
        rest = stretch_term - high
        middle = lax.reduce_precision(rest, exponent_bits=8, mantissa_bits=7)
        low = rest - middle
        split = jnp.stack([high, middle, low], axis=0).astype(jnp.bfloat16)
        split = jnp.transpose(split.reshape(3, stretch_filters, seq_count, block_rows), (2, 0, 1, 3))
        split = split.reshape(seq_count, used_rows, stretch_width)
        split = jnp.pad(split, ((0, 0), (0, extra_rows - used_rows), (0, 0)))
        outgoing = lax.dynamic_update_slice_in_dim(local_grad, split, block_rows, 1)
    returned = lax.all_to_all(outgoing, "seq", split_axis=0, concat_axis=0, tiled=True)
    input_grad = jnp.transpose(returned[:, :block_rows, :], (1, 0, 2)).reshape(
        block_rows, chan_width
    )
    sharers = seq_count * stretch_filters // filters
    if stretch_group % 128 == 0:
        parts = returned[:, block_rows : block_rows + 3, :].astype(jnp.float32)
        parts = parts.reshape(seq_count, 3, stretch_filters, stretch_group)[..., :block_rows]
        parts = parts[:, 0] + parts[:, 1] + parts[:, 2]
    else:
        parts = returned[:, block_rows : block_rows + used_rows, :].astype(jnp.float32)
        parts = parts.reshape(seq_count, 3, stretch_filters, block_rows).sum(axis=1)
    filter_grad = jnp.transpose(
        parts.reshape(filters, sharers, block_rows).sum(axis=1)
    )
    return (input_grad, filter_grad)


def solution(mesh):
    return jax.shard_map(
        per_device,
        mesh=mesh,
        in_specs=(
            P(("groups", "seq"), "chan"),
            P(("groups", "seq"), "chan"),
            P(("groups", "seq"), "chan"),
            P("seq", "chan"),
            P("chan"),
        ),
        out_specs=(P(("groups", "seq"), "chan"), P(("groups", "seq"), "chan")),
        check_vma=False,
    )
```

```python
import functools
import math

import jax
import jax.numpy as jnp
import numpy as np
from jax import lax
from jax.experimental import pallas as pl
from jax.experimental.pallas import tpu as pltpu
from jax.sharding import PartitionSpec as P


def local_kernel(g_ref, x_ref, t_ref, gain_ref, out_ref, diag_ref, g_scr, xrev_ref, *, nb, br, scale, fold_rows):
    f = pl.program_id(0)
    me = lax.axis_index("seq")
    slot = [(me - i + nb) % nb for i in range(nb)]
    n = nb * br
    width = n + br
    pick = lax.broadcasted_iota(jnp.int32, (8, 128), 0) == f
    taps = jnp.concatenate(
        [jnp.zeros((1, br), jnp.float32)]
        + [
            jnp.sum(
                jnp.where(pick, t_ref[slot[j]].astype(jnp.float32), 0.0), axis=0, keepdims=True
            )
            for j in range(nb)
        ],
        axis=1,
    )
    taps_row = jnp.broadcast_to(taps, (br, width))
    toeplitz = pltpu.roll(taps_row, width - br, 1, stride=1, stride_axis=0)
    toeplitz = toeplitz[:, :n].astype(jnp.bfloat16)
    rows = lax.broadcasted_iota(jnp.int32, (br, br), 0)
    cols = lax.broadcasted_iota(jnp.int32, (br, br), 1)
    flip = (rows + cols == br - 1).astype(jnp.bfloat16)
    for i in range(nb):
        g_scr[i * br : (i + 1) * br, :] = g_ref[slot[i]]
        xrev_ref[i * br : (i + 1) * br, :] = jnp.dot(
            flip, x_ref[slot[i]], preferred_element_type=jnp.float32
        ).astype(xrev_ref.dtype)
    gain = gain_ref[...]
    for i in range(nb):
        conv = jnp.dot(
            toeplitz[:, : n - i * br], g_scr[i * br :, :], preferred_element_type=jnp.float32
        )
        own = g_scr[i * br : (i + 1) * br, :].astype(jnp.float32)
        out_ref[i, :br, :] = (conv * scale + gain * own).astype(out_ref.dtype)
    sums = [None] * nb
    for j in range(nb):
        row = lax.dot_general(
            g_scr[j * br : (j + 1) * br, :],
            xrev_ref[: (j + 1) * br, :],
            (((1,), (1,)), ((), ())),
            preferred_element_type=jnp.float32,
        )
        for i in range(j + 1):
            piece = row[:, i * br : (i + 1) * br]
            sums[j - i] = piece if sums[j - i] is None else sums[j - i] + piece
    zeros = jnp.zeros((br, br), jnp.float32)
    for k in range(nb):
        padded = jnp.concatenate([sums[k], zeros], axis=1)
        skewed = pltpu.roll(padded, 0, 1, stride=1, stride_axis=0)
        diag_ref[k : k + 1, :] = jnp.sum(skewed, axis=0, keepdims=True)
    if fold_rows:
        diag = diag_ref[...]
        own = pltpu.roll(diag, br + 1, 1)[:, :br]
        nxt = pltpu.roll(diag, 1, 1)[:, :br]
        nxt = jnp.concatenate([nxt[1:], jnp.zeros((1, br), jnp.float32)], axis=0)
        lag_term = (own + nxt) * scale
        high = lag_term.astype(jnp.bfloat16).astype(jnp.float32)
        rest = lag_term - high
        middle = rest.astype(jnp.bfloat16).astype(jnp.float32)
        low = rest - middle
        pick = lax.broadcasted_iota(jnp.int32, (nb, 8, br), 1)
        tile = jnp.where(
            pick == 0,
            high[:, None, :],
            jnp.where(pick == 1, middle[:, None, :], jnp.where(pick == 2, low[:, None, :], 0.0)),
        )
        out_ref[:, br : br + 8, :br] = tile.astype(out_ref.dtype)


def pack_kernel(og_ref, gate_ref, x_ref, taps_ref, out_ref, *, br, sw, sf, gw, per_step):
    filters = taps_ref.shape[0]
    rows = lax.broadcasted_iota(jnp.int32, (8, filters), 0)
    cols = lax.broadcasted_iota(jnp.int32, (8, filters), 1)
    for d in range(per_step):
        j = pl.program_id(0) * per_step + d
        span = slice(d * sw, (d + 1) * sw)
        gated = og_ref[:, span].astype(jnp.float32) * gate_ref[:, span].astype(jnp.float32)
        out_ref[d, :br, :sw] = gated.astype(out_ref.dtype)
        out_ref[d, :br, sw:] = x_ref[:, span]
        pick = ((cols == (j * sw) // gw + rows) & (rows < sf)).astype(jnp.bfloat16)
        tap_rows = jnp.dot(pick, taps_ref[...], preferred_element_type=jnp.float32)
        out_ref[d, br:, :br] = tap_rows.astype(out_ref.dtype)
        out_ref[d, br:, br:] = jnp.zeros((8, 2 * sw - br), out_ref.dtype)


def local_grads(moved, stretch_gain, nb, br, sf, sg, scale, out_rows):
    sw = sf * sg
    fold_rows = sg % 128 == 0
    if sg % 128 == 0:
        grad_in, input_in, input_base = moved, moved, sf
    else:
        grad_in = moved[:, :br, :sw]
        input_in = moved[:, :br, sw : 2 * sw]
        input_base = 0
    if sg % 128 == 0:
        tap_in, tap_base = moved, br // 8
    else:
        tap_in, tap_base = moved[:, br : br + 8, :128], 0
    return pl.pallas_call(
        functools.partial(local_kernel, nb=nb, br=br, scale=scale, fold_rows=fold_rows),
        grid=(sf,),
        in_specs=[
            pl.BlockSpec((nb, br, sg), lambda f: (0, 0, f)),
            pl.BlockSpec((nb, br, sg), lambda f: (0, 0, input_base + f)),
            pl.BlockSpec((nb, 8, 128), lambda f: (0, tap_base, 0)),
            pl.BlockSpec((None, 1, sg), lambda f: (f, 0, 0)),
        ],
        out_specs=[
            pl.BlockSpec((nb, out_rows if fold_rows else br, sg), lambda f: (0, 0, f)),
            pl.BlockSpec((None, nb, 2 * br), lambda f: (f, 0, 0)),
        ],
        out_shape=[
            jax.ShapeDtypeStruct((nb, out_rows, sw), jnp.bfloat16),
            jax.ShapeDtypeStruct((sf, nb, 2 * br), jnp.float32),
        ],
        scratch_shapes=[
            pltpu.VMEM((nb * br, sg), jnp.bfloat16),
            pltpu.VMEM((nb * br, sg), jnp.bfloat16),
        ],
    )(grad_in, input_in, tap_in, stretch_gain.reshape(sf, 1, sg))


def per_device(cached_input, cached_gate, out_grad, filter_taps, skip_gain):
    block_rows = cached_input.shape[0]
    chan_width = cached_input.shape[1]
    filters = filter_taps.shape[1]
    group_width = chan_width // filters
    seq_count = lax.axis_size("seq")
    seq_index = lax.axis_index("seq")
    length = block_rows * seq_count
    taps_scale = 1.0 / math.sqrt(length)
    stretch_width = chan_width // seq_count
    stretch_filters = max(1, stretch_width // group_width)
    stretch_group = stretch_width // stretch_filters
    tap_columns = np.array(
        [
            (target * stretch_width) // group_width + offset
            for target in range(seq_count)
            for offset in range(stretch_filters)
        ]
    )
    def gated_grad():
        product = out_grad.astype(jnp.float32) * cached_gate.astype(jnp.float32)
        return product.astype(jnp.bfloat16)

    if stretch_width % 128 == 0:
        per_step = seq_count // 2 if seq_count % 2 == 0 else seq_count
        column_block = pl.BlockSpec((block_rows, per_step * stretch_width), lambda j: (0, j))
        packed = pl.pallas_call(
            functools.partial(
                pack_kernel,
                br=block_rows,
                sw=stretch_width,
                sf=stretch_filters,
                gw=group_width,
                per_step=per_step,
            ),
            grid=(seq_count // per_step,),
            in_specs=[
                column_block,
                column_block,
                column_block,
                pl.BlockSpec((filters, block_rows), lambda j: (0, 0)),
            ],
            out_specs=pl.BlockSpec(
                (per_step, block_rows + 8, 2 * stretch_width), lambda j: (j, 0, 0)
            ),
            out_shape=jax.ShapeDtypeStruct(
                (seq_count, block_rows + 8, 2 * stretch_width), jnp.bfloat16
            ),
        )(out_grad, cached_gate, cached_input, jnp.transpose(filter_taps))
    else:
        routed_taps = jnp.transpose(filter_taps[:, tap_columns]).reshape(
            seq_count, stretch_filters, block_rows
        )
        tap_rows = jnp.pad(
            routed_taps,
            ((0, 0), (0, 8 - stretch_filters), (0, 2 * stretch_width - block_rows)),
        )
        body = jnp.concatenate(
            [
                jnp.transpose(gated_grad().reshape(block_rows, seq_count, stretch_width), (1, 0, 2)),
                jnp.transpose(cached_input.reshape(block_rows, seq_count, stretch_width), (1, 0, 2)),
            ],
            axis=2,
        )
        packed = jnp.concatenate([body, tap_rows], axis=1)
    arrived = [lax.dynamic_index_in_dim(packed, seq_index, 0, keepdims=True)]
    for shift in range(1, seq_count):
        chunk = lax.dynamic_index_in_dim(packed, (seq_index + shift) % seq_count, 0, keepdims=True)
        pairs = [(i, (i + shift) % seq_count) for i in range(seq_count)]
        arrived.append(lax.ppermute(chunk, "seq", pairs))
    moved = jnp.concatenate(arrived, axis=0)
    stretch_gain = lax.dynamic_slice_in_dim(skip_gain, seq_index * stretch_width, stretch_width, 0)
    used_rows = 3 * stretch_filters * block_rows // stretch_width
    extra_rows = -(-used_rows // 8) * 8
    local_grad, diag = local_grads(
        moved,
        stretch_gain,
        seq_count,
        block_rows,
        stretch_filters,
        stretch_group,
        taps_scale,
        block_rows + extra_rows,
    )
    if stretch_group % 128 == 0:
        outgoing = local_grad
    else:
        front = jnp.pad(diag[:, :, :block_rows], ((0, 0), (0, 1), (0, 0)))
        back = jnp.pad(diag[:, :, block_rows:], ((0, 0), (1, 0), (0, 0)))
        lag_sums = (front + back).reshape(stretch_filters, (seq_count + 1) * block_rows)
        stretch_term = lag_sums[:, block_rows - 1 : block_rows - 1 + length] * taps_scale
        high = lax.reduce_precision(stretch_term, exponent_bits=8, mantissa_bits=7)
        rest = stretch_term - high
        middle = lax.reduce_precision(rest, exponent_bits=8, mantissa_bits=7)
        low = rest - middle
        split = jnp.stack([high, middle, low], axis=0).astype(jnp.bfloat16)
        split = jnp.transpose(split.reshape(3, stretch_filters, seq_count, block_rows), (2, 0, 1, 3))
        split = split.reshape(seq_count, used_rows, stretch_width)
        split = jnp.pad(split, ((0, 0), (0, extra_rows - used_rows), (0, 0)))
        outgoing = lax.dynamic_update_slice_in_dim(local_grad, split, block_rows, 1)
    sharers = seq_count * stretch_filters // filters
    if stretch_group % 128 == 0:
        input_grad = jnp.zeros((block_rows, chan_width), outgoing.dtype)
        lag_slots = []
        for shift in range(seq_count):
            chunk = lax.dynamic_index_in_dim(
                outgoing, (seq_index - shift) % seq_count, 0, keepdims=False
            )
            if shift:
                pairs = [(i, (i - shift) % seq_count) for i in range(seq_count)]
                chunk = lax.ppermute(chunk, "seq", pairs)
            source = (seq_index + shift) % seq_count
            input_grad = lax.dynamic_update_slice_in_dim(
                input_grad, chunk[:block_rows], source * stretch_width, 1
            )
            rows = chunk[block_rows : block_rows + 3].astype(jnp.float32)
            rows = rows.reshape(3, stretch_filters, stretch_group)[..., :block_rows]
            lag_slots.append(rows[0] + rows[1] + rows[2])
        parts = jnp.roll(jnp.stack(lag_slots, axis=0), seq_index, axis=0)
    else:
        returned = lax.all_to_all(outgoing, "seq", split_axis=0, concat_axis=0, tiled=True)
        input_grad = jnp.transpose(returned[:, :block_rows, :], (1, 0, 2)).reshape(
            block_rows, chan_width
        )
        parts = returned[:, block_rows : block_rows + used_rows, :].astype(jnp.float32)
        parts = parts.reshape(seq_count, 3, stretch_filters, block_rows).sum(axis=1)
    filter_grad = jnp.transpose(
        parts.reshape(filters, sharers, block_rows).sum(axis=1)
    )
    return (input_grad, filter_grad)


def solution(mesh):
    return jax.shard_map(
        per_device,
        mesh=mesh,
        in_specs=(
            P(("groups", "seq"), "chan"),
            P(("groups", "seq"), "chan"),
            P(("groups", "seq"), "chan"),
            P("seq", "chan"),
            P("chan"),
        ),
        out_specs=(P(("groups", "seq"), "chan"), P(("groups", "seq"), "chan")),
        check_vma=False,
    )
```

```python
import functools
import math

import jax
import jax.numpy as jnp
import numpy as np
from jax import lax
from jax.experimental import pallas as pl
from jax.experimental.pallas import tpu as pltpu
from jax.sharding import PartitionSpec as P


def local_kernel(g_ref, x_ref, t_ref, gain_ref, out_ref, diag_ref, g_scr, xrev_ref, *, nb, br, scale, fold_rows):
    f = pl.program_id(0)
    me = lax.axis_index("seq")
    slot = [(me - i + nb) % nb for i in range(nb)]
    n = nb * br
    width = n + br
    pick = lax.broadcasted_iota(jnp.int32, (8, 128), 0) == f
    taps = jnp.concatenate(
        [jnp.zeros((1, br), jnp.float32)]
        + [
            jnp.sum(
                jnp.where(pick, t_ref[slot[j]].astype(jnp.float32), 0.0), axis=0, keepdims=True
            )
            for j in range(nb)
        ],
        axis=1,
    )
    taps_row = jnp.broadcast_to(taps, (br, width))
    toeplitz = pltpu.roll(taps_row, width - br, 1, stride=1, stride_axis=0)
    toeplitz = toeplitz[:, :n].astype(jnp.bfloat16)
    rows = lax.broadcasted_iota(jnp.int32, (br, br), 0)
    cols = lax.broadcasted_iota(jnp.int32, (br, br), 1)
    flip = (rows + cols == br - 1).astype(jnp.bfloat16)
    for i in range(nb):
        g_scr[i * br : (i + 1) * br, :] = g_ref[slot[i]]
        xrev_ref[i * br : (i + 1) * br, :] = jnp.dot(
            flip, x_ref[slot[i]], preferred_element_type=jnp.float32
        ).astype(xrev_ref.dtype)
    gain = gain_ref[...]
    for i in range(nb):
        conv = jnp.dot(
            toeplitz[:, : n - i * br], g_scr[i * br :, :], preferred_element_type=jnp.float32
        )
        own = g_scr[i * br : (i + 1) * br, :].astype(jnp.float32)
        out_ref[i, :br, :] = (conv * scale + gain * own).astype(out_ref.dtype)
    sums = [None] * nb
    for j in range(nb):
        row = lax.dot_general(
            g_scr[j * br : (j + 1) * br, :],
            xrev_ref[: (j + 1) * br, :],
            (((1,), (1,)), ((), ())),
            preferred_element_type=jnp.float32,
        )
        for i in range(j + 1):
            piece = row[:, i * br : (i + 1) * br]
            sums[j - i] = piece if sums[j - i] is None else sums[j - i] + piece
    zeros = jnp.zeros((br, br), jnp.float32)
    for k in range(nb):
        padded = jnp.concatenate([sums[k], zeros], axis=1)
        skewed = pltpu.roll(padded, 0, 1, stride=1, stride_axis=0)
        diag_ref[k : k + 1, :] = jnp.sum(skewed, axis=0, keepdims=True)
    if fold_rows:
        diag = diag_ref[...]
        own = pltpu.roll(diag, br + 1, 1)[:, :br]
        nxt = pltpu.roll(diag, 1, 1)[:, :br]
        nxt = jnp.concatenate([nxt[1:], jnp.zeros((1, br), jnp.float32)], axis=0)
        lag_term = (own + nxt) * scale
        high = lag_term.astype(jnp.bfloat16).astype(jnp.float32)
        rest = lag_term - high
        middle = rest.astype(jnp.bfloat16).astype(jnp.float32)
        low = rest - middle
        pick = lax.broadcasted_iota(jnp.int32, (nb, 8, br), 1)
        tile = jnp.where(
            pick == 0,
            high[:, None, :],
            jnp.where(pick == 1, middle[:, None, :], jnp.where(pick == 2, low[:, None, :], 0.0)),
        )
        out_ref[:, br : br + 8, :br] = tile.astype(out_ref.dtype)


def pack_kernel(og_ref, gate_ref, x_ref, taps_ref, out_ref, *, br, sw, sf, gw, per_step):
    filters = taps_ref.shape[0]
    rows = lax.broadcasted_iota(jnp.int32, (8, filters), 0)
    cols = lax.broadcasted_iota(jnp.int32, (8, filters), 1)
    for d in range(per_step):
        j = pl.program_id(0) * per_step + d
        span = slice(d * sw, (d + 1) * sw)
        gated = og_ref[:, span].astype(jnp.float32) * gate_ref[:, span].astype(jnp.float32)
        out_ref[d, :br, :sw] = gated.astype(out_ref.dtype)
        out_ref[d, :br, sw:] = x_ref[:, span]
        pick = ((cols == (j * sw) // gw + rows) & (rows < sf)).astype(jnp.bfloat16)
        tap_rows = jnp.dot(pick, taps_ref[...], preferred_element_type=jnp.float32)
        out_ref[d, br:, :br] = tap_rows.astype(out_ref.dtype)
        out_ref[d, br:, br:] = jnp.zeros((8, 2 * sw - br), out_ref.dtype)


def local_grads(moved, stretch_gain, nb, br, sf, sg, scale, out_rows):
    sw = sf * sg
    fold_rows = sg % 128 == 0
    if sg % 128 == 0:
        grad_in, input_in, input_base = moved, moved, sf
    else:
        grad_in = moved[:, :br, :sw]
        input_in = moved[:, :br, sw : 2 * sw]
        input_base = 0
    if sg % 128 == 0:
        tap_in, tap_base = moved, br // 8
    else:
        tap_in, tap_base = moved[:, br : br + 8, :128], 0
    return pl.pallas_call(
        functools.partial(local_kernel, nb=nb, br=br, scale=scale, fold_rows=fold_rows),
        grid=(sf,),
        in_specs=[
            pl.BlockSpec((nb, br, sg), lambda f: (0, 0, f)),
            pl.BlockSpec((nb, br, sg), lambda f: (0, 0, input_base + f)),
            pl.BlockSpec((nb, 8, 128), lambda f: (0, tap_base, 0)),
            pl.BlockSpec((None, 1, sg), lambda f: (f, 0, 0)),
        ],
        out_specs=[
            pl.BlockSpec((nb, out_rows if fold_rows else br, sg), lambda f: (0, 0, f)),
            pl.BlockSpec((None, nb, 2 * br), lambda f: (f, 0, 0)),
        ],
        out_shape=[
            jax.ShapeDtypeStruct((nb, out_rows, sw), jnp.bfloat16),
            jax.ShapeDtypeStruct((sf, nb, 2 * br), jnp.float32),
        ],
        scratch_shapes=[
            pltpu.VMEM((nb * br, sg), jnp.bfloat16),
            pltpu.VMEM((nb * br, sg), jnp.bfloat16),
        ],
    )(grad_in, input_in, tap_in, stretch_gain.reshape(sf, 1, sg))


def per_device(cached_input, cached_gate, out_grad, filter_taps, skip_gain):
    block_rows = cached_input.shape[0]
    chan_width = cached_input.shape[1]
    filters = filter_taps.shape[1]
    group_width = chan_width // filters
    seq_count = lax.axis_size("seq")
    seq_index = lax.axis_index("seq")
    length = block_rows * seq_count
    taps_scale = 1.0 / math.sqrt(length)
    stretch_width = chan_width // seq_count
    stretch_filters = max(1, stretch_width // group_width)
    stretch_group = stretch_width // stretch_filters
    tap_columns = np.array(
        [
            (target * stretch_width) // group_width + offset
            for target in range(seq_count)
            for offset in range(stretch_filters)
        ]
    )
    def gated_grad():
        product = out_grad.astype(jnp.float32) * cached_gate.astype(jnp.float32)
        return product.astype(jnp.bfloat16)

    if stretch_width % 128 == 0:
        per_step = seq_count // 2 if seq_count % 2 == 0 else seq_count
        column_block = pl.BlockSpec((block_rows, per_step * stretch_width), lambda j: (0, j))
        packed = pl.pallas_call(
            functools.partial(
                pack_kernel,
                br=block_rows,
                sw=stretch_width,
                sf=stretch_filters,
                gw=group_width,
                per_step=per_step,
            ),
            grid=(seq_count // per_step,),
            in_specs=[
                column_block,
                column_block,
                column_block,
                pl.BlockSpec((filters, block_rows), lambda j: (0, 0)),
            ],
            out_specs=pl.BlockSpec(
                (per_step, block_rows + 8, 2 * stretch_width), lambda j: (j, 0, 0)
            ),
            out_shape=jax.ShapeDtypeStruct(
                (seq_count, block_rows + 8, 2 * stretch_width), jnp.bfloat16
            ),
        )(out_grad, cached_gate, cached_input, jnp.transpose(filter_taps))
    else:
        routed_taps = jnp.transpose(filter_taps[:, tap_columns]).reshape(
            seq_count, stretch_filters, block_rows
        )
        tap_rows = jnp.pad(
            routed_taps,
            ((0, 0), (0, 8 - stretch_filters), (0, 2 * stretch_width - block_rows)),
        )
        body = jnp.concatenate(
            [
                jnp.transpose(gated_grad().reshape(block_rows, seq_count, stretch_width), (1, 0, 2)),
                jnp.transpose(cached_input.reshape(block_rows, seq_count, stretch_width), (1, 0, 2)),
            ],
            axis=2,
        )
        packed = jnp.concatenate([body, tap_rows], axis=1)
    order = []
    for step in range(1, seq_count // 2 + 1):
        order += [step] if step == seq_count - step else [step, seq_count - step]
    arrived = [None] * seq_count
    arrived[0] = lax.dynamic_index_in_dim(packed, seq_index, 0, keepdims=True)
    for shift in order:
        chunk = lax.dynamic_index_in_dim(packed, (seq_index + shift) % seq_count, 0, keepdims=True)
        pairs = [(i, (i + shift) % seq_count) for i in range(seq_count)]
        arrived[shift] = lax.ppermute(chunk, "seq", pairs)
    moved = jnp.concatenate(arrived, axis=0)
    stretch_gain = lax.dynamic_slice_in_dim(skip_gain, seq_index * stretch_width, stretch_width, 0)
    used_rows = 3 * stretch_filters * block_rows // stretch_width
    extra_rows = -(-used_rows // 8) * 8
    local_grad, diag = local_grads(
        moved,
        stretch_gain,
        seq_count,
        block_rows,
        stretch_filters,
        stretch_group,
        taps_scale,
        block_rows + extra_rows,
    )
    if stretch_group % 128 == 0:
        outgoing = local_grad
    else:
        front = jnp.pad(diag[:, :, :block_rows], ((0, 0), (0, 1), (0, 0)))
        back = jnp.pad(diag[:, :, block_rows:], ((0, 0), (1, 0), (0, 0)))
        lag_sums = (front + back).reshape(stretch_filters, (seq_count + 1) * block_rows)
        stretch_term = lag_sums[:, block_rows - 1 : block_rows - 1 + length] * taps_scale
        high = lax.reduce_precision(stretch_term, exponent_bits=8, mantissa_bits=7)
        rest = stretch_term - high
        middle = lax.reduce_precision(rest, exponent_bits=8, mantissa_bits=7)
        low = rest - middle
        split = jnp.stack([high, middle, low], axis=0).astype(jnp.bfloat16)
        split = jnp.transpose(split.reshape(3, stretch_filters, seq_count, block_rows), (2, 0, 1, 3))
        split = split.reshape(seq_count, used_rows, stretch_width)
        split = jnp.pad(split, ((0, 0), (0, extra_rows - used_rows), (0, 0)))
        outgoing = lax.dynamic_update_slice_in_dim(local_grad, split, block_rows, 1)
    sharers = seq_count * stretch_filters // filters
    if stretch_group % 128 == 0:
        input_grad = jnp.zeros((block_rows, chan_width), outgoing.dtype)
        lag_slots = []
        for shift in range(seq_count):
            chunk = lax.dynamic_index_in_dim(
                outgoing, (seq_index - shift) % seq_count, 0, keepdims=False
            )
            if shift:
                pairs = [(i, (i - shift) % seq_count) for i in range(seq_count)]
                chunk = lax.ppermute(chunk, "seq", pairs)
            source = (seq_index + shift) % seq_count
            input_grad = lax.dynamic_update_slice_in_dim(
                input_grad, chunk[:block_rows], source * stretch_width, 1
            )
            rows = chunk[block_rows : block_rows + 3].astype(jnp.float32)
            rows = rows.reshape(3, stretch_filters, stretch_group)[..., :block_rows]
            lag_slots.append(rows[0] + rows[1] + rows[2])
        parts = jnp.roll(jnp.stack(lag_slots, axis=0), seq_index, axis=0)
    else:
        returned = lax.all_to_all(outgoing, "seq", split_axis=0, concat_axis=0, tiled=True)
        input_grad = jnp.transpose(returned[:, :block_rows, :], (1, 0, 2)).reshape(
            block_rows, chan_width
        )
        parts = returned[:, block_rows : block_rows + used_rows, :].astype(jnp.float32)
        parts = parts.reshape(seq_count, 3, stretch_filters, block_rows).sum(axis=1)
    filter_grad = jnp.transpose(
        parts.reshape(filters, sharers, block_rows).sum(axis=1)
    )
    return (input_grad, filter_grad)


def solution(mesh):
    return jax.shard_map(
        per_device,
        mesh=mesh,
        in_specs=(
            P(("groups", "seq"), "chan"),
            P(("groups", "seq"), "chan"),
            P(("groups", "seq"), "chan"),
            P("seq", "chan"),
            P("chan"),
        ),
        out_specs=(P(("groups", "seq"), "chan"), P(("groups", "seq"), "chan")),
        check_vma=False,
    )
```

```python
import functools
import math

import jax
import jax.numpy as jnp
import numpy as np
from jax import lax
from jax.experimental import pallas as pl
from jax.experimental.pallas import tpu as pltpu
from jax.sharding import PartitionSpec as P


def local_kernel(g_ref, x_ref, t_ref, gain_ref, out_ref, diag_ref, g_scr, xrev_ref, gt_ref, *, nb, br, sg, scale, fold_rows):
    f = pl.program_id(0)
    me = lax.axis_index("seq")
    slot = [(me - i + nb) % nb for i in range(nb)]
    n = nb * br
    width = n + br
    pick = lax.broadcasted_iota(jnp.int32, (8, 128), 0) == f
    taps = jnp.concatenate(
        [jnp.zeros((1, br), jnp.float32)]
        + [
            jnp.sum(
                jnp.where(pick, t_ref[slot[j]].astype(jnp.float32), 0.0), axis=0, keepdims=True
            )
            for j in range(nb)
        ],
        axis=1,
    )
    taps_row = jnp.broadcast_to(taps, (br, width))
    toeplitz = pltpu.roll(taps_row, width - br, 1, stride=1, stride_axis=0)
    toeplitz = toeplitz[:, :n].astype(jnp.bfloat16)
    rows = lax.broadcasted_iota(jnp.int32, (br, br), 0)
    cols = lax.broadcasted_iota(jnp.int32, (br, br), 1)
    flip = (rows + cols == br - 1).astype(jnp.bfloat16)
    for i in range(nb):
        g_scr[i * br : (i + 1) * br, :] = g_ref[slot[i]]
        flipped = jnp.dot(flip, x_ref[slot[i]], preferred_element_type=jnp.float32)
        if fold_rows:
            gt_ref[:, i * sg : (i + 1) * sg] = g_ref[slot[i]]
            xrev_ref[:, i * sg : (i + 1) * sg] = flipped.astype(xrev_ref.dtype)
        else:
            xrev_ref[i * br : (i + 1) * br, :] = flipped.astype(xrev_ref.dtype)
    gain = gain_ref[...]
    for i in range(nb):
        conv = jnp.dot(
            toeplitz[:, : n - i * br], g_scr[i * br :, :], preferred_element_type=jnp.float32
        )
        own = g_scr[i * br : (i + 1) * br, :].astype(jnp.float32)
        out_ref[i, :br, :] = (conv * scale + gain * own).astype(out_ref.dtype)
    sums = [None] * nb
    if fold_rows:
        for k in range(nb):
            sums[k] = lax.dot_general(
                gt_ref[:, k * sg :],
                xrev_ref[:, : (nb - k) * sg],
                (((1,), (1,)), ((), ())),
                preferred_element_type=jnp.float32,
            )
    else:
        for j in range(nb):
            row = lax.dot_general(
                g_scr[j * br : (j + 1) * br, :],
                xrev_ref[: (j + 1) * br, :],
                (((1,), (1,)), ((), ())),
                preferred_element_type=jnp.float32,
            )
            for i in range(j + 1):
                piece = row[:, i * br : (i + 1) * br]
                sums[j - i] = piece if sums[j - i] is None else sums[j - i] + piece
    zeros = jnp.zeros((br, br), jnp.float32)
    for k in range(nb):
        padded = jnp.concatenate([sums[k], zeros], axis=1)
        skewed = pltpu.roll(padded, 0, 1, stride=1, stride_axis=0)
        diag_ref[k : k + 1, :] = jnp.sum(skewed, axis=0, keepdims=True)
    if fold_rows:
        diag = diag_ref[...]
        own = pltpu.roll(diag, br + 1, 1)[:, :br]
        nxt = pltpu.roll(diag, 1, 1)[:, :br]
        nxt = jnp.concatenate([nxt[1:], jnp.zeros((1, br), jnp.float32)], axis=0)
        lag_term = (own + nxt) * scale
        high = lag_term.astype(jnp.bfloat16).astype(jnp.float32)
        rest = lag_term - high
        middle = rest.astype(jnp.bfloat16).astype(jnp.float32)
        low = rest - middle
        pick = lax.broadcasted_iota(jnp.int32, (nb, 8, br), 1)
        tile = jnp.where(
            pick == 0,
            high[:, None, :],
            jnp.where(pick == 1, middle[:, None, :], jnp.where(pick == 2, low[:, None, :], 0.0)),
        )
        out_ref[:, br : br + 8, :br] = tile.astype(out_ref.dtype)


def pack_kernel(og_ref, gate_ref, x_ref, taps_ref, out_ref, *, br, sw, sf, gw, per_step):
    filters = taps_ref.shape[0]
    rows = lax.broadcasted_iota(jnp.int32, (8, filters), 0)
    cols = lax.broadcasted_iota(jnp.int32, (8, filters), 1)
    for d in range(per_step):
        j = pl.program_id(0) * per_step + d
        span = slice(d * sw, (d + 1) * sw)
        gated = og_ref[:, span].astype(jnp.float32) * gate_ref[:, span].astype(jnp.float32)
        out_ref[d, :br, :sw] = gated.astype(out_ref.dtype)
        out_ref[d, :br, sw:] = x_ref[:, span]
        pick = ((cols == (j * sw) // gw + rows) & (rows < sf)).astype(jnp.bfloat16)
        tap_rows = jnp.dot(pick, taps_ref[...], preferred_element_type=jnp.float32)
        out_ref[d, br:, :br] = tap_rows.astype(out_ref.dtype)
        out_ref[d, br:, br:] = jnp.zeros((8, 2 * sw - br), out_ref.dtype)


def local_grads(moved, stretch_gain, nb, br, sf, sg, scale, out_rows):
    sw = sf * sg
    fold_rows = sg % 128 == 0
    if sg % 128 == 0:
        grad_in, input_in, input_base = moved, moved, sf
    else:
        grad_in = moved[:, :br, :sw]
        input_in = moved[:, :br, sw : 2 * sw]
        input_base = 0
    if sg % 128 == 0:
        tap_in, tap_base = moved, br // 8
    else:
        tap_in, tap_base = moved[:, br : br + 8, :128], 0
    return pl.pallas_call(
        functools.partial(local_kernel, nb=nb, br=br, sg=sg, scale=scale, fold_rows=fold_rows),
        grid=(sf,),
        in_specs=[
            pl.BlockSpec((nb, br, sg), lambda f: (0, 0, f)),
            pl.BlockSpec((nb, br, sg), lambda f: (0, 0, input_base + f)),
            pl.BlockSpec((nb, 8, 128), lambda f: (0, tap_base, 0)),
            pl.BlockSpec((None, 1, sg), lambda f: (f, 0, 0)),
        ],
        out_specs=[
            pl.BlockSpec((nb, out_rows if fold_rows else br, sg), lambda f: (0, 0, f)),
            pl.BlockSpec((None, nb, 2 * br), lambda f: (f, 0, 0)),
        ],
        out_shape=[
            jax.ShapeDtypeStruct((nb, out_rows, sw), jnp.bfloat16),
            jax.ShapeDtypeStruct((sf, nb, 2 * br), jnp.float32),
        ],
        scratch_shapes=[
            pltpu.VMEM((nb * br, sg), jnp.bfloat16),
            pltpu.VMEM((br, nb * sg) if fold_rows else (nb * br, sg), jnp.bfloat16),
            pltpu.VMEM((br, nb * sg) if fold_rows else (8, 128), jnp.bfloat16),
        ],
    )(grad_in, input_in, tap_in, stretch_gain.reshape(sf, 1, sg))


def per_device(cached_input, cached_gate, out_grad, filter_taps, skip_gain):
    block_rows = cached_input.shape[0]
    chan_width = cached_input.shape[1]
    filters = filter_taps.shape[1]
    group_width = chan_width // filters
    seq_count = lax.axis_size("seq")
    seq_index = lax.axis_index("seq")
    length = block_rows * seq_count
    taps_scale = 1.0 / math.sqrt(length)
    stretch_width = chan_width // seq_count
    stretch_filters = max(1, stretch_width // group_width)
    stretch_group = stretch_width // stretch_filters
    tap_columns = np.array(
        [
            (target * stretch_width) // group_width + offset
            for target in range(seq_count)
            for offset in range(stretch_filters)
        ]
    )
    def gated_grad():
        product = out_grad.astype(jnp.float32) * cached_gate.astype(jnp.float32)
        return product.astype(jnp.bfloat16)

    if stretch_width % 128 == 0:
        per_step = seq_count // 2 if seq_count % 2 == 0 else seq_count
        column_block = pl.BlockSpec((block_rows, per_step * stretch_width), lambda j: (0, j))
        packed = pl.pallas_call(
            functools.partial(
                pack_kernel,
                br=block_rows,
                sw=stretch_width,
                sf=stretch_filters,
                gw=group_width,
                per_step=per_step,
            ),
            grid=(seq_count // per_step,),
            in_specs=[
                column_block,
                column_block,
                column_block,
                pl.BlockSpec((filters, block_rows), lambda j: (0, 0)),
            ],
            out_specs=pl.BlockSpec(
                (per_step, block_rows + 8, 2 * stretch_width), lambda j: (j, 0, 0)
            ),
            out_shape=jax.ShapeDtypeStruct(
                (seq_count, block_rows + 8, 2 * stretch_width), jnp.bfloat16
            ),
        )(out_grad, cached_gate, cached_input, jnp.transpose(filter_taps))
    else:
        routed_taps = jnp.transpose(filter_taps[:, tap_columns]).reshape(
            seq_count, stretch_filters, block_rows
        )
        tap_rows = jnp.pad(
            routed_taps,
            ((0, 0), (0, 8 - stretch_filters), (0, 2 * stretch_width - block_rows)),
        )
        body = jnp.concatenate(
            [
                jnp.transpose(gated_grad().reshape(block_rows, seq_count, stretch_width), (1, 0, 2)),
                jnp.transpose(cached_input.reshape(block_rows, seq_count, stretch_width), (1, 0, 2)),
            ],
            axis=2,
        )
        packed = jnp.concatenate([body, tap_rows], axis=1)
    order = []
    for step in range(1, seq_count // 2 + 1):
        order += [step] if step == seq_count - step else [step, seq_count - step]
    arrived = [None] * seq_count
    arrived[0] = lax.dynamic_index_in_dim(packed, seq_index, 0, keepdims=True)
    for shift in order:
        chunk = lax.dynamic_index_in_dim(packed, (seq_index + shift) % seq_count, 0, keepdims=True)
        pairs = [(i, (i + shift) % seq_count) for i in range(seq_count)]
        arrived[shift] = lax.ppermute(chunk, "seq", pairs)
    moved = jnp.concatenate(arrived, axis=0)
    stretch_gain = lax.dynamic_slice_in_dim(skip_gain, seq_index * stretch_width, stretch_width, 0)
    used_rows = 3 * stretch_filters * block_rows // stretch_width
    extra_rows = -(-used_rows // 8) * 8
    local_grad, diag = local_grads(
        moved,
        stretch_gain,
        seq_count,
        block_rows,
        stretch_filters,
        stretch_group,
        taps_scale,
        block_rows + extra_rows,
    )
    if stretch_group % 128 == 0:
        outgoing = local_grad
    else:
        front = jnp.pad(diag[:, :, :block_rows], ((0, 0), (0, 1), (0, 0)))
        back = jnp.pad(diag[:, :, block_rows:], ((0, 0), (1, 0), (0, 0)))
        lag_sums = (front + back).reshape(stretch_filters, (seq_count + 1) * block_rows)
        stretch_term = lag_sums[:, block_rows - 1 : block_rows - 1 + length] * taps_scale
        high = lax.reduce_precision(stretch_term, exponent_bits=8, mantissa_bits=7)
        rest = stretch_term - high
        middle = lax.reduce_precision(rest, exponent_bits=8, mantissa_bits=7)
        low = rest - middle
        split = jnp.stack([high, middle, low], axis=0).astype(jnp.bfloat16)
        split = jnp.transpose(split.reshape(3, stretch_filters, seq_count, block_rows), (2, 0, 1, 3))
        split = split.reshape(seq_count, used_rows, stretch_width)
        split = jnp.pad(split, ((0, 0), (0, extra_rows - used_rows), (0, 0)))
        outgoing = lax.dynamic_update_slice_in_dim(local_grad, split, block_rows, 1)
    sharers = seq_count * stretch_filters // filters
    if stretch_group % 128 == 0:
        input_grad = jnp.zeros((block_rows, chan_width), outgoing.dtype)
        lag_slots = []
        for shift in range(seq_count):
            chunk = lax.dynamic_index_in_dim(
                outgoing, (seq_index - shift) % seq_count, 0, keepdims=False
            )
            if shift:
                pairs = [(i, (i - shift) % seq_count) for i in range(seq_count)]
                chunk = lax.ppermute(chunk, "seq", pairs)
            source = (seq_index + shift) % seq_count
            input_grad = lax.dynamic_update_slice_in_dim(
                input_grad, chunk[:block_rows], source * stretch_width, 1
            )
            rows = chunk[block_rows : block_rows + 3].astype(jnp.float32)
            rows = rows.reshape(3, stretch_filters, stretch_group)[..., :block_rows]
            lag_slots.append(rows[0] + rows[1] + rows[2])
        parts = jnp.roll(jnp.stack(lag_slots, axis=0), seq_index, axis=0)
    else:
        returned = lax.all_to_all(outgoing, "seq", split_axis=0, concat_axis=0, tiled=True)
        input_grad = jnp.transpose(returned[:, :block_rows, :], (1, 0, 2)).reshape(
            block_rows, chan_width
        )
        parts = returned[:, block_rows : block_rows + used_rows, :].astype(jnp.float32)
        parts = parts.reshape(seq_count, 3, stretch_filters, block_rows).sum(axis=1)
    filter_grad = jnp.transpose(
        parts.reshape(filters, sharers, block_rows).sum(axis=1)
    )
    return (input_grad, filter_grad)


def solution(mesh):
    return jax.shard_map(
        per_device,
        mesh=mesh,
        in_specs=(
            P(("groups", "seq"), "chan"),
            P(("groups", "seq"), "chan"),
            P(("groups", "seq"), "chan"),
            P("seq", "chan"),
            P("chan"),
        ),
        out_specs=(P(("groups", "seq"), "chan"), P(("groups", "seq"), "chan")),
        check_vma=False,
    )
```

```python
import functools
import math

import jax
import jax.numpy as jnp
import numpy as np
from jax import lax
from jax.experimental import pallas as pl
from jax.experimental.pallas import tpu as pltpu
from jax.sharding import PartitionSpec as P


def filter_pass(g_ref, x_ref, t_ref, gain_ref, out_ref, diag_ref, g_scr, xrev_ref, gt_ref, f, nb, br, sg, scale, fold_rows):
    me = lax.axis_index("seq")
    slot = [(me - i + nb) % nb for i in range(nb)]
    n = nb * br
    width = n + br
    pick = lax.broadcasted_iota(jnp.int32, (8, 128), 0) == f
    taps = jnp.concatenate(
        [jnp.zeros((1, br), jnp.float32)]
        + [
            jnp.sum(
                jnp.where(pick, t_ref[slot[j]].astype(jnp.float32), 0.0), axis=0, keepdims=True
            )
            for j in range(nb)
        ],
        axis=1,
    )
    taps_row = jnp.broadcast_to(taps, (br, width))
    toeplitz = pltpu.roll(taps_row, width - br, 1, stride=1, stride_axis=0)
    toeplitz = toeplitz[:, :n].astype(jnp.bfloat16)
    rows = lax.broadcasted_iota(jnp.int32, (br, br), 0)
    cols = lax.broadcasted_iota(jnp.int32, (br, br), 1)
    flip = (rows + cols == br - 1).astype(jnp.bfloat16)
    for i in range(nb):
        g_scr[i * br : (i + 1) * br, :] = g_ref[slot[i]]
        flipped = jnp.dot(flip, x_ref[slot[i]], preferred_element_type=jnp.float32)
        if fold_rows:
            gt_ref[:, i * sg : (i + 1) * sg] = g_ref[slot[i]]
            xrev_ref[:, i * sg : (i + 1) * sg] = flipped.astype(xrev_ref.dtype)
        else:
            xrev_ref[i * br : (i + 1) * br, :] = flipped.astype(xrev_ref.dtype)
    gain = gain_ref[...]
    for i in range(nb):
        conv = jnp.dot(
            toeplitz[:, : n - i * br], g_scr[i * br :, :], preferred_element_type=jnp.float32
        )
        own = g_scr[i * br : (i + 1) * br, :].astype(jnp.float32)
        out_ref[i, :br, :] = (conv * scale + gain * own).astype(out_ref.dtype)
    sums = [None] * nb
    if fold_rows:
        for k in range(nb):
            sums[k] = lax.dot_general(
                gt_ref[:, k * sg :],
                xrev_ref[:, : (nb - k) * sg],
                (((1,), (1,)), ((), ())),
                preferred_element_type=jnp.float32,
            )
    else:
        for j in range(nb):
            row = lax.dot_general(
                g_scr[j * br : (j + 1) * br, :],
                xrev_ref[: (j + 1) * br, :],
                (((1,), (1,)), ((), ())),
                preferred_element_type=jnp.float32,
            )
            for i in range(j + 1):
                piece = row[:, i * br : (i + 1) * br]
                sums[j - i] = piece if sums[j - i] is None else sums[j - i] + piece
    zeros = jnp.zeros((br, br), jnp.float32)
    for k in range(nb):
        padded = jnp.concatenate([sums[k], zeros], axis=1)
        skewed = pltpu.roll(padded, 0, 1, stride=1, stride_axis=0)
        diag_ref[k : k + 1, :] = jnp.sum(skewed, axis=0, keepdims=True)
    if fold_rows:
        diag = diag_ref[...]
        own = pltpu.roll(diag, br + 1, 1)[:, :br]
        nxt = pltpu.roll(diag, 1, 1)[:, :br]
        nxt = jnp.concatenate([nxt[1:], jnp.zeros((1, br), jnp.float32)], axis=0)
        lag_term = (own + nxt) * scale
        high = lag_term.astype(jnp.bfloat16).astype(jnp.float32)
        rest = lag_term - high
        middle = rest.astype(jnp.bfloat16).astype(jnp.float32)
        low = rest - middle
        pick = lax.broadcasted_iota(jnp.int32, (nb, 8, br), 1)
        tile = jnp.where(
            pick == 0,
            high[:, None, :],
            jnp.where(pick == 1, middle[:, None, :], jnp.where(pick == 2, low[:, None, :], 0.0)),
        )
        out_ref[:, br : br + 8, :br] = tile.astype(out_ref.dtype)


def pack_kernel(og_ref, gate_ref, x_ref, taps_ref, out_ref, *, br, sw, sf, gw, per_step):
    filters = taps_ref.shape[0]
    rows = lax.broadcasted_iota(jnp.int32, (8, filters), 0)
    cols = lax.broadcasted_iota(jnp.int32, (8, filters), 1)
    for d in range(per_step):
        j = pl.program_id(0) * per_step + d
        span = slice(d * sw, (d + 1) * sw)
        gated = og_ref[:, span].astype(jnp.float32) * gate_ref[:, span].astype(jnp.float32)
        out_ref[d, :br, :sw] = gated.astype(out_ref.dtype)
        out_ref[d, :br, sw:] = x_ref[:, span]
        pick = ((cols == (j * sw) // gw + rows) & (rows < sf)).astype(jnp.bfloat16)
        tap_rows = jnp.dot(pick, taps_ref[...], preferred_element_type=jnp.float32)
        out_ref[d, br:, :br] = tap_rows.astype(out_ref.dtype)
        out_ref[d, br:, br:] = jnp.zeros((8, 2 * sw - br), out_ref.dtype)


def local_kernel(g_ref, x_ref, t_ref, gain_ref, out_ref, diag_ref, g_scr, xrev_ref, gt_ref, *, nb, br, sf, sg, x_base, t_base, scale, fold_rows):
    for f in range(sf):
        filter_pass(
            g_ref.at[:, :br, f * sg : (f + 1) * sg],
            x_ref.at[:, :br, x_base + f * sg : x_base + (f + 1) * sg],
            t_ref.at[:, t_base : t_base + 8, :128],
            gain_ref.at[f],
            out_ref.at[:, :, f * sg : (f + 1) * sg],
            diag_ref.at[f],
            g_scr,
            xrev_ref,
            gt_ref,
            f,
            nb,
            br,
            sg,
            scale,
            fold_rows,
        )


def local_grads(moved, stretch_gain, nb, br, sf, sg, scale, out_rows):
    sw = sf * sg
    fold_rows = sg % 128 == 0
    if fold_rows:
        operands = (moved,)
        x_base, t_base = sw, br
    else:
        operands = (moved[:, :br, :sw], moved[:, :br, sw : 2 * sw], moved[:, br : br + 8, :128])
        x_base, t_base = 0, 0
    def body(*refs):
        if fold_rows:
            refs = refs[:1] * 3 + refs[1:]
        local_kernel(*refs, **params)

    params = dict(
        nb=nb,
        br=br,
        sf=sf,
        sg=sg,
        x_base=x_base,
        t_base=t_base,
        scale=scale,
        fold_rows=fold_rows,
    )
    return pl.pallas_call(
        body,
        out_shape=[
            jax.ShapeDtypeStruct((nb, out_rows, sw), jnp.bfloat16),
            jax.ShapeDtypeStruct((sf, nb, 2 * br), jnp.float32),
        ],
        scratch_shapes=[
            pltpu.VMEM((nb * br, sg), jnp.bfloat16),
            pltpu.VMEM((br, nb * sg) if fold_rows else (nb * br, sg), jnp.bfloat16),
            pltpu.VMEM((br, nb * sg) if fold_rows else (8, 128), jnp.bfloat16),
        ],
    )(*operands, stretch_gain.reshape(sf, 1, sg))


def per_device(cached_input, cached_gate, out_grad, filter_taps, skip_gain):
    block_rows = cached_input.shape[0]
    chan_width = cached_input.shape[1]
    filters = filter_taps.shape[1]
    group_width = chan_width // filters
    seq_count = lax.axis_size("seq")
    seq_index = lax.axis_index("seq")
    length = block_rows * seq_count
    taps_scale = 1.0 / math.sqrt(length)
    stretch_width = chan_width // seq_count
    stretch_filters = max(1, stretch_width // group_width)
    stretch_group = stretch_width // stretch_filters
    tap_columns = np.array(
        [
            (target * stretch_width) // group_width + offset
            for target in range(seq_count)
            for offset in range(stretch_filters)
        ]
    )
    def gated_grad():
        product = out_grad.astype(jnp.float32) * cached_gate.astype(jnp.float32)
        return product.astype(jnp.bfloat16)

    if stretch_width % 128 == 0:
        per_step = seq_count // 2 if seq_count % 2 == 0 else seq_count
        column_block = pl.BlockSpec((block_rows, per_step * stretch_width), lambda j: (0, j))
        packed = pl.pallas_call(
            functools.partial(
                pack_kernel,
                br=block_rows,
                sw=stretch_width,
                sf=stretch_filters,
                gw=group_width,
                per_step=per_step,
            ),
            grid=(seq_count // per_step,),
            in_specs=[
                column_block,
                column_block,
                column_block,
                pl.BlockSpec((filters, block_rows), lambda j: (0, 0)),
            ],
            out_specs=pl.BlockSpec(
                (per_step, block_rows + 8, 2 * stretch_width), lambda j: (j, 0, 0)
            ),
            out_shape=jax.ShapeDtypeStruct(
                (seq_count, block_rows + 8, 2 * stretch_width), jnp.bfloat16
            ),
        )(out_grad, cached_gate, cached_input, jnp.transpose(filter_taps))
    else:
        routed_taps = jnp.transpose(filter_taps[:, tap_columns]).reshape(
            seq_count, stretch_filters, block_rows
        )
        tap_rows = jnp.pad(
            routed_taps,
            ((0, 0), (0, 8 - stretch_filters), (0, 2 * stretch_width - block_rows)),
        )
        body = jnp.concatenate(
            [
                jnp.transpose(gated_grad().reshape(block_rows, seq_count, stretch_width), (1, 0, 2)),
                jnp.transpose(cached_input.reshape(block_rows, seq_count, stretch_width), (1, 0, 2)),
            ],
            axis=2,
        )
        packed = jnp.concatenate([body, tap_rows], axis=1)
    order = []
    for step in range(1, seq_count // 2 + 1):
        order += [step] if step == seq_count - step else [step, seq_count - step]
    arrived = [None] * seq_count
    arrived[0] = lax.dynamic_index_in_dim(packed, seq_index, 0, keepdims=True)
    for shift in order:
        chunk = lax.dynamic_index_in_dim(packed, (seq_index + shift) % seq_count, 0, keepdims=True)
        pairs = [(i, (i + shift) % seq_count) for i in range(seq_count)]
        arrived[shift] = lax.ppermute(chunk, "seq", pairs)
    moved = jnp.concatenate(arrived, axis=0)
    stretch_gain = lax.dynamic_slice_in_dim(skip_gain, seq_index * stretch_width, stretch_width, 0)
    used_rows = 3 * stretch_filters * block_rows // stretch_width
    extra_rows = -(-used_rows // 8) * 8
    local_grad, diag = local_grads(
        moved,
        stretch_gain,
        seq_count,
        block_rows,
        stretch_filters,
        stretch_group,
        taps_scale,
        block_rows + extra_rows,
    )
    if stretch_group % 128 == 0:
        outgoing = local_grad
    else:
        front = jnp.pad(diag[:, :, :block_rows], ((0, 0), (0, 1), (0, 0)))
        back = jnp.pad(diag[:, :, block_rows:], ((0, 0), (1, 0), (0, 0)))
        lag_sums = (front + back).reshape(stretch_filters, (seq_count + 1) * block_rows)
        stretch_term = lag_sums[:, block_rows - 1 : block_rows - 1 + length] * taps_scale
        high = lax.reduce_precision(stretch_term, exponent_bits=8, mantissa_bits=7)
        rest = stretch_term - high
        middle = lax.reduce_precision(rest, exponent_bits=8, mantissa_bits=7)
        low = rest - middle
        split = jnp.stack([high, middle, low], axis=0).astype(jnp.bfloat16)
        split = jnp.transpose(split.reshape(3, stretch_filters, seq_count, block_rows), (2, 0, 1, 3))
        split = split.reshape(seq_count, used_rows, stretch_width)
        split = jnp.pad(split, ((0, 0), (0, extra_rows - used_rows), (0, 0)))
        outgoing = lax.dynamic_update_slice_in_dim(local_grad, split, block_rows, 1)
    sharers = seq_count * stretch_filters // filters
    if stretch_group % 128 == 0:
        input_grad = jnp.zeros((block_rows, chan_width), outgoing.dtype)
        lag_slots = []
        for shift in range(seq_count):
            chunk = lax.dynamic_index_in_dim(
                outgoing, (seq_index - shift) % seq_count, 0, keepdims=False
            )
            if shift:
                pairs = [(i, (i - shift) % seq_count) for i in range(seq_count)]
                chunk = lax.ppermute(chunk, "seq", pairs)
            source = (seq_index + shift) % seq_count
            input_grad = lax.dynamic_update_slice_in_dim(
                input_grad, chunk[:block_rows], source * stretch_width, 1
            )
            rows = chunk[block_rows : block_rows + 3].astype(jnp.float32)
            rows = rows.reshape(3, stretch_filters, stretch_group)[..., :block_rows]
            lag_slots.append(rows[0] + rows[1] + rows[2])
        parts = jnp.roll(jnp.stack(lag_slots, axis=0), seq_index, axis=0)
    else:
        returned = lax.all_to_all(outgoing, "seq", split_axis=0, concat_axis=0, tiled=True)
        input_grad = jnp.transpose(returned[:, :block_rows, :], (1, 0, 2)).reshape(
            block_rows, chan_width
        )
        parts = returned[:, block_rows : block_rows + used_rows, :].astype(jnp.float32)
        parts = parts.reshape(seq_count, 3, stretch_filters, block_rows).sum(axis=1)
    filter_grad = jnp.transpose(
        parts.reshape(filters, sharers, block_rows).sum(axis=1)
    )
    return (input_grad, filter_grad)


def solution(mesh):
    return jax.shard_map(
        per_device,
        mesh=mesh,
        in_specs=(
            P(("groups", "seq"), "chan"),
            P(("groups", "seq"), "chan"),
            P(("groups", "seq"), "chan"),
            P("seq", "chan"),
            P("chan"),
        ),
        out_specs=(P(("groups", "seq"), "chan"), P(("groups", "seq"), "chan")),
        check_vma=False,
    )
```

```python
import functools
import math

import jax
import jax.numpy as jnp
import numpy as np
from jax import lax
from jax.experimental import pallas as pl
from jax.experimental.pallas import tpu as pltpu
from jax.sharding import PartitionSpec as P


def filter_pass(g_ref, x_ref, t_ref, gain_ref, out_ref, diag_ref, g_scr, xrev_ref, gt_ref, f, nb, br, sg, scale, fold_rows):
    me = lax.axis_index("seq")
    slot = [(me - i + nb) % nb for i in range(nb)]
    n = nb * br
    width = n + br
    pick = lax.broadcasted_iota(jnp.int32, (8, 128), 0) == f
    taps = jnp.concatenate(
        [jnp.zeros((1, br), jnp.float32)]
        + [
            jnp.sum(
                jnp.where(pick, t_ref[slot[j]].astype(jnp.float32), 0.0), axis=0, keepdims=True
            )
            for j in range(nb)
        ],
        axis=1,
    )
    taps_row = jnp.broadcast_to(taps, (br, width))
    toeplitz = pltpu.roll(taps_row, width - br, 1, stride=1, stride_axis=0)
    toeplitz = toeplitz[:, :n].astype(jnp.bfloat16)
    rows = lax.broadcasted_iota(jnp.int32, (br, br), 0)
    cols = lax.broadcasted_iota(jnp.int32, (br, br), 1)
    flip = (rows + cols == br - 1).astype(jnp.bfloat16)
    for i in range(nb):
        g_scr[i * br : (i + 1) * br, :] = g_ref[slot[i]]
        flipped = jnp.dot(flip, x_ref[slot[i]], preferred_element_type=jnp.float32)
        if fold_rows:
            gt_ref[:, i * sg : (i + 1) * sg] = g_ref[slot[i]]
            xrev_ref[:, i * sg : (i + 1) * sg] = flipped.astype(xrev_ref.dtype)
        else:
            xrev_ref[i * br : (i + 1) * br, :] = flipped.astype(xrev_ref.dtype)
    gain = gain_ref[me, :, f * sg : (f + 1) * sg]
    for i in range(nb):
        conv = jnp.dot(
            toeplitz[:, : n - i * br], g_scr[i * br :, :], preferred_element_type=jnp.float32
        )
        own = g_scr[i * br : (i + 1) * br, :].astype(jnp.float32)
        out_ref[i, :br, :] = (conv * scale + gain * own).astype(out_ref.dtype)
    sums = [None] * nb
    if fold_rows:
        for k in range(nb):
            sums[k] = lax.dot_general(
                gt_ref[:, k * sg :],
                xrev_ref[:, : (nb - k) * sg],
                (((1,), (1,)), ((), ())),
                preferred_element_type=jnp.float32,
            )
    else:
        for j in range(nb):
            row = lax.dot_general(
                g_scr[j * br : (j + 1) * br, :],
                xrev_ref[: (j + 1) * br, :],
                (((1,), (1,)), ((), ())),
                preferred_element_type=jnp.float32,
            )
            for i in range(j + 1):
                piece = row[:, i * br : (i + 1) * br]
                sums[j - i] = piece if sums[j - i] is None else sums[j - i] + piece
    zeros = jnp.zeros((br, br), jnp.float32)
    for k in range(nb):
        padded = jnp.concatenate([sums[k], zeros], axis=1)
        skewed = pltpu.roll(padded, 0, 1, stride=1, stride_axis=0)
        diag_ref[k : k + 1, :] = jnp.sum(skewed, axis=0, keepdims=True)
    if fold_rows:
        diag = diag_ref[...]
        own = pltpu.roll(diag, br + 1, 1)[:, :br]
        nxt = pltpu.roll(diag, 1, 1)[:, :br]
        nxt = jnp.concatenate([nxt[1:], jnp.zeros((1, br), jnp.float32)], axis=0)
        lag_term = (own + nxt) * scale
        high = lag_term.astype(jnp.bfloat16).astype(jnp.float32)
        rest = lag_term - high
        middle = rest.astype(jnp.bfloat16).astype(jnp.float32)
        low = rest - middle
        pick = lax.broadcasted_iota(jnp.int32, (nb, 8, br), 1)
        tile = jnp.where(
            pick == 0,
            high[:, None, :],
            jnp.where(pick == 1, middle[:, None, :], jnp.where(pick == 2, low[:, None, :], 0.0)),
        )
        out_ref[:, br : br + 8, :br] = tile.astype(out_ref.dtype)


def pack_kernel(og_ref, gate_ref, x_ref, taps_ref, out_ref, *, br, sw, sf, gw, per_step):
    filters = taps_ref.shape[0]
    rows = lax.broadcasted_iota(jnp.int32, (8, filters), 0)
    cols = lax.broadcasted_iota(jnp.int32, (8, filters), 1)
    for d in range(per_step):
        j = pl.program_id(0) * per_step + d
        span = slice(d * sw, (d + 1) * sw)
        gated = og_ref[:, span].astype(jnp.float32) * gate_ref[:, span].astype(jnp.float32)
        out_ref[d, :br, :sw] = gated.astype(out_ref.dtype)
        out_ref[d, :br, sw:] = x_ref[:, span]
        pick = ((cols == (j * sw) // gw + rows) & (rows < sf)).astype(jnp.bfloat16)
        tap_rows = jnp.dot(pick, taps_ref[...], preferred_element_type=jnp.float32)
        out_ref[d, br:, :br] = tap_rows.astype(out_ref.dtype)
        out_ref[d, br:, br:] = jnp.zeros((8, 2 * sw - br), out_ref.dtype)


def local_kernel(g_ref, x_ref, t_ref, gain_ref, out_ref, diag_ref, g_scr, xrev_ref, gt_ref, *, nb, br, sf, sg, x_base, t_base, scale, fold_rows):
    for f in range(sf):
        filter_pass(
            g_ref.at[:, :br, f * sg : (f + 1) * sg],
            x_ref.at[:, :br, x_base + f * sg : x_base + (f + 1) * sg],
            t_ref.at[:, t_base : t_base + 8, :128],
            gain_ref,
            out_ref.at[:, :, f * sg : (f + 1) * sg],
            diag_ref.at[f],
            g_scr,
            xrev_ref,
            gt_ref,
            f,
            nb,
            br,
            sg,
            scale,
            fold_rows,
        )


def local_grads(moved, gains, nb, br, sf, sg, scale, out_rows):
    sw = sf * sg
    fold_rows = sg % 128 == 0
    if fold_rows:
        operands = (moved,)
        x_base, t_base = sw, br
    else:
        operands = (moved[:, :br, :sw], moved[:, :br, sw : 2 * sw], moved[:, br : br + 8, :128])
        x_base, t_base = 0, 0
    def body(*refs):
        if fold_rows:
            refs = refs[:1] * 3 + refs[1:]
        local_kernel(*refs, **params)

    params = dict(
        nb=nb,
        br=br,
        sf=sf,
        sg=sg,
        x_base=x_base,
        t_base=t_base,
        scale=scale,
        fold_rows=fold_rows,
    )
    return pl.pallas_call(
        body,
        out_shape=[
            jax.ShapeDtypeStruct((nb, out_rows, sw), jnp.bfloat16),
            jax.ShapeDtypeStruct((sf, nb, 2 * br), jnp.float32),
        ],
        scratch_shapes=[
            pltpu.VMEM((nb * br, sg), jnp.bfloat16),
            pltpu.VMEM((br, nb * sg) if fold_rows else (nb * br, sg), jnp.bfloat16),
            pltpu.VMEM((br, nb * sg) if fold_rows else (8, 128), jnp.bfloat16),
        ],
    )(*operands, gains.reshape(nb, 1, sw))


def per_device(cached_input, cached_gate, out_grad, filter_taps, skip_gain):
    block_rows = cached_input.shape[0]
    chan_width = cached_input.shape[1]
    filters = filter_taps.shape[1]
    group_width = chan_width // filters
    seq_count = lax.axis_size("seq")
    seq_index = lax.axis_index("seq")
    length = block_rows * seq_count
    taps_scale = 1.0 / math.sqrt(length)
    stretch_width = chan_width // seq_count
    stretch_filters = max(1, stretch_width // group_width)
    stretch_group = stretch_width // stretch_filters
    tap_columns = np.array(
        [
            (target * stretch_width) // group_width + offset
            for target in range(seq_count)
            for offset in range(stretch_filters)
        ]
    )
    def gated_grad():
        product = out_grad.astype(jnp.float32) * cached_gate.astype(jnp.float32)
        return product.astype(jnp.bfloat16)

    if stretch_width % 128 == 0:
        per_step = seq_count // 2 if seq_count % 2 == 0 else seq_count
        column_block = pl.BlockSpec((block_rows, per_step * stretch_width), lambda j: (0, j))
        packed = pl.pallas_call(
            functools.partial(
                pack_kernel,
                br=block_rows,
                sw=stretch_width,
                sf=stretch_filters,
                gw=group_width,
                per_step=per_step,
            ),
            grid=(seq_count // per_step,),
            in_specs=[
                column_block,
                column_block,
                column_block,
                pl.BlockSpec((filters, block_rows), lambda j: (0, 0)),
            ],
            out_specs=pl.BlockSpec(
                (per_step, block_rows + 8, 2 * stretch_width), lambda j: (j, 0, 0)
            ),
            out_shape=jax.ShapeDtypeStruct(
                (seq_count, block_rows + 8, 2 * stretch_width), jnp.bfloat16
            ),
        )(out_grad, cached_gate, cached_input, jnp.transpose(filter_taps))
    else:
        routed_taps = jnp.transpose(filter_taps[:, tap_columns]).reshape(
            seq_count, stretch_filters, block_rows
        )
        tap_rows = jnp.pad(
            routed_taps,
            ((0, 0), (0, 8 - stretch_filters), (0, 2 * stretch_width - block_rows)),
        )
        body = jnp.concatenate(
            [
                jnp.transpose(gated_grad().reshape(block_rows, seq_count, stretch_width), (1, 0, 2)),
                jnp.transpose(cached_input.reshape(block_rows, seq_count, stretch_width), (1, 0, 2)),
            ],
            axis=2,
        )
        packed = jnp.concatenate([body, tap_rows], axis=1)
    order = []
    for step in range(1, seq_count // 2 + 1):
        order += [step] if step == seq_count - step else [step, seq_count - step]
    arrived = [None] * seq_count
    arrived[0] = lax.dynamic_index_in_dim(packed, seq_index, 0, keepdims=True)
    for shift in order:
        chunk = lax.dynamic_index_in_dim(packed, (seq_index + shift) % seq_count, 0, keepdims=True)
        pairs = [(i, (i + shift) % seq_count) for i in range(seq_count)]
        arrived[shift] = lax.ppermute(chunk, "seq", pairs)
    moved = jnp.concatenate(arrived, axis=0)
    used_rows = 3 * stretch_filters * block_rows // stretch_width
    extra_rows = -(-used_rows // 8) * 8
    local_grad, diag = local_grads(
        moved,
        skip_gain,
        seq_count,
        block_rows,
        stretch_filters,
        stretch_group,
        taps_scale,
        block_rows + extra_rows,
    )
    if stretch_group % 128 == 0:
        outgoing = local_grad
    else:
        front = jnp.pad(diag[:, :, :block_rows], ((0, 0), (0, 1), (0, 0)))
        back = jnp.pad(diag[:, :, block_rows:], ((0, 0), (1, 0), (0, 0)))
        lag_sums = (front + back).reshape(stretch_filters, (seq_count + 1) * block_rows)
        stretch_term = lag_sums[:, block_rows - 1 : block_rows - 1 + length] * taps_scale
        high = lax.reduce_precision(stretch_term, exponent_bits=8, mantissa_bits=7)
        rest = stretch_term - high
        middle = lax.reduce_precision(rest, exponent_bits=8, mantissa_bits=7)
        low = rest - middle
        split = jnp.stack([high, middle, low], axis=0).astype(jnp.bfloat16)
        split = jnp.transpose(split.reshape(3, stretch_filters, seq_count, block_rows), (2, 0, 1, 3))
        split = split.reshape(seq_count, used_rows, stretch_width)
        split = jnp.pad(split, ((0, 0), (0, extra_rows - used_rows), (0, 0)))
        outgoing = lax.dynamic_update_slice_in_dim(local_grad, split, block_rows, 1)
    sharers = seq_count * stretch_filters // filters
    if stretch_group % 128 == 0:
        input_grad = jnp.zeros((block_rows, chan_width), outgoing.dtype)
        lag_slots = []
        for shift in range(seq_count):
            chunk = lax.dynamic_index_in_dim(
                outgoing, (seq_index - shift) % seq_count, 0, keepdims=False
            )
            if shift:
                pairs = [(i, (i - shift) % seq_count) for i in range(seq_count)]
                chunk = lax.ppermute(chunk, "seq", pairs)
            source = (seq_index + shift) % seq_count
            input_grad = lax.dynamic_update_slice_in_dim(
                input_grad, chunk[:block_rows], source * stretch_width, 1
            )
            rows = chunk[block_rows : block_rows + 3].astype(jnp.float32)
            rows = rows.reshape(3, stretch_filters, stretch_group)[..., :block_rows]
            lag_slots.append(rows[0] + rows[1] + rows[2])
        parts = jnp.roll(jnp.stack(lag_slots, axis=0), seq_index, axis=0)
    else:
        returned = lax.all_to_all(outgoing, "seq", split_axis=0, concat_axis=0, tiled=True)
        input_grad = jnp.transpose(returned[:, :block_rows, :], (1, 0, 2)).reshape(
            block_rows, chan_width
        )
        parts = returned[:, block_rows : block_rows + used_rows, :].astype(jnp.float32)
        parts = parts.reshape(seq_count, 3, stretch_filters, block_rows).sum(axis=1)
    filter_grad = jnp.transpose(
        parts.reshape(filters, sharers, block_rows).sum(axis=1)
    )
    return (input_grad, filter_grad)


def solution(mesh):
    return jax.shard_map(
        per_device,
        mesh=mesh,
        in_specs=(
            P(("groups", "seq"), "chan"),
            P(("groups", "seq"), "chan"),
            P(("groups", "seq"), "chan"),
            P("seq", "chan"),
            P("chan"),
        ),
        out_specs=(P(("groups", "seq"), "chan"), P(("groups", "seq"), "chan")),
        check_vma=False,
    )
```

```python
import functools
import math

import jax
import jax.numpy as jnp
import numpy as np
from jax import lax
from jax.experimental import pallas as pl
from jax.experimental.pallas import tpu as pltpu
from jax.sharding import PartitionSpec as P


def filter_pass(g_ref, x_ref, t_ref, gain_ref, out_ref, diag_ref, g_scr, xrev_ref, gt_ref, f, nb, br, sg, scale, fold_rows):
    me = lax.axis_index("seq")
    slot = [(me - i + nb) % nb for i in range(nb)]
    n = nb * br
    width = n + br
    pick = lax.broadcasted_iota(jnp.int32, (8, 128), 0) == f
    taps = jnp.concatenate(
        [jnp.zeros((1, br), jnp.float32)]
        + [
            jnp.sum(
                jnp.where(pick, t_ref[slot[j]].astype(jnp.float32), 0.0), axis=0, keepdims=True
            )
            for j in range(nb)
        ],
        axis=1,
    )
    taps_row = jnp.broadcast_to(taps, (br, width))
    toeplitz = pltpu.roll(taps_row, width - br, 1, stride=1, stride_axis=0)
    toeplitz = toeplitz[:, :n].astype(jnp.bfloat16)
    rows = lax.broadcasted_iota(jnp.int32, (br, br), 0)
    cols = lax.broadcasted_iota(jnp.int32, (br, br), 1)
    flip = (rows + cols == br - 1).astype(jnp.bfloat16)
    for i in range(nb):
        g_scr[i * br : (i + 1) * br, :] = g_ref[slot[i]]
        flipped = jnp.dot(flip, x_ref[slot[i]], preferred_element_type=jnp.float32)
        if fold_rows:
            gt_ref[:, i * sg : (i + 1) * sg] = g_ref[slot[i]]
            xrev_ref[:, i * sg : (i + 1) * sg] = flipped.astype(xrev_ref.dtype)
        else:
            xrev_ref[i * br : (i + 1) * br, :] = flipped.astype(xrev_ref.dtype)
    gain = gain_ref[me, :, f * sg : (f + 1) * sg]
    for i in range(nb):
        conv = jnp.dot(
            toeplitz[:, : n - i * br], g_scr[i * br :, :], preferred_element_type=jnp.float32
        )
        own = g_scr[i * br : (i + 1) * br, :].astype(jnp.float32)
        out_ref[i, :br, :] = (conv * scale + gain * own).astype(out_ref.dtype)
    sums = [None] * nb
    if fold_rows:
        for k in range(nb):
            sums[k] = lax.dot_general(
                gt_ref[:, k * sg :],
                xrev_ref[:, : (nb - k) * sg],
                (((1,), (1,)), ((), ())),
                preferred_element_type=jnp.float32,
            )
    else:
        for j in range(nb):
            row = lax.dot_general(
                g_scr[j * br : (j + 1) * br, :],
                xrev_ref[: (j + 1) * br, :],
                (((1,), (1,)), ((), ())),
                preferred_element_type=jnp.float32,
            )
            for i in range(j + 1):
                piece = row[:, i * br : (i + 1) * br]
                sums[j - i] = piece if sums[j - i] is None else sums[j - i] + piece
    zeros = jnp.zeros((br, br), jnp.float32)
    for k in range(nb):
        padded = jnp.concatenate([sums[k], zeros], axis=1)
        skewed = pltpu.roll(padded, 0, 1, stride=1, stride_axis=0)
        diag_ref[k : k + 1, :] = jnp.sum(skewed, axis=0, keepdims=True)
    if fold_rows:
        diag = diag_ref[...]
        own = pltpu.roll(diag, br + 1, 1)[:, :br]
        nxt = pltpu.roll(diag, 1, 1)[:, :br]
        nxt = jnp.concatenate([nxt[1:], jnp.zeros((1, br), jnp.float32)], axis=0)
        lag_term = (own + nxt) * scale
        high = lag_term.astype(jnp.bfloat16).astype(jnp.float32)
        rest = lag_term - high
        middle = rest.astype(jnp.bfloat16).astype(jnp.float32)
        low = rest - middle
        pick = lax.broadcasted_iota(jnp.int32, (nb, 8, br), 1)
        tile = jnp.where(
            pick == 0,
            high[:, None, :],
            jnp.where(pick == 1, middle[:, None, :], jnp.where(pick == 2, low[:, None, :], 0.0)),
        )
        out_ref[:, br : br + 8, :br] = tile.astype(out_ref.dtype)


def pack_kernel(me_ref, *refs, nb, br, sw, sf, gw):
    og_refs, gate_refs, x_refs = refs[:nb], refs[nb : 2 * nb], refs[2 * nb : 3 * nb]
    taps_ref, out_refs = refs[3 * nb], refs[3 * nb + 1 :]
    filters = taps_ref.shape[0]
    rows = lax.broadcasted_iota(jnp.int32, (8, filters), 0)
    cols = lax.broadcasted_iota(jnp.int32, (8, filters), 1)
    for k in range(nb):
        j = (me_ref[0] + k) % nb
        out_ref = out_refs[k]
        gated = og_refs[k][...].astype(jnp.float32) * gate_refs[k][...].astype(jnp.float32)
        out_ref[:br, :sw] = gated.astype(out_ref.dtype)
        out_ref[:br, sw:] = x_refs[k][...]
        pick = ((cols == (j * sw) // gw + rows) & (rows < sf)).astype(jnp.bfloat16)
        tap_rows = jnp.dot(pick, taps_ref[...], preferred_element_type=jnp.float32)
        out_ref[br:, :br] = tap_rows.astype(out_ref.dtype)
        out_ref[br:, br:] = jnp.zeros((8, 2 * sw - br), out_ref.dtype)


def local_kernel(g_ref, x_ref, t_ref, gain_ref, out_ref, diag_ref, g_scr, xrev_ref, gt_ref, *, nb, br, sf, sg, x_base, t_base, scale, fold_rows):
    for f in range(sf):
        filter_pass(
            g_ref.at[:, :br, f * sg : (f + 1) * sg],
            x_ref.at[:, :br, x_base + f * sg : x_base + (f + 1) * sg],
            t_ref.at[:, t_base : t_base + 8, :128],
            gain_ref,
            out_ref.at[:, :, f * sg : (f + 1) * sg],
            diag_ref.at[f],
            g_scr,
            xrev_ref,
            gt_ref,
            f,
            nb,
            br,
            sg,
            scale,
            fold_rows,
        )


def local_grads(moved, gains, nb, br, sf, sg, scale, out_rows):
    sw = sf * sg
    fold_rows = sg % 128 == 0
    if fold_rows:
        operands = (moved,)
        x_base, t_base = sw, br
    else:
        operands = (moved[:, :br, :sw], moved[:, :br, sw : 2 * sw], moved[:, br : br + 8, :128])
        x_base, t_base = 0, 0
    def body(*refs):
        if fold_rows:
            refs = refs[:1] * 3 + refs[1:]
        local_kernel(*refs, **params)

    params = dict(
        nb=nb,
        br=br,
        sf=sf,
        sg=sg,
        x_base=x_base,
        t_base=t_base,
        scale=scale,
        fold_rows=fold_rows,
    )
    return pl.pallas_call(
        body,
        out_shape=[
            jax.ShapeDtypeStruct((nb, out_rows, sw), jnp.bfloat16),
            jax.ShapeDtypeStruct((sf, nb, 2 * br), jnp.float32),
        ],
        scratch_shapes=[
            pltpu.VMEM((nb * br, sg), jnp.bfloat16),
            pltpu.VMEM((br, nb * sg) if fold_rows else (nb * br, sg), jnp.bfloat16),
            pltpu.VMEM((br, nb * sg) if fold_rows else (8, 128), jnp.bfloat16),
        ],
    )(*operands, gains.reshape(nb, 1, sw))


def per_device(cached_input, cached_gate, out_grad, filter_taps, skip_gain):
    block_rows = cached_input.shape[0]
    chan_width = cached_input.shape[1]
    filters = filter_taps.shape[1]
    group_width = chan_width // filters
    seq_count = lax.axis_size("seq")
    seq_index = lax.axis_index("seq")
    length = block_rows * seq_count
    taps_scale = 1.0 / math.sqrt(length)
    stretch_width = chan_width // seq_count
    stretch_filters = max(1, stretch_width // group_width)
    stretch_group = stretch_width // stretch_filters
    tap_columns = np.array(
        [
            (target * stretch_width) // group_width + offset
            for target in range(seq_count)
            for offset in range(stretch_filters)
        ]
    )
    def gated_grad():
        product = out_grad.astype(jnp.float32) * cached_gate.astype(jnp.float32)
        return product.astype(jnp.bfloat16)

    if stretch_width % 128 == 0:
        def column(k):
            return pl.BlockSpec(
                (block_rows, stretch_width), lambda i, me, k=k: (0, (me[0] + k) % seq_count)
            )

        chunk_shape = jax.ShapeDtypeStruct((block_rows + 8, 2 * stretch_width), jnp.bfloat16)
        chunks = pl.pallas_call(
            functools.partial(
                pack_kernel,
                nb=seq_count,
                br=block_rows,
                sw=stretch_width,
                sf=stretch_filters,
                gw=group_width,
            ),
            grid_spec=pltpu.PrefetchScalarGridSpec(
                num_scalar_prefetch=1,
                grid=(1,),
                in_specs=[column(k) for k in range(seq_count)] * 3
                + [pl.BlockSpec((filters, block_rows), lambda i, me: (0, 0))],
                out_specs=[
                    pl.BlockSpec((block_rows + 8, 2 * stretch_width), lambda i, me: (0, 0))
                ]
                * seq_count,
            ),
            out_shape=[chunk_shape] * seq_count,
        )(
            seq_index.reshape(1).astype(jnp.int32),
            *([out_grad] * seq_count),
            *([cached_gate] * seq_count),
            *([cached_input] * seq_count),
            jnp.transpose(filter_taps),
        )
    else:
        routed_taps = jnp.transpose(filter_taps[:, tap_columns]).reshape(
            seq_count, stretch_filters, block_rows
        )
        tap_rows = jnp.pad(
            routed_taps,
            ((0, 0), (0, 8 - stretch_filters), (0, 2 * stretch_width - block_rows)),
        )
        body = jnp.concatenate(
            [
                jnp.transpose(gated_grad().reshape(block_rows, seq_count, stretch_width), (1, 0, 2)),
                jnp.transpose(cached_input.reshape(block_rows, seq_count, stretch_width), (1, 0, 2)),
            ],
            axis=2,
        )
        packed = jnp.concatenate([body, tap_rows], axis=1)
    order = []
    for step in range(1, seq_count // 2 + 1):
        order += [step] if step == seq_count - step else [step, seq_count - step]
    if stretch_width % 128 != 0:
        chunks = [
            lax.dynamic_index_in_dim(packed, (seq_index + shift) % seq_count, 0, keepdims=False)
            for shift in range(seq_count)
        ]
    arrived = [None] * seq_count
    arrived[0] = chunks[0][None]
    for shift in order:
        pairs = [(i, (i + shift) % seq_count) for i in range(seq_count)]
        arrived[shift] = lax.ppermute(chunks[shift], "seq", pairs)[None]
    moved = jnp.concatenate(arrived, axis=0)
    used_rows = 3 * stretch_filters * block_rows // stretch_width
    extra_rows = -(-used_rows // 8) * 8
    local_grad, diag = local_grads(
        moved,
        skip_gain,
        seq_count,
        block_rows,
        stretch_filters,
        stretch_group,
        taps_scale,
        block_rows + extra_rows,
    )
    if stretch_group % 128 == 0:
        outgoing = local_grad
    else:
        front = jnp.pad(diag[:, :, :block_rows], ((0, 0), (0, 1), (0, 0)))
        back = jnp.pad(diag[:, :, block_rows:], ((0, 0), (1, 0), (0, 0)))
        lag_sums = (front + back).reshape(stretch_filters, (seq_count + 1) * block_rows)
        stretch_term = lag_sums[:, block_rows - 1 : block_rows - 1 + length] * taps_scale
        high = lax.reduce_precision(stretch_term, exponent_bits=8, mantissa_bits=7)
        rest = stretch_term - high
        middle = lax.reduce_precision(rest, exponent_bits=8, mantissa_bits=7)
        low = rest - middle
        split = jnp.stack([high, middle, low], axis=0).astype(jnp.bfloat16)
        split = jnp.transpose(split.reshape(3, stretch_filters, seq_count, block_rows), (2, 0, 1, 3))
        split = split.reshape(seq_count, used_rows, stretch_width)
        split = jnp.pad(split, ((0, 0), (0, extra_rows - used_rows), (0, 0)))
        outgoing = lax.dynamic_update_slice_in_dim(local_grad, split, block_rows, 1)
    sharers = seq_count * stretch_filters // filters
    if stretch_group % 128 == 0:
        input_grad = jnp.zeros((block_rows, chan_width), outgoing.dtype)
        lag_slots = []
        for shift in range(seq_count):
            chunk = lax.dynamic_index_in_dim(
                outgoing, (seq_index - shift) % seq_count, 0, keepdims=False
            )
            if shift:
                pairs = [(i, (i - shift) % seq_count) for i in range(seq_count)]
                chunk = lax.ppermute(chunk, "seq", pairs)
            source = (seq_index + shift) % seq_count
            input_grad = lax.dynamic_update_slice_in_dim(
                input_grad, chunk[:block_rows], source * stretch_width, 1
            )
            rows = chunk[block_rows : block_rows + 3].astype(jnp.float32)
            rows = rows.reshape(3, stretch_filters, stretch_group)[..., :block_rows]
            lag_slots.append(rows[0] + rows[1] + rows[2])
        parts = jnp.roll(jnp.stack(lag_slots, axis=0), seq_index, axis=0)
    else:
        returned = lax.all_to_all(outgoing, "seq", split_axis=0, concat_axis=0, tiled=True)
        input_grad = jnp.transpose(returned[:, :block_rows, :], (1, 0, 2)).reshape(
            block_rows, chan_width
        )
        parts = returned[:, block_rows : block_rows + used_rows, :].astype(jnp.float32)
        parts = parts.reshape(seq_count, 3, stretch_filters, block_rows).sum(axis=1)
    filter_grad = jnp.transpose(
        parts.reshape(filters, sharers, block_rows).sum(axis=1)
    )
    return (input_grad, filter_grad)


def solution(mesh):
    return jax.shard_map(
        per_device,
        mesh=mesh,
        in_specs=(
            P(("groups", "seq"), "chan"),
            P(("groups", "seq"), "chan"),
            P(("groups", "seq"), "chan"),
            P("seq", "chan"),
            P("chan"),
        ),
        out_specs=(P(("groups", "seq"), "chan"), P(("groups", "seq"), "chan")),
        check_vma=False,
    )
```

```python
import functools
import math

import jax
import jax.numpy as jnp
import numpy as np
from jax import lax
from jax.experimental import pallas as pl
from jax.experimental.pallas import tpu as pltpu
from jax.sharding import PartitionSpec as P


def filter_pass(g_ref, x_ref, t_ref, gain_ref, out_ref, diag_ref, g_scr, xrev_ref, gt_ref, f, nb, br, sg, scale, fold_rows):
    me = lax.axis_index("seq")
    slot = [(me - i + nb) % nb for i in range(nb)]
    n = nb * br
    width = n + br
    pick = lax.broadcasted_iota(jnp.int32, (8, 128), 0) == f
    taps = jnp.concatenate(
        [jnp.zeros((1, br), jnp.float32)]
        + [
            jnp.sum(
                jnp.where(pick, t_ref[slot[j]].astype(jnp.float32), 0.0), axis=0, keepdims=True
            )
            for j in range(nb)
        ],
        axis=1,
    )
    taps_row = jnp.broadcast_to(taps, (br, width))
    toeplitz = pltpu.roll(taps_row, width - br, 1, stride=1, stride_axis=0)
    toeplitz = toeplitz[:, :n].astype(jnp.bfloat16)
    rows = lax.broadcasted_iota(jnp.int32, (br, br), 0)
    cols = lax.broadcasted_iota(jnp.int32, (br, br), 1)
    flip = (rows + cols == br - 1).astype(jnp.bfloat16)
    for i in range(nb):
        g_scr[i * br : (i + 1) * br, :] = g_ref[slot[i]]
        flipped = jnp.dot(flip, x_ref[slot[i]], preferred_element_type=jnp.float32)
        if fold_rows:
            gt_ref[:, i * sg : (i + 1) * sg] = g_ref[slot[i]]
            xrev_ref[:, i * sg : (i + 1) * sg] = flipped.astype(xrev_ref.dtype)
        else:
            xrev_ref[i * br : (i + 1) * br, :] = flipped.astype(xrev_ref.dtype)
    gain = gain_ref[me, :, f * sg : (f + 1) * sg]
    for i in range(nb):
        conv = jnp.dot(
            toeplitz[:, : n - i * br], g_scr[i * br :, :], preferred_element_type=jnp.float32
        )
        own = g_scr[i * br : (i + 1) * br, :].astype(jnp.float32)
        dest = slot[i] if fold_rows else i
        out_ref[dest, :br, :] = (conv * scale + gain * own).astype(out_ref.dtype)
    sums = [None] * nb
    if fold_rows:
        for k in range(nb):
            sums[k] = lax.dot_general(
                gt_ref[:, k * sg :],
                xrev_ref[:, : (nb - k) * sg],
                (((1,), (1,)), ((), ())),
                preferred_element_type=jnp.float32,
            )
    else:
        for j in range(nb):
            row = lax.dot_general(
                g_scr[j * br : (j + 1) * br, :],
                xrev_ref[: (j + 1) * br, :],
                (((1,), (1,)), ((), ())),
                preferred_element_type=jnp.float32,
            )
            for i in range(j + 1):
                piece = row[:, i * br : (i + 1) * br]
                sums[j - i] = piece if sums[j - i] is None else sums[j - i] + piece
    zeros = jnp.zeros((br, br), jnp.float32)
    for k in range(nb):
        padded = jnp.concatenate([sums[k], zeros], axis=1)
        skewed = pltpu.roll(padded, 0, 1, stride=1, stride_axis=0)
        diag_ref[k : k + 1, :] = jnp.sum(skewed, axis=0, keepdims=True)
    if fold_rows:
        diag = diag_ref[...]
        own = pltpu.roll(diag, br + 1, 1)[:, :br]
        nxt = pltpu.roll(diag, 1, 1)[:, :br]
        nxt = jnp.concatenate([nxt[1:], jnp.zeros((1, br), jnp.float32)], axis=0)
        lag_term = (own + nxt) * scale
        high = lag_term.astype(jnp.bfloat16).astype(jnp.float32)
        rest = lag_term - high
        middle = rest.astype(jnp.bfloat16).astype(jnp.float32)
        low = rest - middle
        pick = lax.broadcasted_iota(jnp.int32, (nb, 8, br), 1)
        tile = jnp.where(
            pick == 0,
            high[:, None, :],
            jnp.where(pick == 1, middle[:, None, :], jnp.where(pick == 2, low[:, None, :], 0.0)),
        )
        tile = tile.astype(out_ref.dtype)
        for i in range(nb):
            out_ref[slot[i], br : br + 8, :br] = tile[i]


def pack_kernel(me_ref, *refs, nb, br, sw, sf, gw):
    og_refs, gate_refs, x_refs = refs[:nb], refs[nb : 2 * nb], refs[2 * nb : 3 * nb]
    taps_ref, out_refs = refs[3 * nb], refs[3 * nb + 1 :]
    filters = taps_ref.shape[0]
    rows = lax.broadcasted_iota(jnp.int32, (8, filters), 0)
    cols = lax.broadcasted_iota(jnp.int32, (8, filters), 1)
    for k in range(nb):
        j = (me_ref[0] + k) % nb
        out_ref = out_refs[k]
        gated = og_refs[k][...].astype(jnp.float32) * gate_refs[k][...].astype(jnp.float32)
        out_ref[:br, :sw] = gated.astype(out_ref.dtype)
        out_ref[:br, sw:] = x_refs[k][...]
        pick = ((cols == (j * sw) // gw + rows) & (rows < sf)).astype(jnp.bfloat16)
        tap_rows = jnp.dot(pick, taps_ref[...], preferred_element_type=jnp.float32)
        out_ref[br:, :br] = tap_rows.astype(out_ref.dtype)
        out_ref[br:, br:] = jnp.zeros((8, 2 * sw - br), out_ref.dtype)


def local_kernel(g_ref, x_ref, t_ref, gain_ref, out_ref, diag_ref, g_scr, xrev_ref, gt_ref, *, nb, br, sf, sg, x_base, t_base, scale, fold_rows):
    for f in range(sf):
        filter_pass(
            g_ref.at[:, :br, f * sg : (f + 1) * sg],
            x_ref.at[:, :br, x_base + f * sg : x_base + (f + 1) * sg],
            t_ref.at[:, t_base : t_base + 8, :128],
            gain_ref,
            out_ref.at[:, :, f * sg : (f + 1) * sg],
            diag_ref.at[f],
            g_scr,
            xrev_ref,
            gt_ref,
            f,
            nb,
            br,
            sg,
            scale,
            fold_rows,
        )


def local_grads(moved, gains, nb, br, sf, sg, scale, out_rows):
    sw = sf * sg
    fold_rows = sg % 128 == 0
    if fold_rows:
        operands = (moved,)
        x_base, t_base = sw, br
    else:
        operands = (moved[:, :br, :sw], moved[:, :br, sw : 2 * sw], moved[:, br : br + 8, :128])
        x_base, t_base = 0, 0
    def body(*refs):
        if fold_rows:
            refs = refs[:1] * 3 + refs[1:]
        local_kernel(*refs, **params)

    params = dict(
        nb=nb,
        br=br,
        sf=sf,
        sg=sg,
        x_base=x_base,
        t_base=t_base,
        scale=scale,
        fold_rows=fold_rows,
    )
    return pl.pallas_call(
        body,
        out_shape=[
            jax.ShapeDtypeStruct((nb, out_rows, sw), jnp.bfloat16),
            jax.ShapeDtypeStruct((sf, nb, 2 * br), jnp.float32),
        ],
        scratch_shapes=[
            pltpu.VMEM((nb * br, sg), jnp.bfloat16),
            pltpu.VMEM((br, nb * sg) if fold_rows else (nb * br, sg), jnp.bfloat16),
            pltpu.VMEM((br, nb * sg) if fold_rows else (8, 128), jnp.bfloat16),
        ],
    )(*operands, gains.reshape(nb, 1, sw))


def per_device(cached_input, cached_gate, out_grad, filter_taps, skip_gain):
    block_rows = cached_input.shape[0]
    chan_width = cached_input.shape[1]
    filters = filter_taps.shape[1]
    group_width = chan_width // filters
    seq_count = lax.axis_size("seq")
    seq_index = lax.axis_index("seq")
    length = block_rows * seq_count
    taps_scale = 1.0 / math.sqrt(length)
    stretch_width = chan_width // seq_count
    stretch_filters = max(1, stretch_width // group_width)
    stretch_group = stretch_width // stretch_filters
    tap_columns = np.array(
        [
            (target * stretch_width) // group_width + offset
            for target in range(seq_count)
            for offset in range(stretch_filters)
        ]
    )
    def gated_grad():
        product = out_grad.astype(jnp.float32) * cached_gate.astype(jnp.float32)
        return product.astype(jnp.bfloat16)

    if stretch_width % 128 == 0:
        def column(k):
            return pl.BlockSpec(
                (block_rows, stretch_width), lambda i, me, k=k: (0, (me[0] + k) % seq_count)
            )

        chunk_shape = jax.ShapeDtypeStruct((block_rows + 8, 2 * stretch_width), jnp.bfloat16)
        chunks = pl.pallas_call(
            functools.partial(
                pack_kernel,
                nb=seq_count,
                br=block_rows,
                sw=stretch_width,
                sf=stretch_filters,
                gw=group_width,
            ),
            grid_spec=pltpu.PrefetchScalarGridSpec(
                num_scalar_prefetch=1,
                grid=(1,),
                in_specs=[column(k) for k in range(seq_count)] * 3
                + [pl.BlockSpec((filters, block_rows), lambda i, me: (0, 0))],
                out_specs=[
                    pl.BlockSpec((block_rows + 8, 2 * stretch_width), lambda i, me: (0, 0))
                ]
                * seq_count,
            ),
            out_shape=[chunk_shape] * seq_count,
        )(
            seq_index.reshape(1).astype(jnp.int32),
            *([out_grad] * seq_count),
            *([cached_gate] * seq_count),
            *([cached_input] * seq_count),
            jnp.transpose(filter_taps),
        )
    else:
        routed_taps = jnp.transpose(filter_taps[:, tap_columns]).reshape(
            seq_count, stretch_filters, block_rows
        )
        tap_rows = jnp.pad(
            routed_taps,
            ((0, 0), (0, 8 - stretch_filters), (0, 2 * stretch_width - block_rows)),
        )
        body = jnp.concatenate(
            [
                jnp.transpose(gated_grad().reshape(block_rows, seq_count, stretch_width), (1, 0, 2)),
                jnp.transpose(cached_input.reshape(block_rows, seq_count, stretch_width), (1, 0, 2)),
            ],
            axis=2,
        )
        packed = jnp.concatenate([body, tap_rows], axis=1)
    order = []
    for step in range(1, seq_count // 2 + 1):
        order += [step] if step == seq_count - step else [step, seq_count - step]
    if stretch_width % 128 != 0:
        chunks = [
            lax.dynamic_index_in_dim(packed, (seq_index + shift) % seq_count, 0, keepdims=False)
            for shift in range(seq_count)
        ]
    arrived = [None] * seq_count
    arrived[0] = chunks[0][None]
    for shift in order:
        pairs = [(i, (i + shift) % seq_count) for i in range(seq_count)]
        arrived[shift] = lax.ppermute(chunks[shift], "seq", pairs)[None]
    moved = jnp.concatenate(arrived, axis=0)
    used_rows = 3 * stretch_filters * block_rows // stretch_width
    extra_rows = -(-used_rows // 8) * 8
    local_grad, diag = local_grads(
        moved,
        skip_gain,
        seq_count,
        block_rows,
        stretch_filters,
        stretch_group,
        taps_scale,
        block_rows + extra_rows,
    )
    if stretch_group % 128 == 0:
        outgoing = local_grad
    else:
        front = jnp.pad(diag[:, :, :block_rows], ((0, 0), (0, 1), (0, 0)))
        back = jnp.pad(diag[:, :, block_rows:], ((0, 0), (1, 0), (0, 0)))
        lag_sums = (front + back).reshape(stretch_filters, (seq_count + 1) * block_rows)
        stretch_term = lag_sums[:, block_rows - 1 : block_rows - 1 + length] * taps_scale
        high = lax.reduce_precision(stretch_term, exponent_bits=8, mantissa_bits=7)
        rest = stretch_term - high
        middle = lax.reduce_precision(rest, exponent_bits=8, mantissa_bits=7)
        low = rest - middle
        split = jnp.stack([high, middle, low], axis=0).astype(jnp.bfloat16)
        split = jnp.transpose(split.reshape(3, stretch_filters, seq_count, block_rows), (2, 0, 1, 3))
        split = split.reshape(seq_count, used_rows, stretch_width)
        split = jnp.pad(split, ((0, 0), (0, extra_rows - used_rows), (0, 0)))
        outgoing = lax.dynamic_update_slice_in_dim(local_grad, split, block_rows, 1)
    sharers = seq_count * stretch_filters // filters
    if stretch_group % 128 == 0:
        input_grad = jnp.zeros((block_rows, chan_width), outgoing.dtype)
        lag_slots = []
        for shift in range(seq_count):
            chunk = outgoing[shift]
            if shift:
                pairs = [(i, (i - shift) % seq_count) for i in range(seq_count)]
                chunk = lax.ppermute(chunk, "seq", pairs)
            source = (seq_index + shift) % seq_count
            input_grad = lax.dynamic_update_slice_in_dim(
                input_grad, chunk[:block_rows], source * stretch_width, 1
            )
            rows = chunk[block_rows : block_rows + 3].astype(jnp.float32)
            rows = rows.reshape(3, stretch_filters, stretch_group)[..., :block_rows]
            lag_slots.append(rows[0] + rows[1] + rows[2])
        parts = jnp.roll(jnp.stack(lag_slots, axis=0), seq_index, axis=0)
    else:
        returned = lax.all_to_all(outgoing, "seq", split_axis=0, concat_axis=0, tiled=True)
        input_grad = jnp.transpose(returned[:, :block_rows, :], (1, 0, 2)).reshape(
            block_rows, chan_width
        )
        parts = returned[:, block_rows : block_rows + used_rows, :].astype(jnp.float32)
        parts = parts.reshape(seq_count, 3, stretch_filters, block_rows).sum(axis=1)
    filter_grad = jnp.transpose(
        parts.reshape(filters, sharers, block_rows).sum(axis=1)
    )
    return (input_grad, filter_grad)


def solution(mesh):
    return jax.shard_map(
        per_device,
        mesh=mesh,
        in_specs=(
            P(("groups", "seq"), "chan"),
            P(("groups", "seq"), "chan"),
            P(("groups", "seq"), "chan"),
            P("seq", "chan"),
            P("chan"),
        ),
        out_specs=(P(("groups", "seq"), "chan"), P(("groups", "seq"), "chan")),
        check_vma=False,
    )
```

```python
import functools
import math

import jax
import jax.numpy as jnp
import numpy as np
from jax import lax
from jax.experimental import pallas as pl
from jax.experimental.pallas import tpu as pltpu
from jax.sharding import PartitionSpec as P


def filter_pass(g_ref, x_ref, t_ref, gain_ref, out_ref, diag_ref, g_scr, xrev_ref, gt_ref, tf_ref, f, nb, br, sg, scale, fold_rows):
    me = lax.axis_index("seq")
    slot = [(me - i + nb) % nb for i in range(nb)]
    n = nb * br
    width = n + br
    pick = lax.broadcasted_iota(jnp.int32, (8, 128), 0) == f
    taps = jnp.concatenate(
        [jnp.zeros((1, br), jnp.float32)]
        + [
            jnp.sum(
                jnp.where(pick, t_ref[slot[j]].astype(jnp.float32), 0.0), axis=0, keepdims=True
            )
            for j in range(nb)
        ],
        axis=1,
    )
    taps_row = jnp.broadcast_to(taps, (br, width))
    toeplitz = pltpu.roll(taps_row, width - br, 1, stride=1, stride_axis=0)
    toeplitz = toeplitz[:, :n].astype(jnp.bfloat16)
    rows = lax.broadcasted_iota(jnp.int32, (br, br), 0)
    cols = lax.broadcasted_iota(jnp.int32, (br, br), 1)
    flip = (rows + cols == br - 1).astype(jnp.bfloat16)
    for i in range(nb):
        g_scr[i * br : (i + 1) * br, :] = g_ref[slot[i]]
        flipped = jnp.dot(flip, x_ref[slot[i]], preferred_element_type=jnp.float32)
        if fold_rows:
            gt_ref[:, i * sg : (i + 1) * sg] = g_ref[slot[i]]
            xrev_ref[:, i * sg : (i + 1) * sg] = flipped.astype(xrev_ref.dtype)
        else:
            xrev_ref[i * br : (i + 1) * br, :] = flipped.astype(xrev_ref.dtype)
    gain = gain_ref[me, :, f * sg : (f + 1) * sg]
    if fold_rows:
        for i in range(nb):
            if i:
                tf_ref[i * br : (i + 1) * br, : i * br] = jnp.zeros((br, i * br), tf_ref.dtype)
            tf_ref[i * br : (i + 1) * br, i * br :] = toeplitz[:, : n - i * br]
        conv_all = jnp.dot(tf_ref[...], g_scr[...], preferred_element_type=jnp.float32)
    for i in range(nb):
        if fold_rows:
            conv = conv_all[i * br : (i + 1) * br, :]
        else:
            conv = jnp.dot(
                toeplitz[:, : n - i * br], g_scr[i * br :, :], preferred_element_type=jnp.float32
            )
        own = g_scr[i * br : (i + 1) * br, :].astype(jnp.float32)
        out_ref[i, :br, :] = (conv * scale + gain * own).astype(out_ref.dtype)
    sums = [None] * nb
    if fold_rows:
        for k in range(nb):
            sums[k] = lax.dot_general(
                gt_ref[:, k * sg :],
                xrev_ref[:, : (nb - k) * sg],
                (((1,), (1,)), ((), ())),
                preferred_element_type=jnp.float32,
            )
    else:
        for j in range(nb):
            row = lax.dot_general(
                g_scr[j * br : (j + 1) * br, :],
                xrev_ref[: (j + 1) * br, :],
                (((1,), (1,)), ((), ())),
                preferred_element_type=jnp.float32,
            )
            for i in range(j + 1):
                piece = row[:, i * br : (i + 1) * br]
                sums[j - i] = piece if sums[j - i] is None else sums[j - i] + piece
    zeros = jnp.zeros((br, br), jnp.float32)
    for k in range(nb):
        padded = jnp.concatenate([sums[k], zeros], axis=1)
        skewed = pltpu.roll(padded, 0, 1, stride=1, stride_axis=0)
        diag_ref[k : k + 1, :] = jnp.sum(skewed, axis=0, keepdims=True)
    if fold_rows:
        diag = diag_ref[...]
        own = pltpu.roll(diag, br + 1, 1)[:, :br]
        nxt = pltpu.roll(diag, 1, 1)[:, :br]
        nxt = jnp.concatenate([nxt[1:], jnp.zeros((1, br), jnp.float32)], axis=0)
        lag_term = (own + nxt) * scale
        high = lag_term.astype(jnp.bfloat16).astype(jnp.float32)
        rest = lag_term - high
        middle = rest.astype(jnp.bfloat16).astype(jnp.float32)
        low = rest - middle
        pick = lax.broadcasted_iota(jnp.int32, (nb, 8, br), 1)
        tile = jnp.where(
            pick == 0,
            high[:, None, :],
            jnp.where(pick == 1, middle[:, None, :], jnp.where(pick == 2, low[:, None, :], 0.0)),
        )
        out_ref[:, br : br + 8, :br] = tile.astype(out_ref.dtype)


def pack_kernel(me_ref, *refs, nb, br, sw, sf, gw):
    og_refs, gate_refs, x_refs = refs[:nb], refs[nb : 2 * nb], refs[2 * nb : 3 * nb]
    taps_ref, out_refs = refs[3 * nb], refs[3 * nb + 1 :]
    filters = taps_ref.shape[0]
    rows = lax.broadcasted_iota(jnp.int32, (8, filters), 0)
    cols = lax.broadcasted_iota(jnp.int32, (8, filters), 1)
    for k in range(nb):
        j = (me_ref[0] + k) % nb
        out_ref = out_refs[k]
        gated = og_refs[k][...].astype(jnp.float32) * gate_refs[k][...].astype(jnp.float32)
        out_ref[:br, :sw] = gated.astype(out_ref.dtype)
        out_ref[:br, sw:] = x_refs[k][...]
        pick = ((cols == (j * sw) // gw + rows) & (rows < sf)).astype(jnp.bfloat16)
        tap_rows = jnp.dot(pick, taps_ref[...], preferred_element_type=jnp.float32)
        out_ref[br:, :br] = tap_rows.astype(out_ref.dtype)
        out_ref[br:, br:] = jnp.zeros((8, 2 * sw - br), out_ref.dtype)


def local_kernel(g_ref, x_ref, t_ref, gain_ref, out_ref, diag_ref, g_scr, xrev_ref, gt_ref, tf_ref, *, nb, br, sf, sg, x_base, t_base, scale, fold_rows):
    for f in range(sf):
        filter_pass(
            g_ref.at[:, :br, f * sg : (f + 1) * sg],
            x_ref.at[:, :br, x_base + f * sg : x_base + (f + 1) * sg],
            t_ref.at[:, t_base : t_base + 8, :128],
            gain_ref,
            out_ref.at[:, :, f * sg : (f + 1) * sg],
            diag_ref.at[f],
            g_scr,
            xrev_ref,
            gt_ref,
            tf_ref,
            f,
            nb,
            br,
            sg,
            scale,
            fold_rows,
        )


def local_grads(moved, gains, nb, br, sf, sg, scale, out_rows):
    sw = sf * sg
    fold_rows = sg % 128 == 0
    if fold_rows:
        operands = (moved,)
        x_base, t_base = sw, br
    else:
        operands = (moved[:, :br, :sw], moved[:, :br, sw : 2 * sw], moved[:, br : br + 8, :128])
        x_base, t_base = 0, 0
    def body(*refs):
        if fold_rows:
            refs = refs[:1] * 3 + refs[1:]
        local_kernel(*refs, **params)

    params = dict(
        nb=nb,
        br=br,
        sf=sf,
        sg=sg,
        x_base=x_base,
        t_base=t_base,
        scale=scale,
        fold_rows=fold_rows,
    )
    return pl.pallas_call(
        body,
        out_shape=[
            jax.ShapeDtypeStruct((nb, out_rows, sw), jnp.bfloat16),
            jax.ShapeDtypeStruct((sf, nb, 2 * br), jnp.float32),
        ],
        scratch_shapes=[
            pltpu.VMEM((nb * br, sg), jnp.bfloat16),
            pltpu.VMEM((br, nb * sg) if fold_rows else (nb * br, sg), jnp.bfloat16),
            pltpu.VMEM((br, nb * sg) if fold_rows else (8, 128), jnp.bfloat16),
            pltpu.VMEM((nb * br, nb * br) if fold_rows else (8, 128), jnp.bfloat16),
        ],
    )(*operands, gains.reshape(nb, 1, sw))


def per_device(cached_input, cached_gate, out_grad, filter_taps, skip_gain):
    block_rows = cached_input.shape[0]
    chan_width = cached_input.shape[1]
    filters = filter_taps.shape[1]
    group_width = chan_width // filters
    seq_count = lax.axis_size("seq")
    seq_index = lax.axis_index("seq")
    length = block_rows * seq_count
    taps_scale = 1.0 / math.sqrt(length)
    stretch_width = chan_width // seq_count
    stretch_filters = max(1, stretch_width // group_width)
    stretch_group = stretch_width // stretch_filters
    tap_columns = np.array(
        [
            (target * stretch_width) // group_width + offset
            for target in range(seq_count)
            for offset in range(stretch_filters)
        ]
    )
    def gated_grad():
        product = out_grad.astype(jnp.float32) * cached_gate.astype(jnp.float32)
        return product.astype(jnp.bfloat16)

    if stretch_width % 128 == 0:
        def column(k):
            return pl.BlockSpec(
                (block_rows, stretch_width), lambda i, me, k=k: (0, (me[0] + k) % seq_count)
            )

        chunk_shape = jax.ShapeDtypeStruct((block_rows + 8, 2 * stretch_width), jnp.bfloat16)
        chunks = pl.pallas_call(
            functools.partial(
                pack_kernel,
                nb=seq_count,
                br=block_rows,
                sw=stretch_width,
                sf=stretch_filters,
                gw=group_width,
            ),
            grid_spec=pltpu.PrefetchScalarGridSpec(
                num_scalar_prefetch=1,
                grid=(1,),
                in_specs=[column(k) for k in range(seq_count)] * 3
                + [pl.BlockSpec((filters, block_rows), lambda i, me: (0, 0))],
                out_specs=[
                    pl.BlockSpec((block_rows + 8, 2 * stretch_width), lambda i, me: (0, 0))
                ]
                * seq_count,
            ),
            out_shape=[chunk_shape] * seq_count,
        )(
            seq_index.reshape(1).astype(jnp.int32),
            *([out_grad] * seq_count),
            *([cached_gate] * seq_count),
            *([cached_input] * seq_count),
            jnp.transpose(filter_taps),
        )
    else:
        routed_taps = jnp.transpose(filter_taps[:, tap_columns]).reshape(
            seq_count, stretch_filters, block_rows
        )
        tap_rows = jnp.pad(
            routed_taps,
            ((0, 0), (0, 8 - stretch_filters), (0, 2 * stretch_width - block_rows)),
        )
        body = jnp.concatenate(
            [
                jnp.transpose(gated_grad().reshape(block_rows, seq_count, stretch_width), (1, 0, 2)),
                jnp.transpose(cached_input.reshape(block_rows, seq_count, stretch_width), (1, 0, 2)),
            ],
            axis=2,
        )
        packed = jnp.concatenate([body, tap_rows], axis=1)
    order = []
    for step in range(1, seq_count // 2 + 1):
        order += [step] if step == seq_count - step else [step, seq_count - step]
    if stretch_width % 128 != 0:
        chunks = [
            lax.dynamic_index_in_dim(packed, (seq_index + shift) % seq_count, 0, keepdims=False)
            for shift in range(seq_count)
        ]
    arrived = [None] * seq_count
    arrived[0] = chunks[0][None]
    for shift in order:
        pairs = [(i, (i + shift) % seq_count) for i in range(seq_count)]
        arrived[shift] = lax.ppermute(chunks[shift], "seq", pairs)[None]
    moved = jnp.concatenate(arrived, axis=0)
    used_rows = 3 * stretch_filters * block_rows // stretch_width
    extra_rows = -(-used_rows // 8) * 8
    local_grad, diag = local_grads(
        moved,
        skip_gain,
        seq_count,
        block_rows,
        stretch_filters,
        stretch_group,
        taps_scale,
        block_rows + extra_rows,
    )
    if stretch_group % 128 == 0:
        outgoing = local_grad
    else:
        front = jnp.pad(diag[:, :, :block_rows], ((0, 0), (0, 1), (0, 0)))
        back = jnp.pad(diag[:, :, block_rows:], ((0, 0), (1, 0), (0, 0)))
        lag_sums = (front + back).reshape(stretch_filters, (seq_count + 1) * block_rows)
        stretch_term = lag_sums[:, block_rows - 1 : block_rows - 1 + length] * taps_scale
        high = lax.reduce_precision(stretch_term, exponent_bits=8, mantissa_bits=7)
        rest = stretch_term - high
        middle = lax.reduce_precision(rest, exponent_bits=8, mantissa_bits=7)
        low = rest - middle
        split = jnp.stack([high, middle, low], axis=0).astype(jnp.bfloat16)
        split = jnp.transpose(split.reshape(3, stretch_filters, seq_count, block_rows), (2, 0, 1, 3))
        split = split.reshape(seq_count, used_rows, stretch_width)
        split = jnp.pad(split, ((0, 0), (0, extra_rows - used_rows), (0, 0)))
        outgoing = lax.dynamic_update_slice_in_dim(local_grad, split, block_rows, 1)
    sharers = seq_count * stretch_filters // filters
    if stretch_group % 128 == 0:
        input_grad = jnp.zeros((block_rows, chan_width), outgoing.dtype)
        lag_slots = []
        for shift in range(seq_count):
            chunk = lax.dynamic_index_in_dim(
                outgoing, (seq_index - shift) % seq_count, 0, keepdims=False
            )
            if shift:
                pairs = [(i, (i - shift) % seq_count) for i in range(seq_count)]
                chunk = lax.ppermute(chunk, "seq", pairs)
            source = (seq_index + shift) % seq_count
            input_grad = lax.dynamic_update_slice_in_dim(
                input_grad, chunk[:block_rows], source * stretch_width, 1
            )
            rows = chunk[block_rows : block_rows + 3].astype(jnp.float32)
            rows = rows.reshape(3, stretch_filters, stretch_group)[..., :block_rows]
            lag_slots.append(rows[0] + rows[1] + rows[2])
        parts = jnp.roll(jnp.stack(lag_slots, axis=0), seq_index, axis=0)
    else:
        returned = lax.all_to_all(outgoing, "seq", split_axis=0, concat_axis=0, tiled=True)
        input_grad = jnp.transpose(returned[:, :block_rows, :], (1, 0, 2)).reshape(
            block_rows, chan_width
        )
        parts = returned[:, block_rows : block_rows + used_rows, :].astype(jnp.float32)
        parts = parts.reshape(seq_count, 3, stretch_filters, block_rows).sum(axis=1)
    filter_grad = jnp.transpose(
        parts.reshape(filters, sharers, block_rows).sum(axis=1)
    )
    return (input_grad, filter_grad)


def solution(mesh):
    return jax.shard_map(
        per_device,
        mesh=mesh,
        in_specs=(
            P(("groups", "seq"), "chan"),
            P(("groups", "seq"), "chan"),
            P(("groups", "seq"), "chan"),
            P("seq", "chan"),
            P("chan"),
        ),
        out_specs=(P(("groups", "seq"), "chan"), P(("groups", "seq"), "chan")),
        check_vma=False,
    )
```

```python
import functools
import math

import jax
import jax.numpy as jnp
import numpy as np
from jax import lax
from jax.experimental import pallas as pl
from jax.experimental.pallas import tpu as pltpu
from jax.sharding import PartitionSpec as P


def filter_pass(g_ref, x_ref, t_ref, gain_ref, out_ref, diag_ref, g_scr, xrev_ref, gt_ref, f, nb, br, sg, scale, fold_rows):
    me = lax.axis_index("seq")
    slot = [(me - i + nb) % nb for i in range(nb)]
    n = nb * br
    width = n + br
    pick = lax.broadcasted_iota(jnp.int32, (8, 128), 0) == f
    taps = jnp.concatenate(
        [jnp.zeros((1, br), jnp.float32)]
        + [
            jnp.sum(
                jnp.where(pick, t_ref[slot[j]].astype(jnp.float32), 0.0), axis=0, keepdims=True
            )
            for j in range(nb)
        ],
        axis=1,
    )
    taps_row = jnp.broadcast_to(taps, (br, width))
    toeplitz = pltpu.roll(taps_row, width - br, 1, stride=1, stride_axis=0)
    toeplitz = toeplitz[:, :n].astype(jnp.bfloat16)
    rows = lax.broadcasted_iota(jnp.int32, (br, br), 0)
    cols = lax.broadcasted_iota(jnp.int32, (br, br), 1)
    flip = (rows + cols == br - 1).astype(jnp.bfloat16)
    for i in range(nb):
        g_scr[i * br : (i + 1) * br, :] = g_ref[slot[i]]
        flipped = jnp.dot(flip, x_ref[slot[i]], preferred_element_type=jnp.float32)
        if fold_rows:
            gt_ref[:, i * sg : (i + 1) * sg] = g_ref[slot[i]]
            xrev_ref[:, i * sg : (i + 1) * sg] = flipped.astype(xrev_ref.dtype)
        else:
            xrev_ref[i * br : (i + 1) * br, :] = flipped.astype(xrev_ref.dtype)
    gain = gain_ref[me, :, f * sg : (f + 1) * sg]
    for i in range(nb):
        conv = jnp.dot(
            toeplitz[:, : n - i * br], g_scr[i * br :, :], preferred_element_type=jnp.float32
        )
        own = g_scr[i * br : (i + 1) * br, :].astype(jnp.float32)
        out_ref[i, :br, :] = (conv * scale + gain * own).astype(out_ref.dtype)
    sums = [None] * nb
    if fold_rows:
        for k in range(nb):
            sums[k] = lax.dot_general(
                gt_ref[:, k * sg :],
                xrev_ref[:, : (nb - k) * sg],
                (((1,), (1,)), ((), ())),
                preferred_element_type=jnp.float32,
            )
    else:
        for j in range(nb):
            row = lax.dot_general(
                g_scr[j * br : (j + 1) * br, :],
                xrev_ref[: (j + 1) * br, :],
                (((1,), (1,)), ((), ())),
                preferred_element_type=jnp.float32,
            )
            for i in range(j + 1):
                piece = row[:, i * br : (i + 1) * br]
                sums[j - i] = piece if sums[j - i] is None else sums[j - i] + piece
    zeros = jnp.zeros((br, br), jnp.float32)
    for k in range(nb):
        padded = jnp.concatenate([sums[k], zeros], axis=1)
        skewed = pltpu.roll(padded, 0, 1, stride=1, stride_axis=0)
        diag_ref[k : k + 1, :] = jnp.sum(skewed, axis=0, keepdims=True)
    if fold_rows:
        diag = diag_ref[...]
        own = pltpu.roll(diag, br + 1, 1)[:, :br]
        nxt = pltpu.roll(diag, 1, 1)[:, :br]
        nxt = jnp.concatenate([nxt[1:], jnp.zeros((1, br), jnp.float32)], axis=0)
        lag_term = (own + nxt) * scale
        high = lag_term.astype(jnp.bfloat16).astype(jnp.float32)
        rest = lag_term - high
        middle = rest.astype(jnp.bfloat16).astype(jnp.float32)
        low = rest - middle
        pick = lax.broadcasted_iota(jnp.int32, (nb, 8, br), 1)
        tile = jnp.where(
            pick == 0,
            high[:, None, :],
            jnp.where(pick == 1, middle[:, None, :], jnp.where(pick == 2, low[:, None, :], 0.0)),
        )
        out_ref[:, br : br + 8, :br] = tile.astype(out_ref.dtype)


def pack_kernel(me_ref, *refs, nb, br, sw, sf, gw):
    og_refs, gate_refs, x_refs = refs[:nb], refs[nb : 2 * nb], refs[2 * nb : 3 * nb]
    taps_ref, out_refs = refs[3 * nb], refs[3 * nb + 1 :]
    filters = taps_ref.shape[0]
    rows = lax.broadcasted_iota(jnp.int32, (8, filters), 0)
    cols = lax.broadcasted_iota(jnp.int32, (8, filters), 1)
    for k in range(nb):
        j = (me_ref[0] + k) % nb
        out_ref = out_refs[k]
        gated = og_refs[k][...].astype(jnp.float32) * gate_refs[k][...].astype(jnp.float32)
        out_ref[:br, :sw] = gated.astype(out_ref.dtype)
        out_ref[:br, sw:] = x_refs[k][...]
        pick = ((cols == (j * sw) // gw + rows) & (rows < sf)).astype(jnp.bfloat16)
        tap_rows = jnp.dot(pick, taps_ref[...], preferred_element_type=jnp.float32)
        out_ref[br:, :br] = tap_rows.astype(out_ref.dtype)
        out_ref[br:, br:] = jnp.zeros((8, 2 * sw - br), out_ref.dtype)


def local_kernel(g_ref, x_ref, t_ref, gain_ref, out_ref, diag_ref, g_scr, xrev_ref, gt_ref, *, nb, br, sf, sg, x_base, t_base, scale, fold_rows):
    for f in range(sf):
        filter_pass(
            g_ref.at[:, :br, f * sg : (f + 1) * sg],
            x_ref.at[:, :br, x_base + f * sg : x_base + (f + 1) * sg],
            t_ref.at[:, t_base : t_base + 8, :128],
            gain_ref,
            out_ref.at[:, :, f * sg : (f + 1) * sg],
            diag_ref.at[f],
            g_scr,
            xrev_ref,
            gt_ref,
            f,
            nb,
            br,
            sg,
            scale,
            fold_rows,
        )


def local_grads(moved, gains, nb, br, sf, sg, scale, out_rows):
    sw = sf * sg
    fold_rows = sg % 128 == 0
    if fold_rows:
        operands = (moved,)
        x_base, t_base = sw, br
    else:
        operands = (moved[:, :br, :sw], moved[:, :br, sw : 2 * sw], moved[:, br : br + 8, :128])
        x_base, t_base = 0, 0
    def body(*refs):
        if fold_rows:
            refs = refs[:1] * 3 + refs[1:]
        local_kernel(*refs, **params)

    params = dict(
        nb=nb,
        br=br,
        sf=sf,
        sg=sg,
        x_base=x_base,
        t_base=t_base,
        scale=scale,
        fold_rows=fold_rows,
    )
    return pl.pallas_call(
        body,
        out_shape=[
            jax.ShapeDtypeStruct((nb, out_rows, sw), jnp.bfloat16),
            jax.ShapeDtypeStruct((sf, nb, 2 * br), jnp.float32),
        ],
        scratch_shapes=[
            pltpu.VMEM((nb * br, sg), jnp.bfloat16),
            pltpu.VMEM((br, nb * sg) if fold_rows else (nb * br, sg), jnp.bfloat16),
            pltpu.VMEM((br, nb * sg) if fold_rows else (8, 128), jnp.bfloat16),
        ],
    )(*operands, gains.reshape(nb, 1, sw))


def per_device(cached_input, cached_gate, out_grad, filter_taps, skip_gain):
    block_rows = cached_input.shape[0]
    chan_width = cached_input.shape[1]
    filters = filter_taps.shape[1]
    group_width = chan_width // filters
    seq_count = lax.axis_size("seq")
    seq_index = lax.axis_index("seq")
    length = block_rows * seq_count
    taps_scale = 1.0 / math.sqrt(length)
    stretch_width = chan_width // seq_count
    stretch_filters = max(1, stretch_width // group_width)
    stretch_group = stretch_width // stretch_filters
    tap_columns = np.array(
        [
            (target * stretch_width) // group_width + offset
            for target in range(seq_count)
            for offset in range(stretch_filters)
        ]
    )
    def gated_grad():
        product = out_grad.astype(jnp.float32) * cached_gate.astype(jnp.float32)
        return product.astype(jnp.bfloat16)

    if stretch_width % 128 == 0:
        def column(k):
            return pl.BlockSpec(
                (block_rows, stretch_width), lambda i, me, k=k: (0, (me[0] + k) % seq_count)
            )

        chunk_shape = jax.ShapeDtypeStruct((block_rows + 8, 2 * stretch_width), jnp.bfloat16)
        chunks = pl.pallas_call(
            functools.partial(
                pack_kernel,
                nb=seq_count,
                br=block_rows,
                sw=stretch_width,
                sf=stretch_filters,
                gw=group_width,
            ),
            grid_spec=pltpu.PrefetchScalarGridSpec(
                num_scalar_prefetch=1,
                grid=(1,),
                in_specs=[column(k) for k in range(seq_count)] * 3
                + [pl.BlockSpec((filters, block_rows), lambda i, me: (0, 0))],
                out_specs=[
                    pl.BlockSpec((block_rows + 8, 2 * stretch_width), lambda i, me: (0, 0))
                ]
                * seq_count,
            ),
            out_shape=[chunk_shape] * seq_count,
        )(
            seq_index.reshape(1).astype(jnp.int32),
            *([out_grad] * seq_count),
            *([cached_gate] * seq_count),
            *([cached_input] * seq_count),
            jnp.transpose(filter_taps),
        )
    else:
        routed_taps = jnp.transpose(filter_taps[:, tap_columns]).reshape(
            seq_count, stretch_filters, block_rows
        )
        tap_rows = jnp.pad(
            routed_taps,
            ((0, 0), (0, 8 - stretch_filters), (0, 2 * stretch_width - block_rows)),
        )
        body = jnp.concatenate(
            [
                jnp.transpose(gated_grad().reshape(block_rows, seq_count, stretch_width), (1, 0, 2)),
                jnp.transpose(cached_input.reshape(block_rows, seq_count, stretch_width), (1, 0, 2)),
            ],
            axis=2,
        )
        packed = jnp.concatenate([body, tap_rows], axis=1)
    order = []
    for step in range(1, seq_count // 2 + 1):
        order += [step] if step == seq_count - step else [step, seq_count - step]
    if stretch_width % 128 != 0:
        chunks = [
            lax.dynamic_index_in_dim(packed, (seq_index + shift) % seq_count, 0, keepdims=False)
            for shift in range(seq_count)
        ]
    arrived = [None] * seq_count
    arrived[0] = chunks[0][None]
    for shift in order:
        pairs = [(i, (i + shift) % seq_count) for i in range(seq_count)]
        arrived[shift] = lax.ppermute(chunks[shift], "seq", pairs)[None]
    moved = jnp.concatenate(arrived, axis=0)
    used_rows = 3 * stretch_filters * block_rows // stretch_width
    extra_rows = -(-used_rows // 8) * 8
    local_grad, diag = local_grads(
        moved,
        skip_gain,
        seq_count,
        block_rows,
        stretch_filters,
        stretch_group,
        taps_scale,
        block_rows + extra_rows,
    )
    if stretch_group % 128 == 0:
        outgoing = local_grad
    else:
        front = jnp.pad(diag[:, :, :block_rows], ((0, 0), (0, 1), (0, 0)))
        back = jnp.pad(diag[:, :, block_rows:], ((0, 0), (1, 0), (0, 0)))
        lag_sums = (front + back).reshape(stretch_filters, (seq_count + 1) * block_rows)
        stretch_term = lag_sums[:, block_rows - 1 : block_rows - 1 + length] * taps_scale
        high = lax.reduce_precision(stretch_term, exponent_bits=8, mantissa_bits=7)
        rest = stretch_term - high
        middle = lax.reduce_precision(rest, exponent_bits=8, mantissa_bits=7)
        low = rest - middle
        split = jnp.stack([high, middle, low], axis=0).astype(jnp.bfloat16)
        split = jnp.transpose(split.reshape(3, stretch_filters, seq_count, block_rows), (2, 0, 1, 3))
        split = split.reshape(seq_count, used_rows, stretch_width)
        split = jnp.pad(split, ((0, 0), (0, extra_rows - used_rows), (0, 0)))
        outgoing = lax.dynamic_update_slice_in_dim(local_grad, split, block_rows, 1)
    sharers = seq_count * stretch_filters // filters
    if stretch_group % 128 == 0:
        input_grad = jnp.zeros((block_rows, chan_width), outgoing.dtype)
        lag_slots = []
        for shift in order + [0]:
            chunk = lax.dynamic_index_in_dim(
                outgoing, (seq_index - shift) % seq_count, 0, keepdims=False
            )
            if shift:
                pairs = [(i, (i - shift) % seq_count) for i in range(seq_count)]
                chunk = lax.ppermute(chunk, "seq", pairs)
            source = (seq_index + shift) % seq_count
            input_grad = lax.dynamic_update_slice_in_dim(
                input_grad, chunk[:block_rows], source * stretch_width, 1
            )
            rows = chunk[block_rows : block_rows + 3].astype(jnp.float32)
            rows = rows.reshape(3, stretch_filters, stretch_group)[..., :block_rows]
            lag_slots.append((shift, rows[0] + rows[1] + rows[2]))
        lag_slots = [part for _, part in sorted(lag_slots, key=lambda item: item[0])]
        parts = jnp.roll(jnp.stack(lag_slots, axis=0), seq_index, axis=0)
    else:
        returned = lax.all_to_all(outgoing, "seq", split_axis=0, concat_axis=0, tiled=True)
        input_grad = jnp.transpose(returned[:, :block_rows, :], (1, 0, 2)).reshape(
            block_rows, chan_width
        )
        parts = returned[:, block_rows : block_rows + used_rows, :].astype(jnp.float32)
        parts = parts.reshape(seq_count, 3, stretch_filters, block_rows).sum(axis=1)
    filter_grad = jnp.transpose(
        parts.reshape(filters, sharers, block_rows).sum(axis=1)
    )
    return (input_grad, filter_grad)


def solution(mesh):
    return jax.shard_map(
        per_device,
        mesh=mesh,
        in_specs=(
            P(("groups", "seq"), "chan"),
            P(("groups", "seq"), "chan"),
            P(("groups", "seq"), "chan"),
            P("seq", "chan"),
            P("chan"),
        ),
        out_specs=(P(("groups", "seq"), "chan"), P(("groups", "seq"), "chan")),
        check_vma=False,
    )
```

```python
import functools
import math

import jax
import jax.numpy as jnp
import numpy as np
from jax import lax
from jax.experimental import pallas as pl
from jax.experimental.pallas import tpu as pltpu
from jax.sharding import PartitionSpec as P


def filter_pass(g_ref, x_ref, t_ref, gain_ref, out_ref, diag_ref, g_scr, xrev_ref, gt_ref, f, nb, br, sg, scale, fold_rows):
    me = lax.axis_index("seq")
    slot = [(me - i + nb) % nb for i in range(nb)]
    n = nb * br
    width = n + br
    pick = lax.broadcasted_iota(jnp.int32, (8, 128), 0) == f
    taps = jnp.concatenate(
        [jnp.zeros((1, br), jnp.float32)]
        + [
            jnp.sum(
                jnp.where(pick, t_ref[slot[j]].astype(jnp.float32), 0.0), axis=0, keepdims=True
            )
            for j in range(nb)
        ],
        axis=1,
    )
    taps_row = jnp.broadcast_to(taps, (br, width))
    toeplitz = pltpu.roll(taps_row, width - br, 1, stride=1, stride_axis=0)
    toeplitz = toeplitz[:, :n].astype(jnp.bfloat16)
    rows = lax.broadcasted_iota(jnp.int32, (br, br), 0)
    cols = lax.broadcasted_iota(jnp.int32, (br, br), 1)
    flip = (rows + cols == br - 1).astype(jnp.bfloat16)
    for i in range(nb):
        g_scr[i * br : (i + 1) * br, :] = g_ref[slot[i]]
        flipped = jnp.dot(flip, x_ref[slot[i]], preferred_element_type=jnp.float32)
        if fold_rows:
            gt_ref[:, i * sg : (i + 1) * sg] = g_ref[slot[i]]
            xrev_ref[:, i * sg : (i + 1) * sg] = flipped.astype(xrev_ref.dtype)
        else:
            xrev_ref[i * br : (i + 1) * br, :] = flipped.astype(xrev_ref.dtype)
    gain = gain_ref[me, :, f * sg : (f + 1) * sg]
    for i in range(nb):
        conv = jnp.dot(
            toeplitz[:, : n - i * br], g_scr[i * br :, :], preferred_element_type=jnp.float32
        )
        own = g_scr[i * br : (i + 1) * br, :].astype(jnp.float32)
        out_ref[i, :br, :] = (conv * scale + gain * own).astype(out_ref.dtype)
    sums = [None] * nb
    if fold_rows:
        for k in range(nb):
            sums[k] = lax.dot_general(
                gt_ref[:, k * sg :],
                xrev_ref[:, : (nb - k) * sg],
                (((1,), (1,)), ((), ())),
                preferred_element_type=jnp.float32,
            )
    else:
        for j in range(nb):
            row = lax.dot_general(
                g_scr[j * br : (j + 1) * br, :],
                xrev_ref[: (j + 1) * br, :],
                (((1,), (1,)), ((), ())),
                preferred_element_type=jnp.float32,
            )
            for i in range(j + 1):
                piece = row[:, i * br : (i + 1) * br]
                sums[j - i] = piece if sums[j - i] is None else sums[j - i] + piece
    zeros = jnp.zeros((br, br), jnp.float32)
    for k in range(nb):
        padded = jnp.concatenate([sums[k], zeros], axis=1)
        skewed = pltpu.roll(padded, 0, 1, stride=1, stride_axis=0)
        diag_ref[k : k + 1, :] = jnp.sum(skewed, axis=0, keepdims=True)
    if fold_rows:
        diag = diag_ref[...]
        own = pltpu.roll(diag, br + 1, 1)[:, :br]
        nxt = pltpu.roll(diag, 1, 1)[:, :br]
        nxt = jnp.concatenate([nxt[1:], jnp.zeros((1, br), jnp.float32)], axis=0)
        lag_term = (own + nxt) * scale
        high = lag_term.astype(jnp.bfloat16).astype(jnp.float32)
        rest = lag_term - high
        middle = rest.astype(jnp.bfloat16).astype(jnp.float32)
        low = rest - middle
        pick = lax.broadcasted_iota(jnp.int32, (nb, 8, br), 1)
        tile = jnp.where(
            pick == 0,
            high[:, None, :],
            jnp.where(pick == 1, middle[:, None, :], jnp.where(pick == 2, low[:, None, :], 0.0)),
        )
        out_ref[:, br : br + 8, :br] = tile.astype(out_ref.dtype)


def pack_kernel(me_ref, *refs, nb, br, sw, sf, gw):
    og_refs, gate_refs, x_refs = refs[:nb], refs[nb : 2 * nb], refs[2 * nb : 3 * nb]
    taps_ref, out_refs = refs[3 * nb], refs[3 * nb + 1 :]
    filters = taps_ref.shape[0]
    rows = lax.broadcasted_iota(jnp.int32, (8, filters), 0)
    cols = lax.broadcasted_iota(jnp.int32, (8, filters), 1)
    for k in range(nb):
        j = (me_ref[0] + k) % nb
        out_ref = out_refs[k]
        gated = og_refs[k][...].astype(jnp.float32) * gate_refs[k][...].astype(jnp.float32)
        out_ref[:br, :sw] = gated.astype(out_ref.dtype)
        out_ref[:br, sw:] = x_refs[k][...]
        pick = ((cols == (j * sw) // gw + rows) & (rows < sf)).astype(jnp.bfloat16)
        tap_rows = jnp.dot(pick, taps_ref[...], preferred_element_type=jnp.float32)
        out_ref[br:, :br] = tap_rows.astype(out_ref.dtype)
        out_ref[br:, br:] = jnp.zeros((8, 2 * sw - br), out_ref.dtype)


def local_kernel(g_ref, x_ref, t_ref, gain_ref, out_ref, diag_ref, g_scr, xrev_ref, gt_ref, *, nb, br, sf, sg, x_base, t_base, scale, fold_rows):
    for f in range(sf):
        filter_pass(
            g_ref.at[:, :br, f * sg : (f + 1) * sg],
            x_ref.at[:, :br, x_base + f * sg : x_base + (f + 1) * sg],
            t_ref.at[:, t_base : t_base + 8, :128],
            gain_ref,
            out_ref.at[:, :, f * sg : (f + 1) * sg],
            diag_ref.at[f],
            g_scr,
            xrev_ref,
            gt_ref,
            f,
            nb,
            br,
            sg,
            scale,
            fold_rows,
        )


def local_grads(moved, gains, nb, br, sf, sg, scale, out_rows):
    sw = sf * sg
    fold_rows = sg % 128 == 0
    if fold_rows:
        operands = (moved,)
        x_base, t_base = sw, br
    else:
        operands = (moved[:, :br, :sw], moved[:, :br, sw : 2 * sw], moved[:, br : br + 8, :128])
        x_base, t_base = 0, 0
    def body(*refs):
        if fold_rows:
            data, gain_ref = refs[0], refs[1]
            chunk_refs, diag_ref = refs[2 : 2 + nb], refs[2 + nb]
            scratch, result = refs[3 + nb : -1], refs[-1]
            local_kernel(data, data, data, gain_ref, result, diag_ref, *scratch, **params)
            me = lax.axis_index("seq")
            for k in range(nb):
                chunk_refs[k][...] = result[(me - k + nb) % nb]
        else:
            local_kernel(*refs, **params)

    params = dict(
        nb=nb,
        br=br,
        sf=sf,
        sg=sg,
        x_base=x_base,
        t_base=t_base,
        scale=scale,
        fold_rows=fold_rows,
    )
    return pl.pallas_call(
        body,
        out_shape=(
            [jax.ShapeDtypeStruct((out_rows, sw), jnp.bfloat16)] * nb if fold_rows
            else [jax.ShapeDtypeStruct((nb, out_rows, sw), jnp.bfloat16)]
        )
        + [jax.ShapeDtypeStruct((sf, nb, 2 * br), jnp.float32)],
        scratch_shapes=[
            pltpu.VMEM((nb * br, sg), jnp.bfloat16),
            pltpu.VMEM((br, nb * sg) if fold_rows else (nb * br, sg), jnp.bfloat16),
            pltpu.VMEM((br, nb * sg) if fold_rows else (8, 128), jnp.bfloat16),
        ]
        + ([pltpu.VMEM((nb, out_rows, sw), jnp.bfloat16)] if fold_rows else []),
    )(*operands, gains.reshape(nb, 1, sw))


def per_device(cached_input, cached_gate, out_grad, filter_taps, skip_gain):
    block_rows = cached_input.shape[0]
    chan_width = cached_input.shape[1]
    filters = filter_taps.shape[1]
    group_width = chan_width // filters
    seq_count = lax.axis_size("seq")
    seq_index = lax.axis_index("seq")
    length = block_rows * seq_count
    taps_scale = 1.0 / math.sqrt(length)
    stretch_width = chan_width // seq_count
    stretch_filters = max(1, stretch_width // group_width)
    stretch_group = stretch_width // stretch_filters
    tap_columns = np.array(
        [
            (target * stretch_width) // group_width + offset
            for target in range(seq_count)
            for offset in range(stretch_filters)
        ]
    )
    def gated_grad():
        product = out_grad.astype(jnp.float32) * cached_gate.astype(jnp.float32)
        return product.astype(jnp.bfloat16)

    if stretch_width % 128 == 0:
        def column(k):
            return pl.BlockSpec(
                (block_rows, stretch_width), lambda i, me, k=k: (0, (me[0] + k) % seq_count)
            )

        chunk_shape = jax.ShapeDtypeStruct((block_rows + 8, 2 * stretch_width), jnp.bfloat16)
        chunks = pl.pallas_call(
            functools.partial(
                pack_kernel,
                nb=seq_count,
                br=block_rows,
                sw=stretch_width,
                sf=stretch_filters,
                gw=group_width,
            ),
            grid_spec=pltpu.PrefetchScalarGridSpec(
                num_scalar_prefetch=1,
                grid=(1,),
                in_specs=[column(k) for k in range(seq_count)] * 3
                + [pl.BlockSpec((filters, block_rows), lambda i, me: (0, 0))],
                out_specs=[
                    pl.BlockSpec((block_rows + 8, 2 * stretch_width), lambda i, me: (0, 0))
                ]
                * seq_count,
            ),
            out_shape=[chunk_shape] * seq_count,
        )(
            seq_index.reshape(1).astype(jnp.int32),
            *([out_grad] * seq_count),
            *([cached_gate] * seq_count),
            *([cached_input] * seq_count),
            jnp.transpose(filter_taps),
        )
    else:
        routed_taps = jnp.transpose(filter_taps[:, tap_columns]).reshape(
            seq_count, stretch_filters, block_rows
        )
        tap_rows = jnp.pad(
            routed_taps,
            ((0, 0), (0, 8 - stretch_filters), (0, 2 * stretch_width - block_rows)),
        )
        body = jnp.concatenate(
            [
                jnp.transpose(gated_grad().reshape(block_rows, seq_count, stretch_width), (1, 0, 2)),
                jnp.transpose(cached_input.reshape(block_rows, seq_count, stretch_width), (1, 0, 2)),
            ],
            axis=2,
        )
        packed = jnp.concatenate([body, tap_rows], axis=1)
    order = []
    for step in range(1, seq_count // 2 + 1):
        order += [step] if step == seq_count - step else [step, seq_count - step]
    if stretch_width % 128 != 0:
        chunks = [
            lax.dynamic_index_in_dim(packed, (seq_index + shift) % seq_count, 0, keepdims=False)
            for shift in range(seq_count)
        ]
    arrived = [None] * seq_count
    arrived[0] = chunks[0][None]
    for shift in order:
        pairs = [(i, (i + shift) % seq_count) for i in range(seq_count)]
        arrived[shift] = lax.ppermute(chunks[shift], "seq", pairs)[None]
    moved = jnp.concatenate(arrived, axis=0)
    used_rows = 3 * stretch_filters * block_rows // stretch_width
    extra_rows = -(-used_rows // 8) * 8
    *local_grad, diag = local_grads(
        moved,
        skip_gain,
        seq_count,
        block_rows,
        stretch_filters,
        stretch_group,
        taps_scale,
        block_rows + extra_rows,
    )
    if stretch_group % 128 == 0:
        outgoing = local_grad
    else:
        local_grad = local_grad[0]
        front = jnp.pad(diag[:, :, :block_rows], ((0, 0), (0, 1), (0, 0)))
        back = jnp.pad(diag[:, :, block_rows:], ((0, 0), (1, 0), (0, 0)))
        lag_sums = (front + back).reshape(stretch_filters, (seq_count + 1) * block_rows)
        stretch_term = lag_sums[:, block_rows - 1 : block_rows - 1 + length] * taps_scale
        high = lax.reduce_precision(stretch_term, exponent_bits=8, mantissa_bits=7)
        rest = stretch_term - high
        middle = lax.reduce_precision(rest, exponent_bits=8, mantissa_bits=7)
        low = rest - middle
        split = jnp.stack([high, middle, low], axis=0).astype(jnp.bfloat16)
        split = jnp.transpose(split.reshape(3, stretch_filters, seq_count, block_rows), (2, 0, 1, 3))
        split = split.reshape(seq_count, used_rows, stretch_width)
        split = jnp.pad(split, ((0, 0), (0, extra_rows - used_rows), (0, 0)))
        outgoing = lax.dynamic_update_slice_in_dim(local_grad, split, block_rows, 1)
    sharers = seq_count * stretch_filters // filters
    if stretch_group % 128 == 0:
        input_grad = jnp.zeros((block_rows, chan_width), jnp.bfloat16)
        lag_slots = []
        for shift in range(seq_count):
            chunk = outgoing[shift]
            if shift:
                pairs = [(i, (i - shift) % seq_count) for i in range(seq_count)]
                chunk = lax.ppermute(chunk, "seq", pairs)
            source = (seq_index + shift) % seq_count
            input_grad = lax.dynamic_update_slice_in_dim(
                input_grad, chunk[:block_rows], source * stretch_width, 1
            )
            rows = chunk[block_rows : block_rows + 3].astype(jnp.float32)
            rows = rows.reshape(3, stretch_filters, stretch_group)[..., :block_rows]
            lag_slots.append(rows[0] + rows[1] + rows[2])
        parts = jnp.roll(jnp.stack(lag_slots, axis=0), seq_index, axis=0)
    else:
        returned = lax.all_to_all(outgoing, "seq", split_axis=0, concat_axis=0, tiled=True)
        input_grad = jnp.transpose(returned[:, :block_rows, :], (1, 0, 2)).reshape(
            block_rows, chan_width
        )
        parts = returned[:, block_rows : block_rows + used_rows, :].astype(jnp.float32)
        parts = parts.reshape(seq_count, 3, stretch_filters, block_rows).sum(axis=1)
    filter_grad = jnp.transpose(
        parts.reshape(filters, sharers, block_rows).sum(axis=1)
    )
    return (input_grad, filter_grad)


def solution(mesh):
    return jax.shard_map(
        per_device,
        mesh=mesh,
        in_specs=(
            P(("groups", "seq"), "chan"),
            P(("groups", "seq"), "chan"),
            P(("groups", "seq"), "chan"),
            P("seq", "chan"),
            P("chan"),
        ),
        out_specs=(P(("groups", "seq"), "chan"), P(("groups", "seq"), "chan")),
        check_vma=False,
    )
```
